128 devices in a mesh: belt: 16 (over x_lo, z, core), mer: 8 (over x_hi, y).
Axes of the slice: x: 4 (x_hi: 2, x_lo: 2; x = x_hi * 2 + x_lo), y: 4, z: 4, core: 2. Of those that a mesh axis runs over, the one named last changes fastest.
Arguments:
- right_side: float32 [120, 64, 12288], P(None, 'mer', 'belt')
- helm_diag: float32 [120, 64, 12288], P(None, 'mer', 'belt'), may hold values from 1 to 3
- east_coef: float32 [120, 64, 12288], P(None, 'mer', 'belt'), may hold values from 0.5 to 1.5
- north_coef: float32 [120, 64, 12288], P(None, 'mer', 'belt'), may hold values from 0.5 to 1.5
- vert_coef: float32 [119, 64, 12288], P(None, 'mer', 'belt'), may hold values from 100 to 1000
- mortar_weights: float32 [8, 2], replicated, may hold values from 0.25 to 2
- weight_index: int32 [4, 64], replicated, may hold values from 0 to 7
- edge_map: int32 [4, 64, 2], replicated, may hold values from 0 to 63, as said below
- refined: int32 [4, 64], replicated, may hold values 0 or 1
Outputs:
- solution: float32 [120, 64, 12288], P(None, 'mer', 'belt')
- residual: float32 [120, 64, 12288], P(None, 'mer', 'belt')
The draws below stay inside these ranges and needn't reach their ends.
Inputs may be any that keep to these rules, and one draw needn't show every extreme that they name: `edge_map`: for each edge and each of the two entries of a row, the 64 rows' entries form a permutation of the rows.
All inputs are finite; a program needn't handle non-finite values.
Results may differ from the reference program's by a relative error of at most 0.0003.
Values sent between devices are 32-bit elements; how exact they have to be, the bound alone decides.
No kernel may reach another device: no remote copies, remote signals or barrier semaphores. Data moves between devices by JAX's collectives and lax.ppermute only.
A program may use at most 128 MiB of HBM per device.

```python
import math
import jax
import jax.numpy as jnp
from jax import lax

LEV = 120
ITERS = 2
NW = 8
NR = 64
NC = 12288


def draw_right_side(key, part):
    key_base, key_rows, key_cols, key_amp = jax.random.split(key, 4)
    level_pos = (jnp.arange(LEV, dtype=jnp.float32) + 0.5) / LEV
    profile = 1.0 + 0.6 * jnp.cos(math.pi * level_pos)
    base = jnp.clip(jax.random.normal(key_base, (LEV, NR, NC), jnp.float32), -4.0, 4.0)
    amplitude = 1.5 * jnp.clip(jax.random.normal(key_amp, (NR, NC), jnp.float32), -4.0, 4.0)
    total = 0.5 * base + amplitude[None, :, :] * profile[:, None, None]
    row_scale = jnp.exp(jax.random.uniform(key_rows, (NR,), jnp.float32, 0.0, math.log(10.0)))
    col_scale = jnp.exp(jax.random.uniform(key_cols, (NC,), jnp.float32, 0.0, math.log(10.0)))
    panel_pos = jnp.arange(NC, dtype=jnp.int32) % (NC // 4)
    near_edge = jnp.logical_or(panel_pos >= NC // 4 - 3, panel_pos <= 1)
    edge_boost = jnp.where(near_edge, 16.0, 1.0).astype(jnp.float32)
    col_scale = col_scale * edge_boost
    return (total * row_scale[None, :, None] * col_scale[None, None, :] * 0.1).astype(jnp.float32)


def draw_edge_map(key, part):
    edges_list = []
    for edge_num in range(4):
        slots = []
        for slot_num in range(2):
            slots.append(jax.random.permutation(jax.random.fold_in(key, 2 * edge_num + slot_num), NR).astype(jnp.int32))
        edges_list.append(jnp.stack(slots, axis=1))
    return jnp.stack(edges_list, axis=0)


def touch_ends(array, rng, smallest, largest):
    shape = array.shape
    index_at = [jax.random.randint(jax.random.fold_in(rng, axis), (), 0, shape[axis]) for axis in range(len(shape))]
    array = array.at[tuple(index_at)].set(smallest)
    longest = shape.index(max(shape))
    index_at[longest] = (index_at[longest] + 1) % shape[longest]
    return array.at[tuple(index_at)].set(largest)


def block_scale(own_key, extent, cuts, least, top_value):
    def one(position, parts):
        steps = jax.random.uniform(jax.random.fold_in(jax.random.fold_in(own_key, 6), position), (parts,), jnp.float32, least / len(cuts), top_value / len(cuts))
        return jnp.repeat(jnp.exp(steps), extent[position] // parts).reshape((-1,) + (1,) * (len(extent) - position - 1))

    factor_of = one(*cuts[0])
    for cut in cuts[1:]:
        factor_of = factor_of * one(*cut)
    return factor_of


def setup_inputs(seed: int = 0) -> dict:
    splits = jax.random.split(jax.random.key(seed), 10)
    return {
        "right_side": draw_right_side(jax.random.fold_in(splits[9], 71), 0),
        "helm_diag": jnp.clip(1.0 + 2.0 * jax.random.uniform(splits[1], (LEV, NR, NC), jnp.float32) ** block_scale(splits[1], (LEV, NR, NC), ((1, 8), (2, 16)), -0.2, 0.2), 1.0, 3.0),
        "east_coef": jnp.clip(0.5 + 1.0 * jax.random.uniform(splits[2], (LEV, NR, NC), jnp.float32) ** block_scale(splits[2], (LEV, NR, NC), ((1, 8), (2, 16)), -0.2, 0.2), 0.5, 1.5),
        "north_coef": jnp.clip(0.5 + 1.0 * jax.random.uniform(splits[3], (LEV, NR, NC), jnp.float32) ** block_scale(splits[3], (LEV, NR, NC), ((1, 8), (2, 16)), -0.2, 0.2), 0.5, 1.5),
        "vert_coef": jnp.clip(jnp.exp(math.log(1000.0) - 2.3025851 * jax.random.uniform(splits[4], (LEV - 1, NR, NC), jnp.float32) ** block_scale(splits[4], (LEV - 1, NR, NC), ((1, 8), (2, 16)), -0.2, 0.2)), 100.0, 1000.0),
        "mortar_weights": jnp.clip(jax.random.uniform(splits[5], (NW, 2), jnp.float32, 0.25, 2.0), 0.25, 2.0),
        "weight_index": touch_ends(jax.random.randint(splits[6], (4, NR), 0, NW), jax.random.fold_in(splits[6], 1), 0, NW - 1).astype(jnp.int32),
        "edge_map": draw_edge_map(jax.random.fold_in(splits[9], 71), 0),
        "refined": touch_ends((jax.random.randint(splits[8], (4, NR), 0, 2) < 1).astype(jnp.int32), jax.random.fold_in(splits[8], 1), 0, 1),
    }


def factor_columns(diagonal_sum, lower_coupling):
    def advance(previous, input_arrays):
        diag_level, lower_level = input_arrays
        ratio = lower_level / previous
        present_entry = diag_level - lower_level * ratio
        return present_entry, (1.0 / present_entry, ratio)
    start_value = jnp.ones_like(diagonal_sum[0])
    last_pivot, (inverse_pivot, ratio_values) = lax.scan(advance, start_value, (diagonal_sum, lower_coupling))
    return inverse_pivot, ratio_values


def solve_columns(values, inverse_pivot, ratio_values, upper_coupling):
    def forward(previous, input_arrays):
        value_level, ratio_layer = input_arrays
        present_entry = value_level + ratio_layer * previous
        return present_entry, present_entry
    zero_level = jnp.zeros_like(values[0])
    last_value, eliminated = lax.scan(forward, zero_level, (values, ratio_values))

    def backward(successor_entry, input_arrays):
        eliminated_layer, pivot_layer, upper_layer = input_arrays
        present_entry = pivot_layer * (eliminated_layer + upper_layer * successor_entry)
        return present_entry, present_entry
    first_value, solved = lax.scan(backward, zero_level, (eliminated, inverse_pivot, upper_coupling), reverse=True)
    return solved


def vertical_parts(vert_coef):
    zero_level = jnp.zeros((1,) + vert_coef.shape[1:], vert_coef.dtype)
    upper = jnp.concatenate([vert_coef, zero_level], axis=0)
    lower = jnp.concatenate([zero_level, vert_coef], axis=0)
    return upper, lower


def apply_operator(field, helm_diag, east_coef, west_coef, north_coef, south_coef, upper, lower,
                   edge_map, weight_index, mortar_weights, refined):
    panel = NC // 4
    east_side = jnp.roll(field, -1, axis=2)
    west_side = jnp.roll(field, 1, axis=2)
    for edge_num in range(4):
        west_col = (edge_num + 1) * panel - 1
        edge_rim = east_side[:, :, west_col]
        first_weight = mortar_weights[weight_index[edge_num], 0]
        second_weight = mortar_weights[weight_index[edge_num], 1]
        mortar = first_weight[None, :] * edge_rim[:, edge_map[edge_num, :, 0]] + second_weight[None, :] * edge_rim[:, edge_map[edge_num, :, 1]]
        east_side = east_side.at[:, :, west_col].set(jnp.where(refined[edge_num][None, :] == 1, mortar, edge_rim))
    zero_row = jnp.zeros((field.shape[0], 1, field.shape[2]), field.dtype)
    north_side = jnp.concatenate([field[:, 1:], zero_row], axis=1)
    south_side = jnp.concatenate([zero_row, field[:, :-1]], axis=1)
    zero_level = jnp.zeros((1,) + field.shape[1:], field.dtype)
    up_side = jnp.concatenate([field[1:], zero_level], axis=0)
    down_side = jnp.concatenate([zero_level, field[:-1]], axis=0)
    return (helm_diag * field + east_coef * (field - east_side) + west_coef * (field - west_side)
            + north_coef * (field - north_side) + south_coef * (field - south_side)
            + upper * (field - up_side) + lower * (field - down_side))


def reference(right_side, helm_diag, east_coef, north_coef, vert_coef, mortar_weights, weight_index, edge_map, refined):
    west_coef = jnp.roll(east_coef, 1, axis=2)
    zero_row = jnp.zeros((north_coef.shape[0], 1, north_coef.shape[2]), north_coef.dtype)
    south_coef = jnp.concatenate([zero_row, north_coef[:, :-1]], axis=1)
    upper, lower = vertical_parts(vert_coef)
    diagonal_sum = helm_diag + east_coef + west_coef + north_coef + south_coef + upper + lower
    inverse_pivot, ratio_values = factor_columns(diagonal_sum, lower)

    def operate(field):
        return apply_operator(field, helm_diag, east_coef, west_coef, north_coef, south_coef, upper, lower,
                              edge_map, weight_index, mortar_weights, refined)

    solution = jnp.zeros_like(right_side)
    residual = right_side
    precond = solve_columns(residual, inverse_pivot, ratio_values, upper)
    norm_now = jnp.sum(residual * precond)
    direction = precond
    for step_num in range(ITERS):
        image = operate(direction)
        step_size = norm_now / jnp.sum(direction * image)
        solution = solution + step_size * direction
        residual = residual - step_size * image
        if step_num + 1 < ITERS:
            precond = solve_columns(residual, inverse_pivot, ratio_values, upper)
            norm_next = jnp.sum(residual * precond)
            direction = precond + (norm_next / norm_now) * direction
            norm_now = norm_next
    return solution, residual
```

```python
import jax
import jax.numpy as jnp
from jax import lax
from jax.experimental import pallas as pl
from jax.experimental.pallas import tpu as pltpu
from jax.sharding import PartitionSpec as P

ITERS = 2
BLOCK_COLS = 256


def extended(cells, sides, width, closed):
    for axis, dim in sides:
        count = lax.axis_size(axis)
        ends = count if closed else count - 1
        head = lax.slice_in_dim(cells, 0, width, axis=dim)
        tail = lax.slice_in_dim(cells, cells.shape[dim] - width, cells.shape[dim], axis=dim)
        cells = jnp.concatenate(
            [
                lax.ppermute(tail, axis, [(i, (i + 1) % count) for i in range(ends)]),
                cells,
                lax.ppermute(head, axis, [((i + 1) % count, i) for i in range(ends)]),
            ],
            axis=dim,
        )
    return cells


def belt_pad(field):
    return extended(field, (("belt", 2),), 1, True)


def mer_pad(field):
    return extended(field, (("mer", 1),), 1, False)


def tree_sum(values):
    for axis in ("mer", "belt"):
        count = lax.axis_size(axis)
        if count & (count - 1):
            values = lax.psum(values, axis)
            continue
        bit = 1
        while bit < count:
            values = values + lax.ppermute(values, axis, [(i, i ^ bit) for i in range(count)])
            bit *= 2
    return values


def gather_rows(column):
    count = lax.axis_size("mer")
    if count & (count - 1):
        return lax.all_gather(column, "mer", axis=1, tiled=True)
    me = lax.axis_index("mer")
    bit = 1
    while bit < count:
        other = lax.ppermute(column, "mer", [(i, i ^ bit) for i in range(count)])
        low_half = (me & bit) == 0
        column = jnp.concatenate(
            [jnp.where(low_half, column, other), jnp.where(low_half, other, column)], axis=1
        )
        bit *= 2
    return column


def column_spec(levels, rows, cols):
    return pl.BlockSpec((levels, rows, cols), lambda j: (0, 0, j))


def factor_solve_kernel(h_ref, e_ref, w_ref, n_ref, s_ref, v_ref, r_ref,
                        inv_ref, ratio_ref, p_ref, part_ref):
    levels = h_ref.shape[0]
    zero = jnp.zeros(h_ref.shape[1:], jnp.float32)

    def forward(k, up, down, prev, elim):
        diag = h_ref[k] + e_ref[k] + w_ref[k] + n_ref[k] + s_ref[k] + up + down
        ratio = down / prev
        pivot = diag - down * ratio
        inv_ref[k] = 1.0 / pivot
        ratio_ref[k] = ratio
        elim = r_ref[k] + ratio * elim
        p_ref[k] = elim
        return pivot, elim

    carry = forward(0, v_ref[0], zero, jnp.ones_like(zero), zero)
    carry = lax.fori_loop(
        1, levels - 1, lambda k, c: forward(k, v_ref[k], v_ref[k - 1], *c), carry, unroll=4
    )
    forward(levels - 1, zero, v_ref[levels - 2], *carry)

    def backward(k, up, succ, acc):
        value = inv_ref[k] * (p_ref[k] + up * succ)
        p_ref[k] = value
        return value, acc + r_ref[k] * value

    carry = backward(levels - 1, zero, zero, zero)
    carry = lax.fori_loop(
        0, levels - 1, lambda i, c: backward(levels - 2 - i, v_ref[levels - 2 - i], *c), carry,
        unroll=4,
    )
    part_ref[...] = carry[1]


def factor_solve(helm_diag, east_coef, west_coef, north_coef, south_coef, vert_coef, rhs):
    levels, rows, cols = rhs.shape
    block = BLOCK_COLS if cols % BLOCK_COLS == 0 else cols
    full = column_spec(levels, rows, block)
    vspec = column_spec(levels - 1, rows, block)
    field = jax.ShapeDtypeStruct(rhs.shape, jnp.float32)
    return pl.pallas_call(
        factor_solve_kernel,
        grid=(cols // block,),
        in_specs=[full, full, full, full, full, vspec, full],
        out_specs=[full, full, full, pl.BlockSpec((rows, block), lambda j: (0, j))],
        out_shape=[field, field, field, jax.ShapeDtypeStruct((rows, cols), jnp.float32)],
    )(helm_diag, east_coef, west_coef, north_coef, south_coef, vert_coef, rhs)


def update_solve_kernel(step_ref, r_ref, img_ref, inv_ref, ratio_ref, v_ref,
                        res_ref, p_ref, part_ref):
    levels = r_ref.shape[0]
    step = step_ref[0]
    zero = jnp.zeros(r_ref.shape[1:], jnp.float32)

    def forward(k, elim):
        res = r_ref[k] - step * img_ref[k]
        res_ref[k] = res
        elim = res + ratio_ref[k] * elim
        p_ref[k] = elim
        return elim

    lax.fori_loop(0, levels, forward, zero, unroll=4)

    def backward(k, up, succ, acc):
        value = inv_ref[k] * (p_ref[k] + up * succ)
        p_ref[k] = value
        return value, acc + res_ref[k] * value

    carry = backward(levels - 1, zero, zero, zero)
    carry = lax.fori_loop(
        0, levels - 1, lambda i, c: backward(levels - 2 - i, v_ref[levels - 2 - i], *c), carry,
        unroll=4,
    )
    part_ref[...] = carry[1]


def update_solve(step, residual, image, inverse_pivot, ratio_values, vert_coef):
    levels, rows, cols = residual.shape
    block = BLOCK_COLS if cols % BLOCK_COLS == 0 else cols
    full = column_spec(levels, rows, block)
    vspec = column_spec(levels - 1, rows, block)
    field = jax.ShapeDtypeStruct(residual.shape, jnp.float32)
    return pl.pallas_call(
        update_solve_kernel,
        grid=(cols // block,),
        in_specs=[pl.BlockSpec(memory_space=pltpu.SMEM), full, full, full, full, vspec],
        out_specs=[full, full, pl.BlockSpec((rows, block), lambda j: (0, j))],
        out_shape=[field, field, jax.ShapeDtypeStruct((rows, cols), jnp.float32)],
    )(jnp.reshape(step, (1,)), residual, image, inverse_pivot, ratio_values, vert_coef)


def vertical_parts(vert_coef):
    zero_level = jnp.zeros((1,) + vert_coef.shape[1:], vert_coef.dtype)
    upper = jnp.concatenate([vert_coef, zero_level], axis=0)
    lower = jnp.concatenate([zero_level, vert_coef], axis=0)
    return (upper, lower)


def edge_tables(edge_num, row_start, rows, weight_index, edge_map, mortar_weights):
    maps = lax.dynamic_slice_in_dim(edge_map[edge_num], row_start, rows, 0)
    picks = lax.dynamic_slice_in_dim(weight_index[edge_num], row_start, rows, 0)
    return (maps[:, 0], maps[:, 1], mortar_weights[picks, 0], mortar_weights[picks, 1])


def combine(column, tables):
    first_map, second_map, first_weight, second_weight = tables
    return (
        first_weight[None, :] * column[:, first_map]
        + second_weight[None, :] * column[:, second_map]
    )


def apply_operator(direction, coefs, tables, use_mortar):
    helm_diag, east_coef, west_coef, north_coef, south_coef, upper, lower = coefs
    padded = belt_pad(direction)
    east_side = padded[:, :, 2:]
    west_side = padded[:, :, :-2]
    edge_rim = padded[:, :, -1]
    arrived = combine(gather_rows(edge_rim), tables)
    east_side = east_side.at[:, :, -1].set(jnp.where(use_mortar, arrived, edge_rim))
    padded_rows = mer_pad(direction)
    north_side = padded_rows[:, 2:, :]
    south_side = padded_rows[:, :-2, :]
    zero_level = jnp.zeros((1,) + direction.shape[1:], direction.dtype)
    up_side = jnp.concatenate([direction[1:], zero_level], axis=0)
    down_side = jnp.concatenate([zero_level, direction[:-1]], axis=0)
    return (
        helm_diag * direction
        + east_coef * (direction - east_side)
        + west_coef * (direction - west_side)
        + north_coef * (direction - north_side)
        + south_coef * (direction - south_side)
        + upper * (direction - up_side)
        + lower * (direction - down_side)
    )


def on_device(
    right_side,
    helm_diag,
    east_coef,
    north_coef,
    vert_coef,
    mortar_weights,
    weight_index,
    edge_map,
    refined,
):
    belt_index = lax.axis_index("belt")
    mer_index = lax.axis_index("mer")
    per_panel = lax.axis_size("belt") // 4
    rows = right_side.shape[1]
    row_start = mer_index * rows
    own_edge = belt_index // per_panel
    row_flags = lax.dynamic_slice_in_dim(refined[own_edge], row_start, rows, 0)
    at_edge = (belt_index + 1) % per_panel == 0
    use_mortar = jnp.logical_and(at_edge, row_flags == 1)[None, :]
    tables = edge_tables(own_edge, row_start, rows, weight_index, edge_map, mortar_weights)
    west_coef = belt_pad(east_coef)[:, :, :-2]
    south_coef = mer_pad(north_coef)[:, :-2, :]
    upper, lower = vertical_parts(vert_coef)
    coefs = (helm_diag, east_coef, west_coef, north_coef, south_coef, upper, lower)

    inverse_pivot, ratio_values, precond0, part0 = factor_solve(
        helm_diag, east_coef, west_coef, north_coef, south_coef, vert_coef, right_side
    )
    image0 = apply_operator(precond0, coefs, tables, use_mortar)
    first = tree_sum(jnp.stack([jnp.sum(part0), jnp.sum(precond0 * image0)]))
    norm0, curv0 = first[0], first[1]
    step0 = norm0 / curv0

    residual1, precond1, part1 = update_solve(
        step0, right_side, image0, inverse_pivot, ratio_values, vert_coef
    )
    image_p1 = apply_operator(precond1, coefs, tables, use_mortar)
    second = tree_sum(
        jnp.stack(
            [
                jnp.sum(part1),
                jnp.sum(precond1 * image_p1),
                jnp.sum(precond1 * image0),
                jnp.sum(precond0 * image_p1),
            ]
        )
    )
    norm1 = second[0]
    beta = norm1 / norm0
    curv1 = second[1] + beta * (second[2] + second[3]) + beta * beta * curv0
    step1 = norm1 / curv1
    direction1 = precond1 + beta * precond0
    image1 = image_p1 + beta * image0
    solution = step0 * precond0 + step1 * direction1
    residual = residual1 - step1 * image1
    return (solution, residual)


def solution(mesh):
    placed = (
        P(None, "mer", "belt"),
        P(None, "mer", "belt"),
        P(None, "mer", "belt"),
        P(None, "mer", "belt"),
        P(None, "mer", "belt"),
        P(),
        P(),
        P(),
        P(),
    )
    return jax.shard_map(
        on_device,
        mesh=mesh,
        in_specs=placed,
        out_specs=(P(None, "mer", "belt"), P(None, "mer", "belt")),
        check_vma=False,
    )
```

```python
import jax
import jax.numpy as jnp
from jax import lax
from jax.experimental import pallas as pl
from jax.experimental.pallas import tpu as pltpu
from jax.sharding import PartitionSpec as P

ITERS = 2
BLOCK_COLS = 256
LEVEL_BLOCK = 24


def tree_sum(values):
    for axis in ("mer", "belt"):
        count = lax.axis_size(axis)
        if count & (count - 1):
            values = lax.psum(values, axis)
            continue
        bit = 1
        while bit < count:
            values = values + lax.ppermute(values, axis, [(i, i ^ bit) for i in range(count)])
            bit *= 2
    return values


def column_spec(levels, rows, cols):
    return pl.BlockSpec((levels, rows, cols), lambda j: (0, 0, j))


def factor_solve_kernel(h_ref, e_ref, n_ref, v_ref, r_ref, eleft_ref, nsouth_ref,
                        inv_ref, ratio_ref, p_ref, part_ref):
    levels, rows, cols = h_ref.shape
    zero = jnp.zeros((rows, cols), jnp.float32)
    first_lane = lax.broadcasted_iota(jnp.int32, (rows, cols), 1) == 0
    first_row = lax.broadcasted_iota(jnp.int32, (rows, cols), 0) == 0

    def forward(k, up, down, prev, elim):
        east = e_ref[k]
        north = n_ref[k]
        west = jnp.where(first_lane, jnp.broadcast_to(eleft_ref[k], (rows, cols)),
                         pltpu.roll(east, 1, 1))
        south = jnp.where(first_row, jnp.broadcast_to(nsouth_ref[k], (rows, cols)),
                          pltpu.roll(north, 1, 0))
        diag = h_ref[k] + east + west + north + south + up + down
        ratio = down / prev
        pivot = diag - down * ratio
        inv_ref[k] = 1.0 / pivot
        ratio_ref[k] = ratio
        elim = r_ref[k] + ratio * elim
        p_ref[k] = elim
        return pivot, elim

    carry = forward(0, v_ref[0], zero, jnp.ones_like(zero), zero)
    carry = lax.fori_loop(
        1, levels - 1, lambda k, c: forward(k, v_ref[k], v_ref[k - 1], *c), carry, unroll=4
    )
    forward(levels - 1, zero, v_ref[levels - 2], *carry)

    def backward(k, up, succ, acc):
        value = inv_ref[k] * (p_ref[k] + up * succ)
        p_ref[k] = value
        return value, acc + r_ref[k] * value

    carry = backward(levels - 1, zero, zero, zero)
    carry = lax.fori_loop(
        0, levels - 1, lambda i, c: backward(levels - 2 - i, v_ref[levels - 2 - i], *c), carry,
        unroll=4,
    )
    part_ref[...] = carry[1]


def factor_solve(helm_diag, east_coef, north_coef, vert_coef, rhs, east_left, north_south):
    levels, rows, cols = rhs.shape
    block = BLOCK_COLS if cols % BLOCK_COLS == 0 else cols
    full = column_spec(levels, rows, block)
    vspec = column_spec(levels - 1, rows, block)
    field = jax.ShapeDtypeStruct(rhs.shape, jnp.float32)
    return pl.pallas_call(
        factor_solve_kernel,
        grid=(cols // block,),
        in_specs=[full, full, full, vspec, full,
                  pl.BlockSpec((None, levels, rows, 1), lambda j: (j, 0, 0, 0)),
                  pl.BlockSpec((levels, 1, block), lambda j: (0, 0, j))],
        out_specs=[full, full, full, pl.BlockSpec((rows, block), lambda j: (0, j))],
        out_shape=[field, field, field, jax.ShapeDtypeStruct((rows, cols), jnp.float32)],
    )(helm_diag, east_coef, north_coef, vert_coef, rhs, east_left, north_south)


def update_solve_kernel(step_ref, r_ref, img_ref, inv_ref, ratio_ref, v_ref,
                        res_ref, p_ref, part_ref):
    levels = r_ref.shape[0]
    step = step_ref[0]
    zero = jnp.zeros(r_ref.shape[1:], jnp.float32)

    def forward(k, elim):
        res = r_ref[k] - step * img_ref[k]
        res_ref[k] = res
        elim = res + ratio_ref[k] * elim
        p_ref[k] = elim
        return elim

    lax.fori_loop(0, levels, forward, zero, unroll=4)

    def backward(k, up, succ, acc):
        value = inv_ref[k] * (p_ref[k] + up * succ)
        p_ref[k] = value
        return value, acc + res_ref[k] * value

    carry = backward(levels - 1, zero, zero, zero)
    carry = lax.fori_loop(
        0, levels - 1, lambda i, c: backward(levels - 2 - i, v_ref[levels - 2 - i], *c), carry,
        unroll=4,
    )
    part_ref[...] = carry[1]


def update_solve(step, residual, image, inverse_pivot, ratio_values, vert_coef):
    levels, rows, cols = residual.shape
    block = BLOCK_COLS if cols % BLOCK_COLS == 0 else cols
    full = column_spec(levels, rows, block)
    vspec = column_spec(levels - 1, rows, block)
    field = jax.ShapeDtypeStruct(residual.shape, jnp.float32)
    return pl.pallas_call(
        update_solve_kernel,
        grid=(cols // block,),
        in_specs=[pl.BlockSpec(memory_space=pltpu.SMEM), full, full, full, full, vspec],
        out_specs=[full, full, pl.BlockSpec((rows, block), lambda j: (0, j))],
        out_shape=[field, field, jax.ShapeDtypeStruct((rows, cols), jnp.float32)],
    )(jnp.reshape(step, (1,)), residual, image, inverse_pivot, ratio_values, vert_coef)


def vertical_parts(vert_coef):
    zero_level = jnp.zeros((1,) + vert_coef.shape[1:], vert_coef.dtype)
    upper = jnp.concatenate([vert_coef, zero_level], axis=0)
    lower = jnp.concatenate([zero_level, vert_coef], axis=0)
    return (upper, lower)


def edge_tables(edge_num, row_start, rows, weight_index, edge_map, mortar_weights):
    maps = lax.dynamic_slice_in_dim(edge_map[edge_num], row_start, rows, 0)
    picks = lax.dynamic_slice_in_dim(weight_index[edge_num], row_start, rows, 0)
    return (maps[:, 0], maps[:, 1], mortar_weights[picks, 0], mortar_weights[picks, 1])


def belt_cols(field):
    count = lax.axis_size("belt")
    first = jnp.transpose(field[:, :, 0])
    last = jnp.transpose(field[:, :, -1])
    west = lax.ppermute(last, "belt", [(i, (i + 1) % count) for i in range(count)])
    east = lax.ppermute(first, "belt", [((i + 1) % count, i) for i in range(count)])
    return west, east


def mer_rows(field):
    count = lax.axis_size("mer")
    south = lax.ppermute(field[:, -1:, :], "mer", [(i, i + 1) for i in range(count - 1)])
    north = lax.ppermute(field[:, :1, :], "mer", [(i + 1, i) for i in range(count - 1)])
    return south, north


def gather_rows(column):
    count = lax.axis_size("mer")
    if count & (count - 1):
        return lax.all_gather(column, "mer", axis=0, tiled=True)
    me = lax.axis_index("mer")
    bit = 1
    while bit < count:
        other = lax.ppermute(column, "mer", [(i, i ^ bit) for i in range(count)])
        low_half = (me & bit) == 0
        column = jnp.concatenate(
            [jnp.where(low_half, column, other), jnp.where(low_half, other, column)], axis=0
        )
        bit *= 2
    return column


def as_lane_column(cols):
    return jnp.transpose(cols)[:, :, None]


def operator_kernel(extra, *refs):
    if extra:
        (v_ref, vab_ref, vbe_ref, h_ref, e_ref, n_ref, up_ref, lo_ref, ew_ref, ns_ref,
         ve_ref, vw_ref, vn_ref, vs_ref, d0_ref, img0_ref, img_ref, part_ref) = refs
    else:
        (v_ref, vab_ref, vbe_ref, h_ref, e_ref, n_ref, up_ref, lo_ref, ew_ref, ns_ref,
         ve_ref, vw_ref, vn_ref, vs_ref, img_ref, part_ref) = refs
    block, rows, cols = v_ref.shape
    i = pl.program_id(0)
    last_block = pl.num_programs(0) - 1
    lane = lax.broadcasted_iota(jnp.int32, (rows, cols), 1)
    row = lax.broadcasted_iota(jnp.int32, (rows, cols), 0)
    first_lane, last_lane = lane == 0, lane == cols - 1
    first_row, last_row = row == 0, row == rows - 1
    zero = jnp.zeros((rows, cols), jnp.float32)
    above = jnp.where(i == last_block, zero, vab_ref[0])
    below = jnp.where(i == 0, zero, vbe_ref[0])

    @pl.when(i == 0)
    def _():
        part_ref[...] = jnp.zeros_like(part_ref)

    def level(k, accs):
        v = v_ref[k]
        up_side = jnp.where(k == block - 1, above, v_ref[jnp.minimum(k + 1, block - 1)])
        down_side = jnp.where(k == 0, below, v_ref[jnp.maximum(k - 1, 0)])
        east_side = jnp.where(last_lane, jnp.broadcast_to(ve_ref[k], (rows, cols)),
                              pltpu.roll(v, cols - 1, 1))
        west_side = jnp.where(first_lane, jnp.broadcast_to(vw_ref[k], (rows, cols)),
                              pltpu.roll(v, 1, 1))
        north_side = jnp.where(last_row, jnp.broadcast_to(vn_ref[k], (rows, cols)),
                               pltpu.roll(v, rows - 1, 0))
        south_side = jnp.where(first_row, jnp.broadcast_to(vs_ref[k], (rows, cols)),
                               pltpu.roll(v, 1, 0))
        east = e_ref[k]
        north = n_ref[k]
        west = jnp.where(first_lane, jnp.broadcast_to(ew_ref[k], (rows, cols)),
                         pltpu.roll(east, 1, 1))
        south = jnp.where(first_row, jnp.broadcast_to(ns_ref[k], (rows, cols)),
                          pltpu.roll(north, 1, 0))
        image = (
            h_ref[k] * v
            + east * (v - east_side)
            + west * (v - west_side)
            + north * (v - north_side)
            + south * (v - south_side)
            + up_ref[k] * (v - up_side)
            + lo_ref[k] * (v - down_side)
        )
        img_ref[k] = image
        if extra:
            return (accs[0] + v * image, accs[1] + v * img0_ref[k], accs[2] + d0_ref[k] * image)
        return (accs[0] + v * image,)

    count = 3 if extra else 1
    accs = lax.fori_loop(0, block, level, (zero,) * count)
    for j in range(count):
        part_ref[j] = part_ref[j] + accs[j]


def apply_operator(direction, coefs, halos, extra=()):
    helm_diag, east_coef, north_coef, upper, lower, east_west, north_south = coefs
    east_halo, west_halo, north_halo, south_halo = halos
    levels, rows, cols = direction.shape
    block = LEVEL_BLOCK if levels % LEVEL_BLOCK == 0 else levels
    blocks = levels // block
    full = pl.BlockSpec((block, rows, cols), lambda i: (i, 0, 0))
    lane_col = pl.BlockSpec((block, rows, 1), lambda i: (i, 0, 0))
    first_col = pl.BlockSpec((None, block, rows, 1), lambda i: (0, i, 0, 0))
    row_spec = pl.BlockSpec((block, 1, cols), lambda i: (i, 0, 0))
    above = pl.BlockSpec((1, rows, cols), lambda i: (jnp.minimum((i + 1) * block, levels - 1), 0, 0))
    below = pl.BlockSpec((1, rows, cols), lambda i: (jnp.maximum(i * block - 1, 0), 0, 0))
    count = 3 if extra else 1
    kernel = lambda *refs: operator_kernel(bool(extra), *refs)
    image, part = pl.pallas_call(
        kernel,
        grid=(blocks,),
        in_specs=[full, above, below, full, full, full, full, full, first_col, row_spec,
                  lane_col, lane_col, row_spec, row_spec] + [full] * len(extra),
        out_specs=[full, pl.BlockSpec((count, rows, cols), lambda i: (0, 0, 0))],
        out_shape=[jax.ShapeDtypeStruct(direction.shape, jnp.float32),
                   jax.ShapeDtypeStruct((count, rows, cols), jnp.float32)],
    )(direction, direction, direction, helm_diag, east_coef, north_coef, upper, lower,
      east_west, north_south, east_halo, west_halo, north_halo, south_halo, *extra)
    return image, part


def exchange(direction, tables, use_mortar):
    west, east = belt_cols(direction)
    first_map, second_map, first_weight, second_weight = tables
    whole = gather_rows(east)
    arrived = first_weight[:, None] * whole[first_map] + second_weight[:, None] * whole[second_map]
    east = jnp.where(use_mortar, arrived, east)
    south, north = mer_rows(direction)
    return as_lane_column(east), as_lane_column(west), north, south


def on_device(
    right_side,
    helm_diag,
    east_coef,
    north_coef,
    vert_coef,
    mortar_weights,
    weight_index,
    edge_map,
    refined,
):
    belt_index = lax.axis_index("belt")
    mer_index = lax.axis_index("mer")
    per_panel = lax.axis_size("belt") // 4
    rows = right_side.shape[1]
    row_start = mer_index * rows
    own_edge = belt_index // per_panel
    row_flags = lax.dynamic_slice_in_dim(refined[own_edge], row_start, rows, 0)
    at_edge = (belt_index + 1) % per_panel == 0
    use_mortar = jnp.logical_and(at_edge, row_flags == 1)[:, None]
    tables = edge_tables(own_edge, row_start, rows, weight_index, edge_map, mortar_weights)
    levels, _, cols = right_side.shape
    block = BLOCK_COLS if cols % BLOCK_COLS == 0 else cols
    coef_west, _ = belt_cols(east_coef)
    coef_south, _ = mer_rows(north_coef)
    east_left = jnp.stack(
        [jnp.transpose(coef_west)]
        + [east_coef[:, :, j * block - 1] for j in range(1, cols // block)],
        axis=0,
    )[..., None]
    upper, lower = vertical_parts(vert_coef)
    coefs = (helm_diag, east_coef, north_coef, upper, lower, east_left, coef_south)

    inverse_pivot, ratio_values, precond0, part0 = factor_solve(
        helm_diag, east_coef, north_coef, vert_coef, right_side, east_left, coef_south
    )
    image0, curv_part0 = apply_operator(precond0, coefs, exchange(precond0, tables, use_mortar))
    first = tree_sum(jnp.stack([jnp.sum(part0), jnp.sum(curv_part0)]))
    norm0, curv0 = first[0], first[1]
    step0 = norm0 / curv0

    residual1, precond1, part1 = update_solve(
        step0, right_side, image0, inverse_pivot, ratio_values, vert_coef
    )
    image_p1, parts = apply_operator(
        precond1, coefs, exchange(precond1, tables, use_mortar), (precond0, image0)
    )
    second = tree_sum(jnp.concatenate([jnp.sum(part1)[None], jnp.sum(parts, axis=(1, 2))]))
    norm1 = second[0]
    beta = norm1 / norm0
    curv1 = second[1] + beta * (second[2] + second[3]) + beta * beta * curv0
    step1 = norm1 / curv1
    direction1 = precond1 + beta * precond0
    image1 = image_p1 + beta * image0
    solution = step0 * precond0 + step1 * direction1
    residual = residual1 - step1 * image1
    return (solution, residual)


def solution(mesh):
    placed = (
        P(None, "mer", "belt"),
        P(None, "mer", "belt"),
        P(None, "mer", "belt"),
        P(None, "mer", "belt"),
        P(None, "mer", "belt"),
        P(),
        P(),
        P(),
        P(),
    )
    return jax.shard_map(
        on_device,
        mesh=mesh,
        in_specs=placed,
        out_specs=(P(None, "mer", "belt"), P(None, "mer", "belt")),
        check_vma=False,
    )
```

```python
import jax
import jax.numpy as jnp
from jax import lax
from jax.experimental import pallas as pl
from jax.experimental.pallas import tpu as pltpu
from jax.sharding import PartitionSpec as P

ITERS = 2
BLOCK_COLS = 256
LEVEL_BLOCK = 24


def tree_sum(values):
    count = values.shape[0]
    values = jnp.zeros((8, 128), jnp.float32).at[0, :count].set(values)
    return _tree_sum(values)[0, :count]


def _tree_sum(values):
    for axis in ("mer", "belt"):
        count = lax.axis_size(axis)
        if count & (count - 1):
            values = lax.psum(values, axis)
            continue
        bit = 1
        while bit < count:
            values = values + lax.ppermute(values, axis, [(i, i ^ bit) for i in range(count)])
            bit *= 2
    return values


def column_spec(levels, rows, cols):
    return pl.BlockSpec((levels, rows, cols), lambda j: (0, 0, j))


def factor_solve_kernel(h_ref, e_ref, n_ref, v_ref, r_ref, eleft_ref, nsouth_ref,
                        inv_ref, ratio_ref, p_ref, part_ref):
    levels, rows, cols = h_ref.shape
    zero = jnp.zeros((rows, cols), jnp.float32)
    first_lane = lax.broadcasted_iota(jnp.int32, (rows, cols), 1) == 0
    first_row = lax.broadcasted_iota(jnp.int32, (rows, cols), 0) == 0

    def forward(k, up, down, prev, elim):
        east = e_ref[k]
        north = n_ref[k]
        west = jnp.where(first_lane, jnp.broadcast_to(eleft_ref[k], (rows, cols)),
                         pltpu.roll(east, 1, 1))
        south = jnp.where(first_row, jnp.broadcast_to(nsouth_ref[k], (rows, cols)),
                          pltpu.roll(north, 1, 0))
        diag = h_ref[k] + east + west + north + south + up + down
        ratio = down / prev
        pivot = diag - down * ratio
        inv_ref[k] = 1.0 / pivot
        ratio_ref[k] = ratio
        elim = r_ref[k] + ratio * elim
        p_ref[k] = elim
        return pivot, elim

    carry = forward(0, v_ref[0], zero, jnp.ones_like(zero), zero)
    carry = lax.fori_loop(
        1, levels - 1, lambda k, c: forward(k, v_ref[k], v_ref[k - 1], *c), carry, unroll=4
    )
    forward(levels - 1, zero, v_ref[levels - 2], *carry)

    def backward(k, up, succ, acc):
        value = inv_ref[k] * (p_ref[k] + up * succ)
        p_ref[k] = value
        return value, acc + r_ref[k] * value

    carry = backward(levels - 1, zero, zero, zero)
    carry = lax.fori_loop(
        0, levels - 1, lambda i, c: backward(levels - 2 - i, v_ref[levels - 2 - i], *c), carry,
        unroll=4,
    )
    part_ref[...] = carry[1]


def factor_solve(helm_diag, east_coef, north_coef, vert_coef, rhs, east_left, north_south):
    levels, rows, cols = rhs.shape
    block = BLOCK_COLS if cols % BLOCK_COLS == 0 else cols
    full = column_spec(levels, rows, block)
    vspec = column_spec(levels - 1, rows, block)
    field = jax.ShapeDtypeStruct(rhs.shape, jnp.float32)
    return pl.pallas_call(
        factor_solve_kernel,
        grid=(cols // block,),
        in_specs=[full, full, full, vspec, full,
                  pl.BlockSpec((None, levels, rows, 1), lambda j: (j, 0, 0, 0)),
                  pl.BlockSpec((levels, 1, block), lambda j: (0, 0, j))],
        out_specs=[full, full, full, pl.BlockSpec((rows, block), lambda j: (0, j))],
        out_shape=[field, field, field, jax.ShapeDtypeStruct((rows, cols), jnp.float32)],
    )(helm_diag, east_coef, north_coef, vert_coef, rhs, east_left, north_south)


def solve_kernel(count, *refs):
    val_ref, inv_ref, ratio_ref, v_ref = refs[:4]
    partner_refs = refs[4:4 + count]
    p_ref, part_ref = refs[4 + count:]
    levels = val_ref.shape[0]
    zero = jnp.zeros(val_ref.shape[1:], jnp.float32)

    def forward(k, elim):
        elim = val_ref[k] + ratio_ref[k] * elim
        p_ref[k] = elim
        return elim

    lax.fori_loop(0, levels, forward, zero, unroll=4)

    def backward(k, up, succ, accs):
        value = inv_ref[k] * (p_ref[k] + up * succ)
        p_ref[k] = value
        return value, tuple(acc + ref[k] * value for acc, ref in zip(accs, partner_refs))

    carry = backward(levels - 1, zero, zero, (zero,) * count)
    carry = lax.fori_loop(
        0, levels - 1, lambda i, c: backward(levels - 2 - i, v_ref[levels - 2 - i], *c), carry,
        unroll=4,
    )
    for j in range(count):
        part_ref[j] = carry[1][j]


def solve(values, inverse_pivot, ratio_values, vert_coef, partners):
    levels, rows, cols = values.shape
    block = BLOCK_COLS if cols % BLOCK_COLS == 0 else cols
    full = column_spec(levels, rows, block)
    vspec = column_spec(levels - 1, rows, block)
    count = len(partners)
    return pl.pallas_call(
        lambda *refs: solve_kernel(count, *refs),
        grid=(cols // block,),
        in_specs=[full, full, full, vspec] + [full] * count,
        out_specs=[full, pl.BlockSpec((count, rows, block), lambda j: (0, 0, j))],
        out_shape=[jax.ShapeDtypeStruct(values.shape, jnp.float32),
                   jax.ShapeDtypeStruct((count, rows, cols), jnp.float32)],
    )(values, inverse_pivot, ratio_values, vert_coef, *partners)


def vertical_parts(vert_coef):
    zero_level = jnp.zeros((1,) + vert_coef.shape[1:], vert_coef.dtype)
    upper = jnp.concatenate([vert_coef, zero_level], axis=0)
    lower = jnp.concatenate([zero_level, vert_coef], axis=0)
    return (upper, lower)


def edge_tables(edge_num, row_start, rows, weight_index, edge_map, mortar_weights):
    maps = lax.dynamic_slice_in_dim(edge_map[edge_num], row_start, rows, 0)
    picks = lax.dynamic_slice_in_dim(weight_index[edge_num], row_start, rows, 0)
    return (maps[:, 0], maps[:, 1], mortar_weights[picks, 0], mortar_weights[picks, 1])


def belt_cols(field):
    count = lax.axis_size("belt")
    first = jnp.transpose(field[:, :, 0])
    last = jnp.transpose(field[:, :, -1])
    west = lax.ppermute(last, "belt", [(i, (i + 1) % count) for i in range(count)])
    east = lax.ppermute(first, "belt", [((i + 1) % count, i) for i in range(count)])
    return west, east


def mer_rows(field):
    count = lax.axis_size("mer")
    south = lax.ppermute(field[:, -1:, :], "mer", [(i, i + 1) for i in range(count - 1)])
    north = lax.ppermute(field[:, :1, :], "mer", [(i + 1, i) for i in range(count - 1)])
    return south, north


def gather_rows(column):
    count = lax.axis_size("mer")
    if count & (count - 1):
        return lax.all_gather(column, "mer", axis=0, tiled=True)
    me = lax.axis_index("mer")
    bit = 1
    while bit < count:
        other = lax.ppermute(column, "mer", [(i, i ^ bit) for i in range(count)])
        low_half = (me & bit) == 0
        column = jnp.concatenate(
            [jnp.where(low_half, column, other), jnp.where(low_half, other, column)], axis=0
        )
        bit *= 2
    return column


def as_lane_column(cols):
    return jnp.transpose(cols)[:, :, None]


def operator_kernel(extra, *refs):
    (v_ref, vab_ref, vbe_ref, h_ref, e_ref, n_ref, up_ref, lo_ref, ew_ref, ns_ref,
     ve_ref, vw_ref, vn_ref, vs_ref) = refs[:14]
    partner_refs = (v_ref,) + refs[14:14 + extra]
    img_ref, part_ref = refs[14 + extra:]
    block, rows, cols = v_ref.shape
    i = pl.program_id(0)
    last_block = pl.num_programs(0) - 1
    lane = lax.broadcasted_iota(jnp.int32, (rows, cols), 1)
    row = lax.broadcasted_iota(jnp.int32, (rows, cols), 0)
    first_lane, last_lane = lane == 0, lane == cols - 1
    first_row, last_row = row == 0, row == rows - 1
    zero = jnp.zeros((rows, cols), jnp.float32)
    above = jnp.where(i == last_block, zero, vab_ref[0])
    below = jnp.where(i == 0, zero, vbe_ref[0])

    @pl.when(i == 0)
    def _():
        part_ref[...] = jnp.zeros_like(part_ref)

    def level(k, accs):
        v = v_ref[k]
        up_side = jnp.where(k == block - 1, above, v_ref[jnp.minimum(k + 1, block - 1)])
        down_side = jnp.where(k == 0, below, v_ref[jnp.maximum(k - 1, 0)])
        east_side = jnp.where(last_lane, jnp.broadcast_to(ve_ref[k], (rows, cols)),
                              pltpu.roll(v, cols - 1, 1))
        west_side = jnp.where(first_lane, jnp.broadcast_to(vw_ref[k], (rows, cols)),
                              pltpu.roll(v, 1, 1))
        north_side = jnp.where(last_row, jnp.broadcast_to(vn_ref[k], (rows, cols)),
                               pltpu.roll(v, rows - 1, 0))
        south_side = jnp.where(first_row, jnp.broadcast_to(vs_ref[k], (rows, cols)),
                               pltpu.roll(v, 1, 0))
        east = e_ref[k]
        north = n_ref[k]
        west = jnp.where(first_lane, jnp.broadcast_to(ew_ref[k], (rows, cols)),
                         pltpu.roll(east, 1, 1))
        south = jnp.where(first_row, jnp.broadcast_to(ns_ref[k], (rows, cols)),
                          pltpu.roll(north, 1, 0))
        image = (
            h_ref[k] * v
            + east * (v - east_side)
            + west * (v - west_side)
            + north * (v - north_side)
            + south * (v - south_side)
            + up_ref[k] * (v - up_side)
            + lo_ref[k] * (v - down_side)
        )
        img_ref[k] = image
        return tuple(acc + ref[k] * image for acc, ref in zip(accs, partner_refs))

    count = 1 + extra
    accs = lax.fori_loop(0, block, level, (zero,) * count)
    for j in range(count):
        part_ref[j] = part_ref[j] + accs[j]


def apply_operator(direction, coefs, halos, extra=()):
    helm_diag, east_coef, north_coef, upper, lower, east_west, north_south = coefs
    east_halo, west_halo, north_halo, south_halo = halos
    levels, rows, cols = direction.shape
    block = LEVEL_BLOCK if levels % LEVEL_BLOCK == 0 else levels
    blocks = levels // block
    full = pl.BlockSpec((block, rows, cols), lambda i: (i, 0, 0))
    lane_col = pl.BlockSpec((block, rows, 1), lambda i: (i, 0, 0))
    first_col = pl.BlockSpec((None, block, rows, 1), lambda i: (0, i, 0, 0))
    row_spec = pl.BlockSpec((block, 1, cols), lambda i: (i, 0, 0))
    above = pl.BlockSpec((1, rows, cols), lambda i: (jnp.minimum((i + 1) * block, levels - 1), 0, 0))
    below = pl.BlockSpec((1, rows, cols), lambda i: (jnp.maximum(i * block - 1, 0), 0, 0))
    count = 1 + len(extra)
    kernel = lambda *refs: operator_kernel(len(extra), *refs)
    image, part = pl.pallas_call(
        kernel,
        grid=(blocks,),
        in_specs=[full, above, below, full, full, full, full, full, first_col, row_spec,
                  lane_col, lane_col, row_spec, row_spec] + [full] * len(extra),
        out_specs=[full, pl.BlockSpec((count, rows, cols), lambda i: (0, 0, 0))],
        out_shape=[jax.ShapeDtypeStruct(direction.shape, jnp.float32),
                   jax.ShapeDtypeStruct((count, rows, cols), jnp.float32)],
    )(direction, direction, direction, helm_diag, east_coef, north_coef, upper, lower,
      east_west, north_south, east_halo, west_halo, north_halo, south_halo, *extra)
    return image, part


def exchange(direction, tables, use_mortar):
    west, east = belt_cols(direction)
    first_map, second_map, first_weight, second_weight = tables
    whole = gather_rows(east)
    arrived = first_weight[:, None] * whole[first_map] + second_weight[:, None] * whole[second_map]
    east = jnp.where(use_mortar, arrived, east)
    south, north = mer_rows(direction)
    return as_lane_column(east), as_lane_column(west), north, south


def on_device(
    right_side,
    helm_diag,
    east_coef,
    north_coef,
    vert_coef,
    mortar_weights,
    weight_index,
    edge_map,
    refined,
):
    belt_index = lax.axis_index("belt")
    mer_index = lax.axis_index("mer")
    per_panel = lax.axis_size("belt") // 4
    rows = right_side.shape[1]
    row_start = mer_index * rows
    own_edge = belt_index // per_panel
    row_flags = lax.dynamic_slice_in_dim(refined[own_edge], row_start, rows, 0)
    at_edge = (belt_index + 1) % per_panel == 0
    use_mortar = jnp.logical_and(at_edge, row_flags == 1)[:, None]
    tables = edge_tables(own_edge, row_start, rows, weight_index, edge_map, mortar_weights)
    levels, _, cols = right_side.shape
    block = BLOCK_COLS if cols % BLOCK_COLS == 0 else cols
    coef_west, _ = belt_cols(east_coef)
    coef_south, _ = mer_rows(north_coef)
    east_left = jnp.stack(
        [jnp.transpose(coef_west)]
        + [east_coef[:, :, j * block - 1] for j in range(1, cols // block)],
        axis=0,
    )[..., None]
    upper, lower = vertical_parts(vert_coef)
    coefs = (helm_diag, east_coef, north_coef, upper, lower, east_left, coef_south)

    inverse_pivot, ratio_values, precond0, part0 = factor_solve(
        helm_diag, east_coef, north_coef, vert_coef, right_side, east_left, coef_south
    )
    image0, curv_part0 = apply_operator(precond0, coefs, exchange(precond0, tables, use_mortar))
    basis, basis_part = solve(image0, inverse_pivot, ratio_values, vert_coef,
                              (right_side, image0))
    image_q, image_q_part = apply_operator(
        basis, coefs, exchange(basis, tables, use_mortar), (precond0,)
    )
    sums = tree_sum(jnp.stack([
        jnp.sum(part0), jnp.sum(curv_part0), jnp.sum(basis_part[0]), jnp.sum(basis_part[1]),
        jnp.sum(image_q_part[0]), jnp.sum(image_q_part[1]),
    ]))
    norm0, curv0, r0q, a0q, qaq, p0aq = (sums[j] for j in range(6))
    step0 = norm0 / curv0
    norm1 = norm0 - step0 * (r0q + curv0) + step0 * step0 * a0q
    p1ap1 = curv0 - step0 * (p0aq + a0q) + step0 * step0 * qaq
    p1a0 = curv0 - step0 * a0q
    d0ap1 = curv0 - step0 * p0aq
    beta = norm1 / norm0
    curv1 = p1ap1 + beta * (p1a0 + d0ap1) + beta * beta * curv0
    step1 = norm1 / curv1
    precond1 = precond0 - step0 * basis
    residual1 = right_side - step0 * image0
    direction1 = precond1 + beta * precond0
    image1 = (image0 - step0 * image_q) + beta * image0
    solution = step0 * precond0 + step1 * direction1
    residual = residual1 - step1 * image1
    return (solution, residual)


def solution(mesh):
    placed = (
        P(None, "mer", "belt"),
        P(None, "mer", "belt"),
        P(None, "mer", "belt"),
        P(None, "mer", "belt"),
        P(None, "mer", "belt"),
        P(),
        P(),
        P(),
        P(),
    )
    return jax.shard_map(
        on_device,
        mesh=mesh,
        in_specs=placed,
        out_specs=(P(None, "mer", "belt"), P(None, "mer", "belt")),
        check_vma=False,
    )
```

```python
import jax
import jax.numpy as jnp
from jax import lax
from jax.experimental import pallas as pl
from jax.experimental.pallas import tpu as pltpu
from jax.sharding import PartitionSpec as P

ITERS = 2
BLOCK_COLS = 256
LEVEL_BLOCK = 24


def tree_sum(values):
    for axis in ("mer", "belt"):
        count = lax.axis_size(axis)
        if count & (count - 1):
            values = lax.psum(values, axis)
            continue
        bit = 1
        while bit < count:
            values = values + lax.ppermute(values, axis, [(i, i ^ bit) for i in range(count)])
            bit *= 2
    return values


def add_totals(part_ref, slots, accs):
    row = lax.broadcasted_iota(jnp.int32, part_ref.shape, 0)
    tile = part_ref[...]
    for slot, acc in zip(slots, accs):
        tile = tile + jnp.where(row == slot, jnp.sum(acc), 0.0)
    part_ref[...] = tile


def tile_spec():
    return pl.BlockSpec((8, 128), lambda j: (0, 0))


def tile_shape():
    return jax.ShapeDtypeStruct((8, 128), jnp.float32)


def column_spec(levels, rows, cols):
    return pl.BlockSpec((levels, rows, cols), lambda j: (0, 0, j))


def factor_solve_kernel(h_ref, e_ref, n_ref, v_ref, r_ref, eleft_ref, nsouth_ref,
                        inv_ref, ratio_ref, p_ref, part_ref):
    levels, rows, cols = h_ref.shape

    @pl.when(pl.program_id(0) == 0)
    def _():
        part_ref[...] = jnp.zeros_like(part_ref)

    zero = jnp.zeros((rows, cols), jnp.float32)
    first_lane = lax.broadcasted_iota(jnp.int32, (rows, cols), 1) == 0
    first_row = lax.broadcasted_iota(jnp.int32, (rows, cols), 0) == 0

    def forward(k, up, down, prev, elim):
        east = e_ref[k]
        north = n_ref[k]
        west = jnp.where(first_lane, jnp.broadcast_to(eleft_ref[k], (rows, cols)),
                         pltpu.roll(east, 1, 1))
        south = jnp.where(first_row, jnp.broadcast_to(nsouth_ref[k], (rows, cols)),
                          pltpu.roll(north, 1, 0))
        diag = h_ref[k] + east + west + north + south + up + down
        ratio = down / prev
        pivot = diag - down * ratio
        inv_ref[k] = 1.0 / pivot
        ratio_ref[k] = ratio
        elim = r_ref[k] + ratio * elim
        p_ref[k] = elim
        return pivot, elim

    carry = forward(0, v_ref[0], zero, jnp.ones_like(zero), zero)
    carry = lax.fori_loop(
        1, levels - 1, lambda k, c: forward(k, v_ref[k], v_ref[k - 1], *c), carry, unroll=4
    )
    forward(levels - 1, zero, v_ref[levels - 2], *carry)

    def backward(k, up, succ, acc):
        value = inv_ref[k] * (p_ref[k] + up * succ)
        p_ref[k] = value
        return value, acc + r_ref[k] * value

    carry = backward(levels - 1, zero, zero, zero)
    carry = lax.fori_loop(
        0, levels - 1, lambda i, c: backward(levels - 2 - i, v_ref[levels - 2 - i], *c), carry,
        unroll=4,
    )
    add_totals(part_ref, (0,), (carry[1],))


def factor_solve(helm_diag, east_coef, north_coef, vert_coef, rhs, east_left, north_south):
    levels, rows, cols = rhs.shape
    block = BLOCK_COLS if cols % BLOCK_COLS == 0 else cols
    full = column_spec(levels, rows, block)
    vspec = column_spec(levels - 1, rows, block)
    field = jax.ShapeDtypeStruct(rhs.shape, jnp.float32)
    return pl.pallas_call(
        factor_solve_kernel,
        grid=(cols // block,),
        in_specs=[full, full, full, vspec, full,
                  pl.BlockSpec((None, levels, rows, 1), lambda j: (j, 0, 0, 0)),
                  pl.BlockSpec((levels, 1, block), lambda j: (0, 0, j))],
        out_specs=[full, full, full, tile_spec()],
        out_shape=[field, field, field, tile_shape()],
    )(helm_diag, east_coef, north_coef, vert_coef, rhs, east_left, north_south)


def solve_kernel(slots, *refs):
    count = len(slots)
    val_ref, inv_ref, ratio_ref, v_ref = refs[:4]
    partner_refs = refs[4:4 + count]
    p_ref, part_ref = refs[4 + count:]
    levels = val_ref.shape[0]
    zero = jnp.zeros(val_ref.shape[1:], jnp.float32)

    @pl.when(pl.program_id(0) == 0)
    def _():
        part_ref[...] = jnp.zeros_like(part_ref)

    def forward(k, elim):
        elim = val_ref[k] + ratio_ref[k] * elim
        p_ref[k] = elim
        return elim

    lax.fori_loop(0, levels, forward, zero, unroll=4)

    def backward(k, up, succ, accs):
        value = inv_ref[k] * (p_ref[k] + up * succ)
        p_ref[k] = value
        return value, tuple(acc + ref[k] * value for acc, ref in zip(accs, partner_refs))

    carry = backward(levels - 1, zero, zero, (zero,) * count)
    carry = lax.fori_loop(
        0, levels - 1, lambda i, c: backward(levels - 2 - i, v_ref[levels - 2 - i], *c), carry,
        unroll=4,
    )
    add_totals(part_ref, slots, carry[1])


def solve(values, inverse_pivot, ratio_values, vert_coef, partners, slots):
    levels, rows, cols = values.shape
    block = BLOCK_COLS if cols % BLOCK_COLS == 0 else cols
    full = column_spec(levels, rows, block)
    vspec = column_spec(levels - 1, rows, block)
    return pl.pallas_call(
        lambda *refs: solve_kernel(slots, *refs),
        grid=(cols // block,),
        in_specs=[full, full, full, vspec] + [full] * len(partners),
        out_specs=[full, tile_spec()],
        out_shape=[jax.ShapeDtypeStruct(values.shape, jnp.float32), tile_shape()],
    )(values, inverse_pivot, ratio_values, vert_coef, *partners)


def vertical_parts(vert_coef):
    zero_level = jnp.zeros((1,) + vert_coef.shape[1:], vert_coef.dtype)
    upper = jnp.concatenate([vert_coef, zero_level], axis=0)
    lower = jnp.concatenate([zero_level, vert_coef], axis=0)
    return (upper, lower)


def edge_tables(edge_num, row_start, rows, weight_index, edge_map, mortar_weights):
    maps = lax.dynamic_slice_in_dim(edge_map[edge_num], row_start, rows, 0)
    picks = lax.dynamic_slice_in_dim(weight_index[edge_num], row_start, rows, 0)
    return (maps[:, 0], maps[:, 1], mortar_weights[picks, 0], mortar_weights[picks, 1])


def belt_cols(field):
    count = lax.axis_size("belt")
    first = jnp.transpose(field[:, :, 0])
    last = jnp.transpose(field[:, :, -1])
    west = lax.ppermute(last, "belt", [(i, (i + 1) % count) for i in range(count)])
    east = lax.ppermute(first, "belt", [((i + 1) % count, i) for i in range(count)])
    return west, east


def mer_rows(field):
    count = lax.axis_size("mer")
    south = lax.ppermute(field[:, -1:, :], "mer", [(i, i + 1) for i in range(count - 1)])
    north = lax.ppermute(field[:, :1, :], "mer", [(i + 1, i) for i in range(count - 1)])
    return south, north


def gather_rows(column):
    count = lax.axis_size("mer")
    if count & (count - 1):
        return lax.all_gather(column, "mer", axis=0, tiled=True)
    me = lax.axis_index("mer")
    bit = 1
    while bit < count:
        other = lax.ppermute(column, "mer", [(i, i ^ bit) for i in range(count)])
        low_half = (me & bit) == 0
        column = jnp.concatenate(
            [jnp.where(low_half, column, other), jnp.where(low_half, other, column)], axis=0
        )
        bit *= 2
    return column


def as_lane_column(cols):
    return jnp.transpose(cols)[:, :, None]


def operator_kernel(slots, *refs):
    extra = len(slots) - 1
    (v_ref, vab_ref, vbe_ref, h_ref, e_ref, n_ref, up_ref, lo_ref, ew_ref, ns_ref,
     ve_ref, vw_ref, vn_ref, vs_ref) = refs[:14]
    partner_refs = (v_ref,) + refs[14:14 + extra]
    img_ref, part_ref = refs[14 + extra:]
    block, rows, cols = v_ref.shape
    i = pl.program_id(0)
    last_block = pl.num_programs(0) - 1
    lane = lax.broadcasted_iota(jnp.int32, (rows, cols), 1)
    row = lax.broadcasted_iota(jnp.int32, (rows, cols), 0)
    first_lane, last_lane = lane == 0, lane == cols - 1
    first_row, last_row = row == 0, row == rows - 1
    zero = jnp.zeros((rows, cols), jnp.float32)
    above = jnp.where(i == last_block, zero, vab_ref[0])
    below = jnp.where(i == 0, zero, vbe_ref[0])

    @pl.when(i == 0)
    def _():
        part_ref[...] = jnp.zeros_like(part_ref)

    def level(k, accs):
        v = v_ref[k]
        up_side = jnp.where(k == block - 1, above, v_ref[jnp.minimum(k + 1, block - 1)])
        down_side = jnp.where(k == 0, below, v_ref[jnp.maximum(k - 1, 0)])
        east_side = jnp.where(last_lane, jnp.broadcast_to(ve_ref[k], (rows, cols)),
                              pltpu.roll(v, cols - 1, 1))
        west_side = jnp.where(first_lane, jnp.broadcast_to(vw_ref[k], (rows, cols)),
                              pltpu.roll(v, 1, 1))
        north_side = jnp.where(last_row, jnp.broadcast_to(vn_ref[k], (rows, cols)),
                               pltpu.roll(v, rows - 1, 0))
        south_side = jnp.where(first_row, jnp.broadcast_to(vs_ref[k], (rows, cols)),
                               pltpu.roll(v, 1, 0))
        east = e_ref[k]
        north = n_ref[k]
        west = jnp.where(first_lane, jnp.broadcast_to(ew_ref[k], (rows, cols)),
                         pltpu.roll(east, 1, 1))
        south = jnp.where(first_row, jnp.broadcast_to(ns_ref[k], (rows, cols)),
                          pltpu.roll(north, 1, 0))
        image = (
            h_ref[k] * v
            + east * (v - east_side)
            + west * (v - west_side)
            + north * (v - north_side)
            + south * (v - south_side)
            + up_ref[k] * (v - up_side)
            + lo_ref[k] * (v - down_side)
        )
        img_ref[k] = image
        return tuple(acc + ref[k] * image for acc, ref in zip(accs, partner_refs))

    accs = lax.fori_loop(0, block, level, (zero,) * len(slots))
    add_totals(part_ref, slots, accs)


def apply_operator(direction, coefs, halos, slots, extra=()):
    helm_diag, east_coef, north_coef, upper, lower, east_west, north_south = coefs
    east_halo, west_halo, north_halo, south_halo = halos
    levels, rows, cols = direction.shape
    block = LEVEL_BLOCK if levels % LEVEL_BLOCK == 0 else levels
    blocks = levels // block
    full = pl.BlockSpec((block, rows, cols), lambda i: (i, 0, 0))
    lane_col = pl.BlockSpec((block, rows, 1), lambda i: (i, 0, 0))
    first_col = pl.BlockSpec((None, block, rows, 1), lambda i: (0, i, 0, 0))
    row_spec = pl.BlockSpec((block, 1, cols), lambda i: (i, 0, 0))
    above = pl.BlockSpec((1, rows, cols), lambda i: (jnp.minimum((i + 1) * block, levels - 1), 0, 0))
    below = pl.BlockSpec((1, rows, cols), lambda i: (jnp.maximum(i * block - 1, 0), 0, 0))
    kernel = lambda *refs: operator_kernel(slots, *refs)
    image, part = pl.pallas_call(
        kernel,
        grid=(blocks,),
        in_specs=[full, above, below, full, full, full, full, full, first_col, row_spec,
                  lane_col, lane_col, row_spec, row_spec] + [full] * len(extra),
        out_specs=[full, tile_spec()],
        out_shape=[jax.ShapeDtypeStruct(direction.shape, jnp.float32), tile_shape()],
    )(direction, direction, direction, helm_diag, east_coef, north_coef, upper, lower,
      east_west, north_south, east_halo, west_halo, north_halo, south_halo, *extra)
    return image, part


def finish_kernel(sums_ref, p0_ref, q_ref, r0_ref, a0_ref, aq_ref, sol_ref, res_ref):
    block, rows, cols = p0_ref.shape
    sums = sums_ref[...]
    norm0, curv0, r0q, a0q, qaq, p0aq = (
        jnp.broadcast_to(sums[j:j + 1, :], sums.shape) for j in range(6)
    )
    step0 = norm0 / curv0
    norm1 = norm0 - step0 * (r0q + curv0) + step0 * step0 * a0q
    p1ap1 = curv0 - step0 * (p0aq + a0q) + step0 * step0 * qaq
    p1a0 = curv0 - step0 * a0q
    d0ap1 = curv0 - step0 * p0aq
    beta = norm1 / norm0
    curv1 = p1ap1 + beta * (p1a0 + d0ap1) + beta * beta * curv0
    step1 = norm1 / curv1
    widen = lambda x: jnp.concatenate([x[:rows]] * (cols // x.shape[1]), axis=1)
    step0, beta, step1 = widen(step0), widen(beta), widen(step1)

    def level(k, carry):
        p0 = p0_ref[k]
        a0 = a0_ref[k]
        precond1 = p0 - step0 * q_ref[k]
        direction1 = precond1 + beta * p0
        image1 = (a0 - step0 * aq_ref[k]) + beta * a0
        sol_ref[k] = step0 * p0 + step1 * direction1
        res_ref[k] = (r0_ref[k] - step0 * a0) - step1 * image1
        return carry

    lax.fori_loop(0, block, level, 0)


def finish(sums, precond0, basis, right_side, image0, image_q):
    levels, rows, cols = precond0.shape
    block = LEVEL_BLOCK if levels % LEVEL_BLOCK == 0 else levels
    full = pl.BlockSpec((block, rows, cols), lambda i: (i, 0, 0))
    field = jax.ShapeDtypeStruct(precond0.shape, jnp.float32)
    return pl.pallas_call(
        finish_kernel,
        grid=(levels // block,),
        in_specs=[tile_spec(), full, full, full, full, full],
        out_specs=[full, full],
        out_shape=[field, field],
    )(sums, precond0, basis, right_side, image0, image_q)


def exchange(direction, tables, use_mortar):
    west, east = belt_cols(direction)
    first_map, second_map, first_weight, second_weight = tables
    whole = gather_rows(east)
    arrived = first_weight[:, None] * whole[first_map] + second_weight[:, None] * whole[second_map]
    east = jnp.where(use_mortar, arrived, east)
    south, north = mer_rows(direction)
    return as_lane_column(east), as_lane_column(west), north, south


def on_device(
    right_side,
    helm_diag,
    east_coef,
    north_coef,
    vert_coef,
    mortar_weights,
    weight_index,
    edge_map,
    refined,
):
    belt_index = lax.axis_index("belt")
    mer_index = lax.axis_index("mer")
    per_panel = lax.axis_size("belt") // 4
    rows = right_side.shape[1]
    row_start = mer_index * rows
    own_edge = belt_index // per_panel
    row_flags = lax.dynamic_slice_in_dim(refined[own_edge], row_start, rows, 0)
    at_edge = (belt_index + 1) % per_panel == 0
    use_mortar = jnp.logical_and(at_edge, row_flags == 1)[:, None]
    tables = edge_tables(own_edge, row_start, rows, weight_index, edge_map, mortar_weights)
    levels, _, cols = right_side.shape
    block = BLOCK_COLS if cols % BLOCK_COLS == 0 else cols
    coef_west, _ = belt_cols(east_coef)
    coef_south, _ = mer_rows(north_coef)
    east_left = jnp.stack(
        [jnp.transpose(coef_west)]
        + [east_coef[:, :, j * block - 1] for j in range(1, cols // block)],
        axis=0,
    )[..., None]
    upper, lower = vertical_parts(vert_coef)
    coefs = (helm_diag, east_coef, north_coef, upper, lower, east_left, coef_south)

    inverse_pivot, ratio_values, precond0, part0 = factor_solve(
        helm_diag, east_coef, north_coef, vert_coef, right_side, east_left, coef_south
    )
    image0, curv_part0 = apply_operator(
        precond0, coefs, exchange(precond0, tables, use_mortar), (1,)
    )
    basis, basis_part = solve(image0, inverse_pivot, ratio_values, vert_coef,
                              (right_side, image0), (2, 3))
    image_q, image_q_part = apply_operator(
        basis, coefs, exchange(basis, tables, use_mortar), (4, 5), (precond0,)
    )
    sums = tree_sum(part0 + curv_part0 + basis_part + image_q_part)
    return finish(sums, precond0, basis, right_side, image0, image_q)


def solution(mesh):
    placed = (
        P(None, "mer", "belt"),
        P(None, "mer", "belt"),
        P(None, "mer", "belt"),
        P(None, "mer", "belt"),
        P(None, "mer", "belt"),
        P(),
        P(),
        P(),
        P(),
    )
    return jax.shard_map(
        on_device,
        mesh=mesh,
        in_specs=placed,
        out_specs=(P(None, "mer", "belt"), P(None, "mer", "belt")),
        check_vma=False,
    )
```

```python
import jax
import jax.numpy as jnp
from jax import lax
from jax.experimental import pallas as pl
from jax.experimental.pallas import tpu as pltpu
from jax.sharding import PartitionSpec as P

ITERS = 2
BLOCK_COLS = 384
LEVEL_BLOCK = 24


def tree_sum(values):
    for axis in ("mer", "belt"):
        count = lax.axis_size(axis)
        if count & (count - 1):
            values = lax.psum(values, axis)
            continue
        bit = 1
        while bit < count:
            values = values + lax.ppermute(values, axis, [(i, i ^ bit) for i in range(count)])
            bit *= 2
    return values


def add_totals(part_ref, slots, accs):
    row = lax.broadcasted_iota(jnp.int32, part_ref.shape, 0)
    tile = part_ref[...]
    for slot, acc in zip(slots, accs):
        tile = tile + jnp.where(row == slot, jnp.sum(acc), 0.0)
    part_ref[...] = tile


def tile_spec():
    return pl.BlockSpec((8, 128), lambda j: (0, 0))


def tile_shape():
    return jax.ShapeDtypeStruct((8, 128), jnp.float32)


def column_spec(levels, rows, cols):
    return pl.BlockSpec((levels, rows, cols), lambda j: (0, 0, j))


def factor_solve_kernel(h_ref, e_ref, n_ref, v_ref, r_ref, eleft_ref, nsouth_ref,
                        inv_ref, ratio_ref, p_ref, part_ref):
    levels, rows, cols = h_ref.shape

    @pl.when(pl.program_id(0) == 0)
    def _():
        part_ref[...] = jnp.zeros_like(part_ref)

    zero = jnp.zeros((rows, cols), jnp.float32)
    first_lane = lax.broadcasted_iota(jnp.int32, (rows, cols), 1) == 0
    first_row = lax.broadcasted_iota(jnp.int32, (rows, cols), 0) == 0

    def forward(k, up, down, prev, elim):
        east = e_ref[k]
        north = n_ref[k]
        west = jnp.where(first_lane, jnp.broadcast_to(eleft_ref[k], (rows, cols)),
                         pltpu.roll(east, 1, 1))
        south = jnp.where(first_row, jnp.broadcast_to(nsouth_ref[k], (rows, cols)),
                          pltpu.roll(north, 1, 0))
        diag = h_ref[k] + east + west + north + south + up + down
        ratio = down / prev
        pivot = diag - down * ratio
        inv_ref[k] = 1.0 / pivot
        ratio_ref[k] = ratio
        elim = r_ref[k] + ratio * elim
        p_ref[k] = elim
        return pivot, elim

    carry = forward(0, v_ref[0], zero, jnp.ones_like(zero), zero)
    carry = lax.fori_loop(
        1, levels - 1, lambda k, c: forward(k, v_ref[k], v_ref[k - 1], *c), carry, unroll=4
    )
    forward(levels - 1, zero, v_ref[levels - 2], *carry)

    def backward(k, up, succ, acc):
        value = inv_ref[k] * (p_ref[k] + up * succ)
        p_ref[k] = value
        return value, acc + r_ref[k] * value

    carry = backward(levels - 1, zero, zero, zero)
    carry = lax.fori_loop(
        0, levels - 1, lambda i, c: backward(levels - 2 - i, v_ref[levels - 2 - i], *c), carry,
        unroll=4,
    )
    add_totals(part_ref, (0,), (carry[1],))


def factor_solve(helm_diag, east_coef, north_coef, vert_coef, rhs, east_left, north_south):
    levels, rows, cols = rhs.shape
    block = BLOCK_COLS if cols % BLOCK_COLS == 0 else cols
    full = column_spec(levels, rows, block)
    vspec = column_spec(levels - 1, rows, block)
    field = jax.ShapeDtypeStruct(rhs.shape, jnp.float32)
    return pl.pallas_call(
        factor_solve_kernel,
        grid=(cols // block,),
        in_specs=[full, full, full, vspec, full,
                  pl.BlockSpec((None, levels, rows, 1), lambda j: (j, 0, 0, 0)),
                  pl.BlockSpec((levels, 1, block), lambda j: (0, 0, j))],
        out_specs=[full, full, full, tile_spec()],
        out_shape=[field, field, field, tile_shape()],
    )(helm_diag, east_coef, north_coef, vert_coef, rhs, east_left, north_south)


def solve_kernel(slots, *refs):
    count = len(slots)
    val_ref, inv_ref, ratio_ref, v_ref = refs[:4]
    partner_refs = refs[4:4 + count]
    p_ref, part_ref = refs[4 + count:]
    levels = val_ref.shape[0]
    zero = jnp.zeros(val_ref.shape[1:], jnp.float32)

    @pl.when(pl.program_id(0) == 0)
    def _():
        part_ref[...] = jnp.zeros_like(part_ref)

    def forward(k, elim):
        elim = val_ref[k] + ratio_ref[k] * elim
        p_ref[k] = elim
        return elim

    lax.fori_loop(0, levels, forward, zero, unroll=4)

    def backward(k, up, succ, accs):
        value = inv_ref[k] * (p_ref[k] + up * succ)
        p_ref[k] = value
        return value, tuple(acc + ref[k] * value for acc, ref in zip(accs, partner_refs))

    carry = backward(levels - 1, zero, zero, (zero,) * count)
    carry = lax.fori_loop(
        0, levels - 1, lambda i, c: backward(levels - 2 - i, v_ref[levels - 2 - i], *c), carry,
        unroll=4,
    )
    add_totals(part_ref, slots, carry[1])


def solve(values, inverse_pivot, ratio_values, vert_coef, partners, slots):
    levels, rows, cols = values.shape
    block = BLOCK_COLS if cols % BLOCK_COLS == 0 else cols
    full = column_spec(levels, rows, block)
    vspec = column_spec(levels - 1, rows, block)
    return pl.pallas_call(
        lambda *refs: solve_kernel(slots, *refs),
        grid=(cols // block,),
        in_specs=[full, full, full, vspec] + [full] * len(partners),
        out_specs=[full, tile_spec()],
        out_shape=[jax.ShapeDtypeStruct(values.shape, jnp.float32), tile_shape()],
    )(values, inverse_pivot, ratio_values, vert_coef, *partners)


def vertical_parts(vert_coef):
    zero_level = jnp.zeros((1,) + vert_coef.shape[1:], vert_coef.dtype)
    upper = jnp.concatenate([vert_coef, zero_level], axis=0)
    lower = jnp.concatenate([zero_level, vert_coef], axis=0)
    return (upper, lower)


def edge_tables(edge_num, row_start, rows, weight_index, edge_map, mortar_weights):
    maps = lax.dynamic_slice_in_dim(edge_map[edge_num], row_start, rows, 0)
    picks = lax.dynamic_slice_in_dim(weight_index[edge_num], row_start, rows, 0)
    return (maps[:, 0], maps[:, 1], mortar_weights[picks, 0], mortar_weights[picks, 1])


def belt_cols(field):
    count = lax.axis_size("belt")
    first = jnp.transpose(field[:, :, 0])
    last = jnp.transpose(field[:, :, -1])
    west = lax.ppermute(last, "belt", [(i, (i + 1) % count) for i in range(count)])
    east = lax.ppermute(first, "belt", [((i + 1) % count, i) for i in range(count)])
    return west, east


def mer_rows(field):
    count = lax.axis_size("mer")
    south = lax.ppermute(field[:, -1:, :], "mer", [(i, i + 1) for i in range(count - 1)])
    north = lax.ppermute(field[:, :1, :], "mer", [(i + 1, i) for i in range(count - 1)])
    return south, north


def gather_rows(column):
    count = lax.axis_size("mer")
    if count & (count - 1):
        return lax.all_gather(column, "mer", axis=0, tiled=True)
    me = lax.axis_index("mer")
    bit = 1
    while bit < count:
        other = lax.ppermute(column, "mer", [(i, i ^ bit) for i in range(count)])
        low_half = (me & bit) == 0
        column = jnp.concatenate(
            [jnp.where(low_half, column, other), jnp.where(low_half, other, column)], axis=0
        )
        bit *= 2
    return column


def as_lane_column(cols):
    return jnp.transpose(cols)[:, :, None]


def operator_kernel(slots, *refs):
    extra = len(slots) - 1
    (v_ref, vab_ref, vbe_ref, h_ref, e_ref, n_ref, up_ref, lo_ref, ew_ref, ns_ref,
     ve_ref, vw_ref, vn_ref, vs_ref) = refs[:14]
    partner_refs = (v_ref,) + refs[14:14 + extra]
    img_ref, part_ref = refs[14 + extra:]
    block, rows, cols = v_ref.shape
    i = pl.program_id(0)
    last_block = pl.num_programs(0) - 1
    lane = lax.broadcasted_iota(jnp.int32, (rows, cols), 1)
    row = lax.broadcasted_iota(jnp.int32, (rows, cols), 0)
    first_lane, last_lane = lane == 0, lane == cols - 1
    first_row, last_row = row == 0, row == rows - 1
    zero = jnp.zeros((rows, cols), jnp.float32)
    above = jnp.where(i == last_block, zero, vab_ref[0])
    below = jnp.where(i == 0, zero, vbe_ref[0])

    @pl.when(i == 0)
    def _():
        part_ref[...] = jnp.zeros_like(part_ref)

    def level(k, accs):
        v = v_ref[k]
        up_side = jnp.where(k == block - 1, above, v_ref[jnp.minimum(k + 1, block - 1)])
        down_side = jnp.where(k == 0, below, v_ref[jnp.maximum(k - 1, 0)])
        east_side = jnp.where(last_lane, jnp.broadcast_to(ve_ref[k], (rows, cols)),
                              pltpu.roll(v, cols - 1, 1))
        west_side = jnp.where(first_lane, jnp.broadcast_to(vw_ref[k], (rows, cols)),
                              pltpu.roll(v, 1, 1))
        north_side = jnp.where(last_row, jnp.broadcast_to(vn_ref[k], (rows, cols)),
                               pltpu.roll(v, rows - 1, 0))
        south_side = jnp.where(first_row, jnp.broadcast_to(vs_ref[k], (rows, cols)),
                               pltpu.roll(v, 1, 0))
        east = e_ref[k]
        north = n_ref[k]
        west = jnp.where(first_lane, jnp.broadcast_to(ew_ref[k], (rows, cols)),
                         pltpu.roll(east, 1, 1))
        south = jnp.where(first_row, jnp.broadcast_to(ns_ref[k], (rows, cols)),
                          pltpu.roll(north, 1, 0))
        image = (
            h_ref[k] * v
            + east * (v - east_side)
            + west * (v - west_side)
            + north * (v - north_side)
            + south * (v - south_side)
            + up_ref[k] * (v - up_side)
            + lo_ref[k] * (v - down_side)
        )
        img_ref[k] = image
        return tuple(acc + ref[k] * image for acc, ref in zip(accs, partner_refs))

    accs = lax.fori_loop(0, block, level, (zero,) * len(slots))
    add_totals(part_ref, slots, accs)


def apply_operator(direction, coefs, halos, slots, extra=()):
    helm_diag, east_coef, north_coef, upper, lower, east_west, north_south = coefs
    east_halo, west_halo, north_halo, south_halo = halos
    levels, rows, cols = direction.shape
    block = LEVEL_BLOCK if levels % LEVEL_BLOCK == 0 else levels
    blocks = levels // block
    full = pl.BlockSpec((block, rows, cols), lambda i: (i, 0, 0))
    lane_col = pl.BlockSpec((block, rows, 1), lambda i: (i, 0, 0))
    first_col = pl.BlockSpec((None, block, rows, 1), lambda i: (0, i, 0, 0))
    row_spec = pl.BlockSpec((block, 1, cols), lambda i: (i, 0, 0))
    above = pl.BlockSpec((1, rows, cols), lambda i: (jnp.minimum((i + 1) * block, levels - 1), 0, 0))
    below = pl.BlockSpec((1, rows, cols), lambda i: (jnp.maximum(i * block - 1, 0), 0, 0))
    kernel = lambda *refs: operator_kernel(slots, *refs)
    image, part = pl.pallas_call(
        kernel,
        grid=(blocks,),
        in_specs=[full, above, below, full, full, full, full, full, first_col, row_spec,
                  lane_col, lane_col, row_spec, row_spec] + [full] * len(extra),
        out_specs=[full, tile_spec()],
        out_shape=[jax.ShapeDtypeStruct(direction.shape, jnp.float32), tile_shape()],
    )(direction, direction, direction, helm_diag, east_coef, north_coef, upper, lower,
      east_west, north_south, east_halo, west_halo, north_halo, south_halo, *extra)
    return image, part


def finish_kernel(sums_ref, p0_ref, q_ref, r0_ref, a0_ref, aq_ref, sol_ref, res_ref):
    block, rows, cols = p0_ref.shape
    sums = sums_ref[...]
    norm0, curv0, r0q, a0q, qaq, p0aq = (
        jnp.broadcast_to(sums[j:j + 1, :], sums.shape) for j in range(6)
    )
    step0 = norm0 / curv0
    norm1 = norm0 - step0 * (r0q + curv0) + step0 * step0 * a0q
    p1ap1 = curv0 - step0 * (p0aq + a0q) + step0 * step0 * qaq
    p1a0 = curv0 - step0 * a0q
    d0ap1 = curv0 - step0 * p0aq
    beta = norm1 / norm0
    curv1 = p1ap1 + beta * (p1a0 + d0ap1) + beta * beta * curv0
    step1 = norm1 / curv1
    widen = lambda x: jnp.concatenate([x[:rows]] * (cols // x.shape[1]), axis=1)
    step0, beta, step1 = widen(step0), widen(beta), widen(step1)

    def level(k, carry):
        p0 = p0_ref[k]
        a0 = a0_ref[k]
        precond1 = p0 - step0 * q_ref[k]
        direction1 = precond1 + beta * p0
        image1 = (a0 - step0 * aq_ref[k]) + beta * a0
        sol_ref[k] = step0 * p0 + step1 * direction1
        res_ref[k] = (r0_ref[k] - step0 * a0) - step1 * image1
        return carry

    lax.fori_loop(0, block, level, 0)


def finish(sums, precond0, basis, right_side, image0, image_q):
    levels, rows, cols = precond0.shape
    block = LEVEL_BLOCK if levels % LEVEL_BLOCK == 0 else levels
    full = pl.BlockSpec((block, rows, cols), lambda i: (i, 0, 0))
    field = jax.ShapeDtypeStruct(precond0.shape, jnp.float32)
    return pl.pallas_call(
        finish_kernel,
        grid=(levels // block,),
        in_specs=[tile_spec(), full, full, full, full, full],
        out_specs=[full, full],
        out_shape=[field, field],
    )(sums, precond0, basis, right_side, image0, image_q)


def exchange(direction, tables, use_mortar):
    west, east = belt_cols(direction)
    first_map, second_map, first_weight, second_weight = tables
    whole = gather_rows(east)
    arrived = first_weight[:, None] * whole[first_map] + second_weight[:, None] * whole[second_map]
    east = jnp.where(use_mortar, arrived, east)
    south, north = mer_rows(direction)
    return as_lane_column(east), as_lane_column(west), north, south


def on_device(
    right_side,
    helm_diag,
    east_coef,
    north_coef,
    vert_coef,
    mortar_weights,
    weight_index,
    edge_map,
    refined,
):
    belt_index = lax.axis_index("belt")
    mer_index = lax.axis_index("mer")
    per_panel = lax.axis_size("belt") // 4
    rows = right_side.shape[1]
    row_start = mer_index * rows
    own_edge = belt_index // per_panel
    row_flags = lax.dynamic_slice_in_dim(refined[own_edge], row_start, rows, 0)
    at_edge = (belt_index + 1) % per_panel == 0
    use_mortar = jnp.logical_and(at_edge, row_flags == 1)[:, None]
    tables = edge_tables(own_edge, row_start, rows, weight_index, edge_map, mortar_weights)
    levels, _, cols = right_side.shape
    block = BLOCK_COLS if cols % BLOCK_COLS == 0 else cols
    coef_west, _ = belt_cols(east_coef)
    coef_south, _ = mer_rows(north_coef)
    east_left = jnp.stack(
        [jnp.transpose(coef_west)]
        + [east_coef[:, :, j * block - 1] for j in range(1, cols // block)],
        axis=0,
    )[..., None]
    upper, lower = vertical_parts(vert_coef)
    coefs = (helm_diag, east_coef, north_coef, upper, lower, east_left, coef_south)

    inverse_pivot, ratio_values, precond0, part0 = factor_solve(
        helm_diag, east_coef, north_coef, vert_coef, right_side, east_left, coef_south
    )
    image0, curv_part0 = apply_operator(
        precond0, coefs, exchange(precond0, tables, use_mortar), (1,)
    )
    basis, basis_part = solve(image0, inverse_pivot, ratio_values, vert_coef,
                              (right_side, image0), (2, 3))
    image_q, image_q_part = apply_operator(
        basis, coefs, exchange(basis, tables, use_mortar), (4, 5), (precond0,)
    )
    sums = tree_sum(part0 + curv_part0 + basis_part + image_q_part)
    return finish(sums, precond0, basis, right_side, image0, image_q)


def solution(mesh):
    placed = (
        P(None, "mer", "belt"),
        P(None, "mer", "belt"),
        P(None, "mer", "belt"),
        P(None, "mer", "belt"),
        P(None, "mer", "belt"),
        P(),
        P(),
        P(),
        P(),
    )
    return jax.shard_map(
        on_device,
        mesh=mesh,
        in_specs=placed,
        out_specs=(P(None, "mer", "belt"), P(None, "mer", "belt")),
        check_vma=False,
    )
```

```python
import jax
import jax.numpy as jnp
from jax import lax
from jax.experimental import pallas as pl
from jax.experimental.pallas import tpu as pltpu
from jax.sharding import PartitionSpec as P

ITERS = 2
BLOCK_COLS = 384
LEVEL_BLOCK = 24


def tree_sum(values):
    for axis in ("mer", "belt"):
        count = lax.axis_size(axis)
        if count & (count - 1):
            values = lax.psum(values, axis)
            continue
        bit = 1
        while bit < count:
            values = values + lax.ppermute(values, axis, [(i, i ^ bit) for i in range(count)])
            bit *= 2
    return values


def add_totals(part_ref, slots, accs):
    row = lax.broadcasted_iota(jnp.int32, part_ref.shape, 0)
    tile = part_ref[...]
    for slot, acc in zip(slots, accs):
        tile = tile + jnp.where(row == slot, jnp.sum(acc), 0.0)
    part_ref[...] = tile


def tile_spec():
    return pl.BlockSpec((8, 128), lambda j: (0, 0))


def tile_shape():
    return jax.ShapeDtypeStruct((8, 128), jnp.float32)


def row_block(levels, block):
    return pl.BlockSpec((levels, 1, block), lambda j: (0, 0, j))


def row_shape(levels, cols):
    return jax.ShapeDtypeStruct((levels, 1, cols), jnp.float32)


def column_spec(levels, rows, cols):
    return pl.BlockSpec((levels, rows, cols), lambda j: (0, 0, j))


def factor_solve_kernel(h_ref, e_ref, n_ref, v_ref, r_ref, eleft_ref, nsouth_ref,
                        inv_ref, ratio_ref, p_ref, top_ref, bottom_ref, part_ref):
    levels, rows, cols = h_ref.shape

    @pl.when(pl.program_id(0) == 0)
    def _():
        part_ref[...] = jnp.zeros_like(part_ref)

    zero = jnp.zeros((rows, cols), jnp.float32)
    first_lane = lax.broadcasted_iota(jnp.int32, (rows, cols), 1) == 0
    first_row = lax.broadcasted_iota(jnp.int32, (rows, cols), 0) == 0

    def forward(k, up, down, prev, elim):
        east = e_ref[k]
        north = n_ref[k]
        west = jnp.where(first_lane, jnp.broadcast_to(eleft_ref[k], (rows, cols)),
                         pltpu.roll(east, 1, 1))
        south = jnp.where(first_row, jnp.broadcast_to(nsouth_ref[k], (rows, cols)),
                          pltpu.roll(north, 1, 0))
        diag = h_ref[k] + east + west + north + south + up + down
        ratio = down / prev
        pivot = diag - down * ratio
        inv_ref[k] = 1.0 / pivot
        ratio_ref[k] = ratio
        elim = r_ref[k] + ratio * elim
        p_ref[k] = elim
        return pivot, elim

    carry = forward(0, v_ref[0], zero, jnp.ones_like(zero), zero)
    carry = lax.fori_loop(
        1, levels - 1, lambda k, c: forward(k, v_ref[k], v_ref[k - 1], *c), carry, unroll=4
    )
    forward(levels - 1, zero, v_ref[levels - 2], *carry)

    def backward(k, up, succ, acc):
        value = inv_ref[k] * (p_ref[k] + up * succ)
        p_ref[k] = value
        top_ref[k] = value[rows - 1:rows]
        bottom_ref[k] = value[:1]
        return value, acc + r_ref[k] * value

    carry = backward(levels - 1, zero, zero, zero)
    carry = lax.fori_loop(
        0, levels - 1, lambda i, c: backward(levels - 2 - i, v_ref[levels - 2 - i], *c), carry,
        unroll=4,
    )
    add_totals(part_ref, (0,), (carry[1],))


def factor_solve(helm_diag, east_coef, north_coef, vert_coef, rhs, east_left, north_south):
    levels, rows, cols = rhs.shape
    block = BLOCK_COLS if cols % BLOCK_COLS == 0 else cols
    full = column_spec(levels, rows, block)
    vspec = column_spec(levels - 1, rows, block)
    field = jax.ShapeDtypeStruct(rhs.shape, jnp.float32)
    return pl.pallas_call(
        factor_solve_kernel,
        grid=(cols // block,),
        in_specs=[full, full, full, vspec, full,
                  pl.BlockSpec((None, levels, rows, 1), lambda j: (j, 0, 0, 0)),
                  pl.BlockSpec((levels, 1, block), lambda j: (0, 0, j))],
        out_specs=[full, full, full, row_block(levels, block), row_block(levels, block),
                   tile_spec()],
        out_shape=[field, field, field, row_shape(levels, cols), row_shape(levels, cols),
                   tile_shape()],
    )(helm_diag, east_coef, north_coef, vert_coef, rhs, east_left, north_south)


def solve_kernel(slots, *refs):
    count = len(slots)
    val_ref, inv_ref, ratio_ref, v_ref = refs[:4]
    partner_refs = refs[4:4 + count - 1] + (val_ref,)
    p_ref, top_ref, bottom_ref, part_ref = refs[4 + count - 1:]
    levels = val_ref.shape[0]
    zero = jnp.zeros(val_ref.shape[1:], jnp.float32)

    @pl.when(pl.program_id(0) == 0)
    def _():
        part_ref[...] = jnp.zeros_like(part_ref)

    def forward(k, elim):
        elim = val_ref[k] + ratio_ref[k] * elim
        p_ref[k] = elim
        return elim

    lax.fori_loop(0, levels, forward, zero, unroll=4)

    def backward(k, up, succ, accs):
        value = inv_ref[k] * (p_ref[k] + up * succ)
        p_ref[k] = value
        top_ref[k] = value[value.shape[0] - 1:]
        bottom_ref[k] = value[:1]
        return value, tuple(acc + ref[k] * value for acc, ref in zip(accs, partner_refs))

    carry = backward(levels - 1, zero, zero, (zero,) * count)
    carry = lax.fori_loop(
        0, levels - 1, lambda i, c: backward(levels - 2 - i, v_ref[levels - 2 - i], *c), carry,
        unroll=4,
    )
    add_totals(part_ref, slots, carry[1])


def solve(values, inverse_pivot, ratio_values, vert_coef, partners, slots):
    levels, rows, cols = values.shape
    block = BLOCK_COLS if cols % BLOCK_COLS == 0 else cols
    full = column_spec(levels, rows, block)
    vspec = column_spec(levels - 1, rows, block)
    return pl.pallas_call(
        lambda *refs: solve_kernel(slots, *refs),
        grid=(cols // block,),
        in_specs=[full, full, full, vspec] + [full] * len(partners),
        out_specs=[full, row_block(levels, block), row_block(levels, block), tile_spec()],
        out_shape=[jax.ShapeDtypeStruct(values.shape, jnp.float32), row_shape(levels, cols),
                   row_shape(levels, cols), tile_shape()],
    )(values, inverse_pivot, ratio_values, vert_coef, *partners)


def edge_tables(edge_num, row_start, rows, weight_index, edge_map, mortar_weights):
    maps = lax.dynamic_slice_in_dim(edge_map[edge_num], row_start, rows, 0)
    picks = lax.dynamic_slice_in_dim(weight_index[edge_num], row_start, rows, 0)
    return (maps[:, 0], maps[:, 1], mortar_weights[picks, 0], mortar_weights[picks, 1])


def belt_cols(field):
    count = lax.axis_size("belt")
    first = jnp.transpose(field[:, :, 0])
    last = jnp.transpose(field[:, :, -1])
    west = lax.ppermute(last, "belt", [(i, (i + 1) % count) for i in range(count)])
    east = lax.ppermute(first, "belt", [((i + 1) % count, i) for i in range(count)])
    return west, east


def mer_rows(top, bottom):
    count = lax.axis_size("mer")
    south = lax.ppermute(top, "mer", [(i, i + 1) for i in range(count - 1)])
    north = lax.ppermute(bottom, "mer", [(i + 1, i) for i in range(count - 1)])
    return south, north


def gather_rows(column):
    count = lax.axis_size("mer")
    if count & (count - 1):
        return lax.all_gather(column, "mer", axis=0, tiled=True)
    me = lax.axis_index("mer")
    bit = 1
    while bit < count:
        other = lax.ppermute(column, "mer", [(i, i ^ bit) for i in range(count)])
        low_half = (me & bit) == 0
        column = jnp.concatenate(
            [jnp.where(low_half, column, other), jnp.where(low_half, other, column)], axis=0
        )
        bit *= 2
    return column


def as_lane_column(cols):
    return jnp.transpose(cols)[:, :, None]


def operator_kernel(slots, *refs):
    extra = len(slots) - 1
    (v_ref, vab_ref, vbe_ref, h_ref, e_ref, n_ref, up_ref, upb_ref, ew_ref, ns_ref,
     ve_ref, vw_ref, vn_ref, vs_ref) = refs[:14]
    partner_refs = (v_ref,) + refs[14:14 + extra]
    img_ref, part_ref = refs[14 + extra:]
    block, rows, cols = v_ref.shape
    i = pl.program_id(0)
    last_block = pl.num_programs(0) - 1
    lane = lax.broadcasted_iota(jnp.int32, (rows, cols), 1)
    row = lax.broadcasted_iota(jnp.int32, (rows, cols), 0)
    first_lane, last_lane = lane == 0, lane == cols - 1
    first_row, last_row = row == 0, row == rows - 1
    zero = jnp.zeros((rows, cols), jnp.float32)
    above = jnp.where(i == last_block, zero, vab_ref[0])
    below = jnp.where(i == 0, zero, vbe_ref[0])
    up_below = jnp.where(i == 0, zero, upb_ref[0])

    @pl.when(i == 0)
    def _():
        part_ref[...] = jnp.zeros_like(part_ref)

    def level(k, accs):
        v = v_ref[k]
        up_side = jnp.where(k == block - 1, above, v_ref[jnp.minimum(k + 1, block - 1)])
        down_side = jnp.where(k == 0, below, v_ref[jnp.maximum(k - 1, 0)])
        lower = jnp.where(k == 0, up_below, up_ref[jnp.maximum(k - 1, 0)])
        east_side = jnp.where(last_lane, jnp.broadcast_to(ve_ref[k], (rows, cols)),
                              pltpu.roll(v, cols - 1, 1))
        west_side = jnp.where(first_lane, jnp.broadcast_to(vw_ref[k], (rows, cols)),
                              pltpu.roll(v, 1, 1))
        north_side = jnp.where(last_row, jnp.broadcast_to(vn_ref[k], (rows, cols)),
                               pltpu.roll(v, rows - 1, 0))
        south_side = jnp.where(first_row, jnp.broadcast_to(vs_ref[k], (rows, cols)),
                               pltpu.roll(v, 1, 0))
        east = e_ref[k]
        north = n_ref[k]
        west = jnp.where(first_lane, jnp.broadcast_to(ew_ref[k], (rows, cols)),
                         pltpu.roll(east, 1, 1))
        south = jnp.where(first_row, jnp.broadcast_to(ns_ref[k], (rows, cols)),
                          pltpu.roll(north, 1, 0))
        image = (
            h_ref[k] * v
            + east * (v - east_side)
            + west * (v - west_side)
            + north * (v - north_side)
            + south * (v - south_side)
            + up_ref[k] * (v - up_side)
            + lower * (v - down_side)
        )
        img_ref[k] = image
        return tuple(acc + ref[k] * image for acc, ref in zip(accs, partner_refs))

    accs = lax.fori_loop(0, block, level, (zero,) * len(slots))
    add_totals(part_ref, slots, accs)


def apply_operator(direction, coefs, halos, slots, extra=()):
    helm_diag, east_coef, north_coef, upper, east_west, north_south = coefs
    east_halo, west_halo, north_halo, south_halo = halos
    levels, rows, cols = direction.shape
    block = LEVEL_BLOCK if levels % LEVEL_BLOCK == 0 else levels
    blocks = levels // block
    full = pl.BlockSpec((block, rows, cols), lambda i: (i, 0, 0))
    lane_col = pl.BlockSpec((block, rows, 1), lambda i: (i, 0, 0))
    first_col = pl.BlockSpec((None, block, rows, 1), lambda i: (0, i, 0, 0))
    row_spec = pl.BlockSpec((block, 1, cols), lambda i: (i, 0, 0))
    above = pl.BlockSpec((1, rows, cols), lambda i: (jnp.minimum((i + 1) * block, levels - 1), 0, 0))
    below = pl.BlockSpec((1, rows, cols), lambda i: (jnp.maximum(i * block - 1, 0), 0, 0))
    kernel = lambda *refs: operator_kernel(slots, *refs)
    image, part = pl.pallas_call(
        kernel,
        grid=(blocks,),
        in_specs=[full, above, below, full, full, full, full, below, first_col, row_spec,
                  lane_col, lane_col, row_spec, row_spec] + [full] * len(extra),
        out_specs=[full, tile_spec()],
        out_shape=[jax.ShapeDtypeStruct(direction.shape, jnp.float32), tile_shape()],
    )(direction, direction, direction, helm_diag, east_coef, north_coef, upper, upper,
      east_west, north_south, east_halo, west_halo, north_halo, south_halo, *extra)
    return image, part


def finish_kernel(sums_ref, p0_ref, q_ref, r0_ref, a0_ref, aq_ref, sol_ref, res_ref):
    block, rows, cols = p0_ref.shape
    sums = sums_ref[...]
    norm0, curv0, r0q, a0q, qaq, p0aq = (
        jnp.broadcast_to(sums[j:j + 1, :], sums.shape) for j in range(6)
    )
    step0 = norm0 / curv0
    norm1 = norm0 - step0 * (r0q + curv0) + step0 * step0 * a0q
    p1ap1 = curv0 - step0 * (p0aq + a0q) + step0 * step0 * qaq
    p1a0 = curv0 - step0 * a0q
    d0ap1 = curv0 - step0 * p0aq
    beta = norm1 / norm0
    curv1 = p1ap1 + beta * (p1a0 + d0ap1) + beta * beta * curv0
    step1 = norm1 / curv1
    widen = lambda x: jnp.concatenate([x[:rows]] * (cols // x.shape[1]), axis=1)
    step0, beta, step1 = widen(step0), widen(beta), widen(step1)

    def level(k, carry):
        p0 = p0_ref[k]
        a0 = a0_ref[k]
        precond1 = p0 - step0 * q_ref[k]
        direction1 = precond1 + beta * p0
        image1 = (a0 - step0 * aq_ref[k]) + beta * a0
        sol_ref[k] = step0 * p0 + step1 * direction1
        res_ref[k] = (r0_ref[k] - step0 * a0) - step1 * image1
        return carry

    lax.fori_loop(0, block, level, 0)


def finish(sums, precond0, basis, right_side, image0, image_q):
    levels, rows, cols = precond0.shape
    block = LEVEL_BLOCK if levels % LEVEL_BLOCK == 0 else levels
    full = pl.BlockSpec((block, rows, cols), lambda i: (i, 0, 0))
    field = jax.ShapeDtypeStruct(precond0.shape, jnp.float32)
    return pl.pallas_call(
        finish_kernel,
        grid=(levels // block,),
        in_specs=[tile_spec(), full, full, full, full, full],
        out_specs=[full, full],
        out_shape=[field, field],
    )(sums, precond0, basis, right_side, image0, image_q)


def exchange(direction, top, bottom, tables, use_mortar):
    west, east = belt_cols(direction)
    first_map, second_map, first_weight, second_weight = tables
    whole = gather_rows(east)
    arrived = first_weight[:, None] * whole[first_map] + second_weight[:, None] * whole[second_map]
    east = jnp.where(use_mortar, arrived, east)
    south, north = mer_rows(top, bottom)
    return as_lane_column(east), as_lane_column(west), north, south


def on_device(
    right_side,
    helm_diag,
    east_coef,
    north_coef,
    vert_coef,
    mortar_weights,
    weight_index,
    edge_map,
    refined,
):
    belt_index = lax.axis_index("belt")
    mer_index = lax.axis_index("mer")
    per_panel = lax.axis_size("belt") // 4
    rows = right_side.shape[1]
    row_start = mer_index * rows
    own_edge = belt_index // per_panel
    row_flags = lax.dynamic_slice_in_dim(refined[own_edge], row_start, rows, 0)
    at_edge = (belt_index + 1) % per_panel == 0
    use_mortar = jnp.logical_and(at_edge, row_flags == 1)[:, None]
    tables = edge_tables(own_edge, row_start, rows, weight_index, edge_map, mortar_weights)
    levels, _, cols = right_side.shape
    block = BLOCK_COLS if cols % BLOCK_COLS == 0 else cols
    coef_west, _ = belt_cols(east_coef)
    coef_south, _ = mer_rows(north_coef[:, -1:, :], north_coef[:, :1, :])
    east_left = jnp.stack(
        [jnp.transpose(coef_west)]
        + [east_coef[:, :, j * block - 1] for j in range(1, cols // block)],
        axis=0,
    )[..., None]
    upper = jnp.concatenate([vert_coef, jnp.zeros_like(vert_coef[:1])], axis=0)
    coefs = (helm_diag, east_coef, north_coef, upper, east_left, coef_south)

    inverse_pivot, ratio_values, precond0, top0, bottom0, part0 = factor_solve(
        helm_diag, east_coef, north_coef, vert_coef, right_side, east_left, coef_south
    )
    image0, curv_part0 = apply_operator(
        precond0, coefs, exchange(precond0, top0, bottom0, tables, use_mortar), (1,)
    )
    basis, top_q, bottom_q, basis_part = solve(
        image0, inverse_pivot, ratio_values, vert_coef, (right_side,), (2, 3)
    )
    image_q, image_q_part = apply_operator(
        basis, coefs, exchange(basis, top_q, bottom_q, tables, use_mortar), (4, 5), (precond0,)
    )
    sums = tree_sum(part0 + curv_part0 + basis_part + image_q_part)
    return finish(sums, precond0, basis, right_side, image0, image_q)


def solution(mesh):
    placed = (
        P(None, "mer", "belt"),
        P(None, "mer", "belt"),
        P(None, "mer", "belt"),
        P(None, "mer", "belt"),
        P(None, "mer", "belt"),
        P(),
        P(),
        P(),
        P(),
    )
    return jax.shard_map(
        on_device,
        mesh=mesh,
        in_specs=placed,
        out_specs=(P(None, "mer", "belt"), P(None, "mer", "belt")),
        check_vma=False,
    )
```

```python
import jax
import jax.numpy as jnp
from jax import lax
from jax.experimental import pallas as pl
from jax.experimental.pallas import tpu as pltpu
from jax.sharding import PartitionSpec as P

ITERS = 2
BLOCK_COLS = 384
LEVEL_BLOCK = 24


def tree_sum(values):
    for axis in ("mer", "belt"):
        count = lax.axis_size(axis)
        if count & (count - 1):
            values = lax.psum(values, axis)
            continue
        bit = 1
        while bit < count:
            values = values + lax.ppermute(values, axis, [(i, i ^ bit) for i in range(count)])
            bit *= 2
    return values


def add_totals(part_ref, slots, accs):
    row = lax.broadcasted_iota(jnp.int32, part_ref.shape, 0)
    tile = part_ref[...]
    for slot, acc in zip(slots, accs):
        tile = tile + jnp.where(row == slot, jnp.sum(acc), 0.0)
    part_ref[...] = tile


def tile_spec():
    return pl.BlockSpec((8, 128), lambda j: (0, 0))


def tile_shape():
    return jax.ShapeDtypeStruct((8, 128), jnp.float32)


def row_block(levels, block):
    return pl.BlockSpec((levels, 1, block), lambda j: (0, 0, j))


def row_shape(levels, cols):
    return jax.ShapeDtypeStruct((levels, 1, cols), jnp.float32)


def column_spec(levels, rows, cols):
    return pl.BlockSpec((levels, rows, cols), lambda j: (0, 0, j))


def factor_solve_kernel(h_ref, e_ref, n_ref, v_ref, r_ref, eleft_ref, nsouth_ref,
                        inv_ref, ratio_ref, p_ref, top_ref, bottom_ref, part_ref):
    levels, rows, cols = h_ref.shape

    @pl.when(pl.program_id(0) == 0)
    def _():
        part_ref[...] = jnp.zeros_like(part_ref)

    zero = jnp.zeros((rows, cols), jnp.float32)
    first_lane = lax.broadcasted_iota(jnp.int32, (rows, cols), 1) == 0
    first_row = lax.broadcasted_iota(jnp.int32, (rows, cols), 0) == 0

    def forward(k, up, down, prev, elim):
        east = e_ref[k]
        north = n_ref[k]
        west = jnp.where(first_lane, jnp.broadcast_to(eleft_ref[k], (rows, cols)),
                         pltpu.roll(east, 1, 1))
        south = jnp.where(first_row, jnp.broadcast_to(nsouth_ref[k], (rows, cols)),
                          pltpu.roll(north, 1, 0))
        diag = h_ref[k] + east + west + north + south + up + down
        ratio = down / prev
        pivot = diag - down * ratio
        inv_ref[k] = 1.0 / pivot
        ratio_ref[k] = ratio
        elim = r_ref[k] + ratio * elim
        p_ref[k] = elim
        return pivot, elim

    carry = forward(0, v_ref[0], zero, jnp.ones_like(zero), zero)
    carry = lax.fori_loop(
        1, levels - 1, lambda k, c: forward(k, v_ref[k], v_ref[k - 1], *c), carry, unroll=4
    )
    forward(levels - 1, zero, v_ref[levels - 2], *carry)

    def backward(k, up, succ, acc):
        value = inv_ref[k] * (p_ref[k] + up * succ)
        p_ref[k] = value
        top_ref[k] = value[rows - 1:rows]
        bottom_ref[k] = value[:1]
        return value, acc + r_ref[k] * value

    carry = backward(levels - 1, zero, zero, zero)
    carry = lax.fori_loop(
        0, levels - 1, lambda i, c: backward(levels - 2 - i, v_ref[levels - 2 - i], *c), carry,
        unroll=4,
    )
    add_totals(part_ref, (0,), (carry[1],))


def factor_solve(helm_diag, east_coef, north_coef, vert_coef, rhs, east_left, north_south):
    levels, rows, cols = rhs.shape
    block = BLOCK_COLS if cols % BLOCK_COLS == 0 else cols
    full = column_spec(levels, rows, block)
    vspec = column_spec(levels - 1, rows, block)
    field = jax.ShapeDtypeStruct(rhs.shape, jnp.float32)
    return pl.pallas_call(
        factor_solve_kernel,
        grid=(cols // block,),
        in_specs=[full, full, full, vspec, full,
                  pl.BlockSpec((None, levels, rows, 1), lambda j: (j, 0, 0, 0)),
                  pl.BlockSpec((levels, 1, block), lambda j: (0, 0, j))],
        out_specs=[full, full, full, row_block(levels, block), row_block(levels, block),
                   tile_spec()],
        out_shape=[field, field, field, row_shape(levels, cols), row_shape(levels, cols),
                   tile_shape()],
    )(helm_diag, east_coef, north_coef, vert_coef, rhs, east_left, north_south)


def solve_kernel(slots, *refs):
    count = len(slots)
    val_ref, inv_ref, ratio_ref, v_ref = refs[:4]
    partner_refs = refs[4:4 + count - 1] + (val_ref,)
    p_ref, top_ref, bottom_ref, part_ref = refs[4 + count - 1:]
    levels = val_ref.shape[0]
    zero = jnp.zeros(val_ref.shape[1:], jnp.float32)

    @pl.when(pl.program_id(0) == 0)
    def _():
        part_ref[...] = jnp.zeros_like(part_ref)

    def forward(k, elim):
        elim = val_ref[k] + ratio_ref[k] * elim
        p_ref[k] = elim
        return elim

    lax.fori_loop(0, levels, forward, zero, unroll=4)

    def backward(k, up, succ, accs):
        value = inv_ref[k] * (p_ref[k] + up * succ)
        p_ref[k] = value
        top_ref[k] = value[value.shape[0] - 1:]
        bottom_ref[k] = value[:1]
        return value, tuple(acc + ref[k] * value for acc, ref in zip(accs, partner_refs))

    carry = backward(levels - 1, zero, zero, (zero,) * count)
    carry = lax.fori_loop(
        0, levels - 1, lambda i, c: backward(levels - 2 - i, v_ref[levels - 2 - i], *c), carry,
        unroll=4,
    )
    add_totals(part_ref, slots, carry[1])


def solve(values, inverse_pivot, ratio_values, vert_coef, partners, slots):
    levels, rows, cols = values.shape
    block = BLOCK_COLS if cols % BLOCK_COLS == 0 else cols
    full = column_spec(levels, rows, block)
    vspec = column_spec(levels - 1, rows, block)
    return pl.pallas_call(
        lambda *refs: solve_kernel(slots, *refs),
        grid=(cols // block,),
        in_specs=[full, full, full, vspec] + [full] * len(partners),
        out_specs=[full, row_block(levels, block), row_block(levels, block), tile_spec()],
        out_shape=[jax.ShapeDtypeStruct(values.shape, jnp.float32), row_shape(levels, cols),
                   row_shape(levels, cols), tile_shape()],
    )(values, inverse_pivot, ratio_values, vert_coef, *partners)


def edge_tables(edge_num, row_start, rows, weight_index, edge_map, mortar_weights):
    maps = lax.dynamic_slice_in_dim(edge_map[edge_num], row_start, rows, 0)
    picks = lax.dynamic_slice_in_dim(weight_index[edge_num], row_start, rows, 0)
    return (maps[:, 0], maps[:, 1], mortar_weights[picks, 0], mortar_weights[picks, 1])


def belt_cols(field):
    count = lax.axis_size("belt")
    first = jnp.transpose(field[:, :, 0])
    last = jnp.transpose(field[:, :, -1])
    west = lax.ppermute(last, "belt", [(i, (i + 1) % count) for i in range(count)])
    east = lax.ppermute(first, "belt", [((i + 1) % count, i) for i in range(count)])
    return west, east


def mer_rows(top, bottom):
    count = lax.axis_size("mer")
    south = lax.ppermute(top, "mer", [(i, i + 1) for i in range(count - 1)])
    north = lax.ppermute(bottom, "mer", [(i + 1, i) for i in range(count - 1)])
    return south, north


def gather_rows(column, axis=0):
    count = lax.axis_size("mer")
    if count & (count - 1):
        return lax.all_gather(column, "mer", axis=axis, tiled=True)
    me = lax.axis_index("mer")
    bit = 1
    while bit < count:
        other = lax.ppermute(column, "mer", [(i, i ^ bit) for i in range(count)])
        low_half = (me & bit) == 0
        column = jnp.concatenate(
            [jnp.where(low_half, column, other), jnp.where(low_half, other, column)], axis=axis
        )
        bit *= 2
    return column


def as_lane_column(cols):
    return jnp.transpose(cols)[:, :, None]


def operator_kernel(slots, *refs):
    extra = len(slots) - 1
    (v_ref, vab_ref, vbe_ref, h_ref, e_ref, n_ref, up_ref, upb_ref, ew_ref, ns_ref,
     ve_ref, vw_ref, vn_ref, vs_ref) = refs[:14]
    partner_refs = (v_ref,) + refs[14:14 + extra]
    img_ref, part_ref = refs[14 + extra:]
    block, rows, cols = v_ref.shape
    i = pl.program_id(0)
    last_block = pl.num_programs(0) - 1
    lane = lax.broadcasted_iota(jnp.int32, (rows, cols), 1)
    row = lax.broadcasted_iota(jnp.int32, (rows, cols), 0)
    first_lane, last_lane = lane == 0, lane == cols - 1
    first_row, last_row = row == 0, row == rows - 1
    zero = jnp.zeros((rows, cols), jnp.float32)
    above = jnp.where(i == last_block, zero, vab_ref[0])
    below = jnp.where(i == 0, zero, vbe_ref[0])
    up_below = jnp.where(i == 0, zero, upb_ref[0])

    @pl.when(i == 0)
    def _():
        part_ref[...] = jnp.zeros_like(part_ref)

    def level(k, accs):
        v = v_ref[k]
        up_side = jnp.where(k == block - 1, above, v_ref[jnp.minimum(k + 1, block - 1)])
        down_side = jnp.where(k == 0, below, v_ref[jnp.maximum(k - 1, 0)])
        lower = jnp.where(k == 0, up_below, up_ref[jnp.maximum(k - 1, 0)])
        east_side = jnp.where(last_lane, jnp.broadcast_to(ve_ref[k], (rows, cols)),
                              pltpu.roll(v, cols - 1, 1))
        west_side = jnp.where(first_lane, jnp.broadcast_to(vw_ref[k], (rows, cols)),
                              pltpu.roll(v, 1, 1))
        north_side = jnp.where(last_row, jnp.broadcast_to(vn_ref[k], (rows, cols)),
                               pltpu.roll(v, rows - 1, 0))
        south_side = jnp.where(first_row, jnp.broadcast_to(vs_ref[k], (rows, cols)),
                               pltpu.roll(v, 1, 0))
        east = e_ref[k]
        north = n_ref[k]
        west = jnp.where(first_lane, jnp.broadcast_to(ew_ref[k], (rows, cols)),
                         pltpu.roll(east, 1, 1))
        south = jnp.where(first_row, jnp.broadcast_to(ns_ref[k], (rows, cols)),
                          pltpu.roll(north, 1, 0))
        image = (
            h_ref[k] * v
            + east * (v - east_side)
            + west * (v - west_side)
            + north * (v - north_side)
            + south * (v - south_side)
            + up_ref[k] * (v - up_side)
            + lower * (v - down_side)
        )
        img_ref[k] = image
        return tuple(acc + ref[k] * image for acc, ref in zip(accs, partner_refs))

    accs = lax.fori_loop(0, block, level, (zero,) * len(slots))
    add_totals(part_ref, slots, accs)


def apply_operator(direction, coefs, halos, slots, extra=()):
    helm_diag, east_coef, north_coef, upper, east_west, north_south = coefs
    east_halo, west_halo, north_halo, south_halo = halos
    levels, rows, cols = direction.shape
    block = LEVEL_BLOCK if levels % LEVEL_BLOCK == 0 else levels
    blocks = levels // block
    full = pl.BlockSpec((block, rows, cols), lambda i: (i, 0, 0))
    lane_col = pl.BlockSpec((block, rows, 1), lambda i: (i, 0, 0))
    first_col = pl.BlockSpec((None, block, rows, 1), lambda i: (0, i, 0, 0))
    row_spec = pl.BlockSpec((block, 1, cols), lambda i: (i, 0, 0))
    above = pl.BlockSpec((1, rows, cols), lambda i: (jnp.minimum((i + 1) * block, levels - 1), 0, 0))
    below = pl.BlockSpec((1, rows, cols), lambda i: (jnp.maximum(i * block - 1, 0), 0, 0))
    kernel = lambda *refs: operator_kernel(slots, *refs)
    image, part = pl.pallas_call(
        kernel,
        grid=(blocks,),
        in_specs=[full, above, below, full, full, full, full, below, first_col, row_spec,
                  lane_col, lane_col, row_spec, row_spec] + [full] * len(extra),
        out_specs=[full, tile_spec()],
        out_shape=[jax.ShapeDtypeStruct(direction.shape, jnp.float32), tile_shape()],
    )(direction, direction, direction, helm_diag, east_coef, north_coef, upper, upper,
      east_west, north_south, east_halo, west_halo, north_halo, south_halo, *extra)
    return image, part


def finish_kernel(sums_ref, p0_ref, q_ref, r0_ref, a0_ref, aq_ref, sol_ref, res_ref):
    block, rows, cols = p0_ref.shape
    sums = sums_ref[...]
    norm0, curv0, r0q, a0q, qaq, p0aq = (
        jnp.broadcast_to(sums[j:j + 1, :], sums.shape) for j in range(6)
    )
    step0 = norm0 / curv0
    norm1 = norm0 - step0 * (r0q + curv0) + step0 * step0 * a0q
    p1ap1 = curv0 - step0 * (p0aq + a0q) + step0 * step0 * qaq
    p1a0 = curv0 - step0 * a0q
    d0ap1 = curv0 - step0 * p0aq
    beta = norm1 / norm0
    curv1 = p1ap1 + beta * (p1a0 + d0ap1) + beta * beta * curv0
    step1 = norm1 / curv1
    widen = lambda x: jnp.concatenate([x[:rows]] * (cols // x.shape[1]), axis=1)
    step0, beta, step1 = widen(step0), widen(beta), widen(step1)

    def level(k, carry):
        p0 = p0_ref[k]
        a0 = a0_ref[k]
        precond1 = p0 - step0 * q_ref[k]
        direction1 = precond1 + beta * p0
        image1 = (a0 - step0 * aq_ref[k]) + beta * a0
        sol_ref[k] = step0 * p0 + step1 * direction1
        res_ref[k] = (r0_ref[k] - step0 * a0) - step1 * image1
        return carry

    lax.fori_loop(0, block, level, 0)


def finish(sums, precond0, basis, right_side, image0, image_q):
    levels, rows, cols = precond0.shape
    block = LEVEL_BLOCK if levels % LEVEL_BLOCK == 0 else levels
    full = pl.BlockSpec((block, rows, cols), lambda i: (i, 0, 0))
    field = jax.ShapeDtypeStruct(precond0.shape, jnp.float32)
    return pl.pallas_call(
        finish_kernel,
        grid=(levels // block,),
        in_specs=[tile_spec(), full, full, full, full, full],
        out_specs=[full, full],
        out_shape=[field, field],
    )(sums, precond0, basis, right_side, image0, image_q)


def edge_kernel(r_ref, h_ref, e_ref, n_ref, v_ref, p_ref, q_ref, inv_ref, ratio_ref, img_ref):
    levels, subl, lanes = r_ref.shape
    zero = jnp.zeros((subl, lanes), jnp.float32)

    def coef(k):
        east = e_ref[k]
        north = n_ref[k]
        return east, pltpu.roll(east, 1, 0), north, pltpu.roll(north, 1, 1)

    def factor(k, up, down, prev, elim):
        east, west, north, south = coef(k)
        diag = h_ref[k] + east + west + north + south + up + down
        ratio = down / prev
        pivot = diag - down * ratio
        inv_ref[k] = 1.0 / pivot
        ratio_ref[k] = ratio
        elim = r_ref[k] + ratio * elim
        p_ref[k] = elim
        return pivot, elim

    carry = factor(0, v_ref[0], zero, jnp.ones_like(zero), zero)
    carry = lax.fori_loop(1, levels, lambda k, c: factor(k, v_ref[k], v_ref[k - 1], *c), carry)

    def back(out_ref):
        def step(i, succ):
            k = levels - 1 - i
            up = jnp.where(k == levels - 1, zero, v_ref[k])
            value = inv_ref[k] * (out_ref[k] + up * succ)
            out_ref[k] = value
            return value
        lax.fori_loop(0, levels, step, zero)

    back(p_ref)

    def apply(k, carry):
        v = p_ref[k]
        up_side = jnp.where(k == levels - 1, zero, p_ref[jnp.minimum(k + 1, levels - 1)])
        down_side = jnp.where(k == 0, zero, p_ref[jnp.maximum(k - 1, 0)])
        lower = jnp.where(k == 0, zero, v_ref[jnp.maximum(k - 1, 0)])
        east, west, north, south = coef(k)
        img_ref[k] = (
            h_ref[k] * v
            + east * (v - pltpu.roll(v, subl - 1, 0))
            + west * (v - pltpu.roll(v, 1, 0))
            + north * (v - pltpu.roll(v, lanes - 1, 1))
            + south * (v - pltpu.roll(v, 1, 1))
            + v_ref[k] * (v - up_side)
            + lower * (v - down_side)
        )
        return carry

    lax.fori_loop(0, levels, apply, 0)

    def forward(k, elim):
        elim = img_ref[k] + ratio_ref[k] * elim
        q_ref[k] = elim
        return elim

    lax.fori_loop(0, levels, forward, zero)
    back(q_ref)


def edge_columns(fields):
    levels = fields[0].shape[0]
    tile = jax.ShapeDtypeStruct(fields[0].shape, jnp.float32)
    whole = pl.BlockSpec(memory_space=pltpu.VMEM)
    return pl.pallas_call(
        edge_kernel,
        in_specs=[whole] * 5,
        out_specs=[whole, whole],
        out_shape=[tile, tile],
        scratch_shapes=[pltpu.VMEM(fields[0].shape, jnp.float32)] * 3,
    )(*fields)


def edge_inputs(right_side, helm_diag, east_coef, north_coef, upper):
    count = lax.axis_size("belt")
    fields = (right_side, helm_diag, east_coef, north_coef, upper)
    own = [jnp.transpose(f[:, :, -1]) for f in fields] + [jnp.transpose(east_coef[:, :, -2])]
    ahead = [jnp.transpose(f[:, :, c]) for c in (0, 1) for f in fields]
    ahead = lax.ppermute(jnp.stack(ahead), "belt", [((i + 1) % count, i) for i in range(count)])
    return gather_rows(jnp.concatenate([jnp.stack(own), ahead], axis=0), 1)


def edge_tiles(columns):
    rows, levels = columns.shape[1:]
    lanes = max(128, -(-rows // 128) * 128)
    tiles = []
    for f, filler in enumerate((0.0, 1.0, 0.0, 0.0, 0.0)):
        blank = jnp.full((rows, levels), filler, jnp.float32)
        west = columns[5] if f == 2 else blank
        subl = [west, columns[f], columns[6 + f], columns[11 + f]] + [blank] * 4
        stacked = jnp.transpose(jnp.stack(subl), (2, 0, 1))
        tiles.append(jnp.pad(stacked, ((0, 0), (0, 0), (0, lanes - rows)),
                             constant_values=filler))
    return tiles


def exchange(direction, top, bottom, tables, use_mortar, whole):
    west, east = belt_cols(direction)
    first_map, second_map, first_weight, second_weight = tables
    arrived = first_weight[:, None] * whole[first_map] + second_weight[:, None] * whole[second_map]
    east = jnp.where(use_mortar, arrived, east)
    south, north = mer_rows(top, bottom)
    return as_lane_column(east), as_lane_column(west), north, south


def on_device(
    right_side,
    helm_diag,
    east_coef,
    north_coef,
    vert_coef,
    mortar_weights,
    weight_index,
    edge_map,
    refined,
):
    belt_index = lax.axis_index("belt")
    mer_index = lax.axis_index("mer")
    per_panel = lax.axis_size("belt") // 4
    rows = right_side.shape[1]
    row_start = mer_index * rows
    own_edge = belt_index // per_panel
    row_flags = lax.dynamic_slice_in_dim(refined[own_edge], row_start, rows, 0)
    at_edge = (belt_index + 1) % per_panel == 0
    use_mortar = jnp.logical_and(at_edge, row_flags == 1)[:, None]
    tables = edge_tables(own_edge, row_start, rows, weight_index, edge_map, mortar_weights)
    levels, _, cols = right_side.shape
    block = BLOCK_COLS if cols % BLOCK_COLS == 0 else cols
    coef_west, _ = belt_cols(east_coef)
    coef_south, _ = mer_rows(north_coef[:, -1:, :], north_coef[:, :1, :])
    east_left = jnp.stack(
        [jnp.transpose(coef_west)]
        + [east_coef[:, :, j * block - 1] for j in range(1, cols // block)],
        axis=0,
    )[..., None]
    upper = jnp.concatenate([vert_coef, jnp.zeros_like(vert_coef[:1])], axis=0)
    coefs = (helm_diag, east_coef, north_coef, upper, east_left, coef_south)
    edge_p, edge_q = edge_columns(
        edge_tiles(edge_inputs(right_side, helm_diag, east_coef, north_coef, upper))
    )
    nrows = rows * lax.axis_size("mer")
    edge_p0 = jnp.transpose(edge_p[:, 2, :nrows])
    edge_basis = jnp.transpose(edge_q[:, 2, :nrows])

    inverse_pivot, ratio_values, precond0, top0, bottom0, part0 = factor_solve(
        helm_diag, east_coef, north_coef, vert_coef, right_side, east_left, coef_south
    )
    image0, curv_part0 = apply_operator(
        precond0, coefs, exchange(precond0, top0, bottom0, tables, use_mortar, edge_p0), (1,)
    )
    basis, top_q, bottom_q, basis_part = solve(
        image0, inverse_pivot, ratio_values, vert_coef, (right_side,), (2, 3)
    )
    image_q, image_q_part = apply_operator(
        basis, coefs, exchange(basis, top_q, bottom_q, tables, use_mortar, edge_basis), (4, 5), (precond0,)
    )
    sums = tree_sum(part0 + curv_part0 + basis_part + image_q_part)
    return finish(sums, precond0, basis, right_side, image0, image_q)


def solution(mesh):
    placed = (
        P(None, "mer", "belt"),
        P(None, "mer", "belt"),
        P(None, "mer", "belt"),
        P(None, "mer", "belt"),
        P(None, "mer", "belt"),
        P(),
        P(),
        P(),
        P(),
    )
    return jax.shard_map(
        on_device,
        mesh=mesh,
        in_specs=placed,
        out_specs=(P(None, "mer", "belt"), P(None, "mer", "belt")),
        check_vma=False,
    )
```

```python
import jax
import jax.numpy as jnp
from jax import lax
from jax.experimental import pallas as pl
from jax.experimental.pallas import tpu as pltpu
from jax.sharding import PartitionSpec as P

ITERS = 2
BLOCK_COLS = 384
LEVEL_BLOCK = 12


def tree_sum(values):
    for axis in ("mer", "belt"):
        count = lax.axis_size(axis)
        if count & (count - 1):
            values = lax.psum(values, axis)
            continue
        bit = 1
        while bit < count:
            values = values + lax.ppermute(values, axis, [(i, i ^ bit) for i in range(count)])
            bit *= 2
    return values


def add_totals(part_ref, slots, accs):
    row = lax.broadcasted_iota(jnp.int32, part_ref.shape, 0)
    tile = part_ref[...]
    for slot, acc in zip(slots, accs):
        tile = tile + jnp.where(row == slot, jnp.sum(acc), 0.0)
    part_ref[...] = tile


def tile_spec():
    return pl.BlockSpec((8, 128), lambda j: (0, 0))


def tile_shape():
    return jax.ShapeDtypeStruct((8, 128), jnp.float32)


def row_block(levels, block):
    return pl.BlockSpec((levels, 1, block), lambda j: (0, 0, j))


def row_shape(levels, cols):
    return jax.ShapeDtypeStruct((levels, 1, cols), jnp.float32)


def column_spec(levels, rows, cols):
    return pl.BlockSpec((levels, rows, cols), lambda j: (0, 0, j))


def factor_solve_kernel(h_ref, e_ref, n_ref, v_ref, r_ref, eleft_ref, nsouth_ref,
                        inv_ref, ratio_ref, p_ref, top_ref, bottom_ref, part_ref):
    levels, rows, cols = h_ref.shape

    @pl.when(pl.program_id(0) == 0)
    def _():
        part_ref[...] = jnp.zeros_like(part_ref)

    zero = jnp.zeros((rows, cols), jnp.float32)
    first_lane = lax.broadcasted_iota(jnp.int32, (rows, cols), 1) == 0
    first_row = lax.broadcasted_iota(jnp.int32, (rows, cols), 0) == 0

    def forward(k, up, down, prev, elim):
        east = e_ref[k]
        north = n_ref[k]
        west = jnp.where(first_lane, jnp.broadcast_to(eleft_ref[k], (rows, cols)),
                         pltpu.roll(east, 1, 1))
        south = jnp.where(first_row, jnp.broadcast_to(nsouth_ref[k], (rows, cols)),
                          pltpu.roll(north, 1, 0))
        diag = h_ref[k] + east + west + north + south + up + down
        ratio = down / prev
        pivot = diag - down * ratio
        inv_ref[k] = 1.0 / pivot
        ratio_ref[k] = ratio
        elim = r_ref[k] + ratio * elim
        p_ref[k] = elim
        return pivot, elim

    carry = forward(0, v_ref[0], zero, jnp.ones_like(zero), zero)
    carry = lax.fori_loop(
        1, levels - 1, lambda k, c: forward(k, v_ref[k], v_ref[k - 1], *c), carry, unroll=4
    )
    forward(levels - 1, zero, v_ref[levels - 2], *carry)

    def backward(k, up, succ, acc):
        value = inv_ref[k] * (p_ref[k] + up * succ)
        p_ref[k] = value
        top_ref[k] = value[rows - 1:rows]
        bottom_ref[k] = value[:1]
        return value, acc + r_ref[k] * value

    carry = backward(levels - 1, zero, zero, zero)
    carry = lax.fori_loop(
        0, levels - 1, lambda i, c: backward(levels - 2 - i, v_ref[levels - 2 - i], *c), carry,
        unroll=4,
    )
    add_totals(part_ref, (0,), (carry[1],))


def factor_solve(helm_diag, east_coef, north_coef, vert_coef, rhs, east_left, north_south):
    levels, rows, cols = rhs.shape
    block = BLOCK_COLS if cols % BLOCK_COLS == 0 else cols
    full = column_spec(levels, rows, block)
    vspec = column_spec(levels - 1, rows, block)
    field = jax.ShapeDtypeStruct(rhs.shape, jnp.float32)
    return pl.pallas_call(
        factor_solve_kernel,
        grid=(cols // block,),
        in_specs=[full, full, full, vspec, full,
                  pl.BlockSpec((None, levels, rows, 1), lambda j: (j, 0, 0, 0)),
                  pl.BlockSpec((levels, 1, block), lambda j: (0, 0, j))],
        out_specs=[full, full, full, row_block(levels, block), row_block(levels, block),
                   tile_spec()],
        out_shape=[field, field, field, row_shape(levels, cols), row_shape(levels, cols),
                   tile_shape()],
    )(helm_diag, east_coef, north_coef, vert_coef, rhs, east_left, north_south)


def solve_kernel(slots, *refs):
    count = len(slots)
    val_ref, inv_ref, ratio_ref, v_ref = refs[:4]
    partner_refs = refs[4:4 + count - 1] + (val_ref,)
    p_ref, top_ref, bottom_ref, part_ref = refs[4 + count - 1:]
    levels = val_ref.shape[0]
    zero = jnp.zeros(val_ref.shape[1:], jnp.float32)

    @pl.when(pl.program_id(0) == 0)
    def _():
        part_ref[...] = jnp.zeros_like(part_ref)

    def forward(k, elim):
        elim = val_ref[k] + ratio_ref[k] * elim
        p_ref[k] = elim
        return elim

    lax.fori_loop(0, levels, forward, zero, unroll=4)

    def backward(k, up, succ, accs):
        value = inv_ref[k] * (p_ref[k] + up * succ)
        p_ref[k] = value
        top_ref[k] = value[value.shape[0] - 1:]
        bottom_ref[k] = value[:1]
        return value, tuple(acc + ref[k] * value for acc, ref in zip(accs, partner_refs))

    carry = backward(levels - 1, zero, zero, (zero,) * count)
    carry = lax.fori_loop(
        0, levels - 1, lambda i, c: backward(levels - 2 - i, v_ref[levels - 2 - i], *c), carry,
        unroll=4,
    )
    add_totals(part_ref, slots, carry[1])


def solve(values, inverse_pivot, ratio_values, vert_coef, partners, slots):
    levels, rows, cols = values.shape
    block = BLOCK_COLS if cols % BLOCK_COLS == 0 else cols
    full = column_spec(levels, rows, block)
    vspec = column_spec(levels - 1, rows, block)
    return pl.pallas_call(
        lambda *refs: solve_kernel(slots, *refs),
        grid=(cols // block,),
        in_specs=[full, full, full, vspec] + [full] * len(partners),
        out_specs=[full, row_block(levels, block), row_block(levels, block), tile_spec()],
        out_shape=[jax.ShapeDtypeStruct(values.shape, jnp.float32), row_shape(levels, cols),
                   row_shape(levels, cols), tile_shape()],
    )(values, inverse_pivot, ratio_values, vert_coef, *partners)


def edge_tables(edge_num, row_start, rows, weight_index, edge_map, mortar_weights):
    maps = lax.dynamic_slice_in_dim(edge_map[edge_num], row_start, rows, 0)
    picks = lax.dynamic_slice_in_dim(weight_index[edge_num], row_start, rows, 0)
    return (maps[:, 0], maps[:, 1], mortar_weights[picks, 0], mortar_weights[picks, 1])


def belt_cols(field):
    count = lax.axis_size("belt")
    first = jnp.transpose(field[:, :, 0])
    last = jnp.transpose(field[:, :, -1])
    west = lax.ppermute(last, "belt", [(i, (i + 1) % count) for i in range(count)])
    east = lax.ppermute(first, "belt", [((i + 1) % count, i) for i in range(count)])
    return west, east


def mer_rows(top, bottom):
    count = lax.axis_size("mer")
    south = lax.ppermute(top, "mer", [(i, i + 1) for i in range(count - 1)])
    north = lax.ppermute(bottom, "mer", [(i + 1, i) for i in range(count - 1)])
    return south, north


def gather_rows(column):
    count = lax.axis_size("mer")
    if count & (count - 1):
        return lax.all_gather(column, "mer", axis=0, tiled=True)
    me = lax.axis_index("mer")
    bit = 1
    while bit < count:
        other = lax.ppermute(column, "mer", [(i, i ^ bit) for i in range(count)])
        low_half = (me & bit) == 0
        column = jnp.concatenate(
            [jnp.where(low_half, column, other), jnp.where(low_half, other, column)], axis=0
        )
        bit *= 2
    return column


def as_lane_column(cols):
    return jnp.transpose(cols)[:, :, None]


def operator_kernel(slots, *refs):
    extra = len(slots) - 1
    (v_ref, vab_ref, vbe_ref, h_ref, e_ref, n_ref, up_ref, upb_ref, ew_ref, ns_ref,
     ve_ref, vw_ref, vn_ref, vs_ref) = refs[:14]
    partner_refs = (v_ref,) + refs[14:14 + extra]
    img_ref, part_ref = refs[14 + extra:]
    block, rows, cols = v_ref.shape
    i = pl.program_id(0)
    last_block = pl.num_programs(0) - 1
    lane = lax.broadcasted_iota(jnp.int32, (rows, cols), 1)
    row = lax.broadcasted_iota(jnp.int32, (rows, cols), 0)
    first_lane, last_lane = lane == 0, lane == cols - 1
    first_row, last_row = row == 0, row == rows - 1
    zero = jnp.zeros((rows, cols), jnp.float32)
    above = jnp.where(i == last_block, zero, vab_ref[0])
    below = jnp.where(i == 0, zero, vbe_ref[0])
    up_below = jnp.where(i == 0, zero, upb_ref[0])

    @pl.when(i == 0)
    def _():
        part_ref[...] = jnp.zeros_like(part_ref)

    def level(k, accs):
        v = v_ref[k]
        up_side = jnp.where(k == block - 1, above, v_ref[jnp.minimum(k + 1, block - 1)])
        down_side = jnp.where(k == 0, below, v_ref[jnp.maximum(k - 1, 0)])
        lower = jnp.where(k == 0, up_below, up_ref[jnp.maximum(k - 1, 0)])
        east_side = jnp.where(last_lane, jnp.broadcast_to(ve_ref[k], (rows, cols)),
                              pltpu.roll(v, cols - 1, 1))
        west_side = jnp.where(first_lane, jnp.broadcast_to(vw_ref[k], (rows, cols)),
                              pltpu.roll(v, 1, 1))
        north_side = jnp.where(last_row, jnp.broadcast_to(vn_ref[k], (rows, cols)),
                               pltpu.roll(v, rows - 1, 0))
        south_side = jnp.where(first_row, jnp.broadcast_to(vs_ref[k], (rows, cols)),
                               pltpu.roll(v, 1, 0))
        east = e_ref[k]
        north = n_ref[k]
        west = jnp.where(first_lane, jnp.broadcast_to(ew_ref[k], (rows, cols)),
                         pltpu.roll(east, 1, 1))
        south = jnp.where(first_row, jnp.broadcast_to(ns_ref[k], (rows, cols)),
                          pltpu.roll(north, 1, 0))
        image = (
            h_ref[k] * v
            + east * (v - east_side)
            + west * (v - west_side)
            + north * (v - north_side)
            + south * (v - south_side)
            + up_ref[k] * (v - up_side)
            + lower * (v - down_side)
        )
        img_ref[k] = image
        return tuple(acc + ref[k] * image for acc, ref in zip(accs, partner_refs))

    accs = lax.fori_loop(0, block, level, (zero,) * len(slots))
    add_totals(part_ref, slots, accs)


def apply_operator(direction, coefs, halos, slots, extra=()):
    helm_diag, east_coef, north_coef, upper, east_west, north_south = coefs
    east_halo, west_halo, north_halo, south_halo = halos
    levels, rows, cols = direction.shape
    block = LEVEL_BLOCK if levels % LEVEL_BLOCK == 0 else levels
    blocks = levels // block
    full = pl.BlockSpec((block, rows, cols), lambda i: (i, 0, 0))
    lane_col = pl.BlockSpec((block, rows, 1), lambda i: (i, 0, 0))
    first_col = pl.BlockSpec((None, block, rows, 1), lambda i: (0, i, 0, 0))
    row_spec = pl.BlockSpec((block, 1, cols), lambda i: (i, 0, 0))
    above = pl.BlockSpec((1, rows, cols), lambda i: (jnp.minimum((i + 1) * block, levels - 1), 0, 0))
    below = pl.BlockSpec((1, rows, cols), lambda i: (jnp.maximum(i * block - 1, 0), 0, 0))
    kernel = lambda *refs: operator_kernel(slots, *refs)
    image, part = pl.pallas_call(
        kernel,
        grid=(blocks,),
        in_specs=[full, above, below, full, full, full, full, below, first_col, row_spec,
                  lane_col, lane_col, row_spec, row_spec] + [full] * len(extra),
        out_specs=[full, tile_spec()],
        out_shape=[jax.ShapeDtypeStruct(direction.shape, jnp.float32), tile_shape()],
    )(direction, direction, direction, helm_diag, east_coef, north_coef, upper, upper,
      east_west, north_south, east_halo, west_halo, north_halo, south_halo, *extra)
    return image, part


def finish_kernel(sums_ref, p0_ref, q_ref, r0_ref, a0_ref, aq_ref, sol_ref, res_ref):
    block, rows, cols = p0_ref.shape
    sums = sums_ref[...]
    norm0, curv0, r0q, a0q, qaq, p0aq = (
        jnp.broadcast_to(sums[j:j + 1, :], sums.shape) for j in range(6)
    )
    step0 = norm0 / curv0
    norm1 = norm0 - step0 * (r0q + curv0) + step0 * step0 * a0q
    p1ap1 = curv0 - step0 * (p0aq + a0q) + step0 * step0 * qaq
    p1a0 = curv0 - step0 * a0q
    d0ap1 = curv0 - step0 * p0aq
    beta = norm1 / norm0
    curv1 = p1ap1 + beta * (p1a0 + d0ap1) + beta * beta * curv0
    step1 = norm1 / curv1
    widen = lambda x: jnp.concatenate([x[:rows]] * (cols // x.shape[1]), axis=1)
    step0, beta, step1 = widen(step0), widen(beta), widen(step1)

    def level(k, carry):
        p0 = p0_ref[k]
        a0 = a0_ref[k]
        precond1 = p0 - step0 * q_ref[k]
        direction1 = precond1 + beta * p0
        image1 = (a0 - step0 * aq_ref[k]) + beta * a0
        sol_ref[k] = step0 * p0 + step1 * direction1
        res_ref[k] = (r0_ref[k] - step0 * a0) - step1 * image1
        return carry

    lax.fori_loop(0, block, level, 0)


def finish(sums, precond0, basis, right_side, image0, image_q):
    levels, rows, cols = precond0.shape
    block = LEVEL_BLOCK if levels % LEVEL_BLOCK == 0 else levels
    full = pl.BlockSpec((block, rows, cols), lambda i: (i, 0, 0))
    field = jax.ShapeDtypeStruct(precond0.shape, jnp.float32)
    return pl.pallas_call(
        finish_kernel,
        grid=(levels // block,),
        in_specs=[tile_spec(), full, full, full, full, full],
        out_specs=[full, full],
        out_shape=[field, field],
    )(sums, precond0, basis, right_side, image0, image_q)


def exchange(direction, top, bottom, tables, use_mortar):
    west, east = belt_cols(direction)
    first_map, second_map, first_weight, second_weight = tables
    whole = gather_rows(east)
    arrived = first_weight[:, None] * whole[first_map] + second_weight[:, None] * whole[second_map]
    east = jnp.where(use_mortar, arrived, east)
    south, north = mer_rows(top, bottom)
    return as_lane_column(east), as_lane_column(west), north, south


def on_device(
    right_side,
    helm_diag,
    east_coef,
    north_coef,
    vert_coef,
    mortar_weights,
    weight_index,
    edge_map,
    refined,
):
    belt_index = lax.axis_index("belt")
    mer_index = lax.axis_index("mer")
    per_panel = lax.axis_size("belt") // 4
    rows = right_side.shape[1]
    row_start = mer_index * rows
    own_edge = belt_index // per_panel
    row_flags = lax.dynamic_slice_in_dim(refined[own_edge], row_start, rows, 0)
    at_edge = (belt_index + 1) % per_panel == 0
    use_mortar = jnp.logical_and(at_edge, row_flags == 1)[:, None]
    tables = edge_tables(own_edge, row_start, rows, weight_index, edge_map, mortar_weights)
    levels, _, cols = right_side.shape
    block = BLOCK_COLS if cols % BLOCK_COLS == 0 else cols
    coef_west, _ = belt_cols(east_coef)
    coef_south, _ = mer_rows(north_coef[:, -1:, :], north_coef[:, :1, :])
    east_left = jnp.stack(
        [jnp.transpose(coef_west)]
        + [east_coef[:, :, j * block - 1] for j in range(1, cols // block)],
        axis=0,
    )[..., None]
    upper = jnp.concatenate([vert_coef, jnp.zeros_like(vert_coef[:1])], axis=0)
    coefs = (helm_diag, east_coef, north_coef, upper, east_left, coef_south)

    inverse_pivot, ratio_values, precond0, top0, bottom0, part0 = factor_solve(
        helm_diag, east_coef, north_coef, vert_coef, right_side, east_left, coef_south
    )
    image0, curv_part0 = apply_operator(
        precond0, coefs, exchange(precond0, top0, bottom0, tables, use_mortar), (1,)
    )
    basis, top_q, bottom_q, basis_part = solve(
        image0, inverse_pivot, ratio_values, vert_coef, (right_side,), (2, 3)
    )
    image_q, image_q_part = apply_operator(
        basis, coefs, exchange(basis, top_q, bottom_q, tables, use_mortar), (4, 5), (precond0,)
    )
    sums = tree_sum(part0 + curv_part0 + basis_part + image_q_part)
    return finish(sums, precond0, basis, right_side, image0, image_q)


def solution(mesh):
    placed = (
        P(None, "mer", "belt"),
        P(None, "mer", "belt"),
        P(None, "mer", "belt"),
        P(None, "mer", "belt"),
        P(None, "mer", "belt"),
        P(),
        P(),
        P(),
        P(),
    )
    return jax.shard_map(
        on_device,
        mesh=mesh,
        in_specs=placed,
        out_specs=(P(None, "mer", "belt"), P(None, "mer", "belt")),
        check_vma=False,
    )
```

```python
import jax
import jax.numpy as jnp
from jax import lax
from jax.experimental import pallas as pl
from jax.experimental.pallas import tpu as pltpu
from jax.sharding import PartitionSpec as P

ITERS = 2
BLOCK_COLS = 384
LEVEL_BLOCK = 24


def tree_sum(values):
    for axis in ("mer", "belt"):
        count = lax.axis_size(axis)
        if count & (count - 1):
            values = lax.psum(values, axis)
            continue
        bit = 1
        while bit < count:
            values = values + lax.ppermute(values, axis, [(i, i ^ bit) for i in range(count)])
            bit *= 2
    return values


def add_totals(part_ref, slots, accs):
    row = lax.broadcasted_iota(jnp.int32, part_ref.shape, 0)
    tile = part_ref[...]
    for slot, acc in zip(slots, accs):
        tile = tile + jnp.where(row == slot, jnp.sum(acc), 0.0)
    part_ref[...] = tile


def tile_spec():
    return pl.BlockSpec((8, 128), lambda j: (0, 0))


def tile_shape():
    return jax.ShapeDtypeStruct((8, 128), jnp.float32)


def row_block(levels, block):
    return pl.BlockSpec((levels, 1, block), lambda j: (0, 0, j))


def row_shape(levels, cols):
    return jax.ShapeDtypeStruct((levels, 1, cols), jnp.float32)


def column_spec(levels, rows, cols):
    return pl.BlockSpec((levels, rows, cols), lambda j: (0, 0, j))


def factor_solve_kernel(h_ref, e_ref, n_ref, v_ref, r_ref, eleft_ref, nsouth_ref,
                        inv_ref, ratio_ref, p_ref, top_ref, bottom_ref, part_ref):
    levels, rows, cols = h_ref.shape

    @pl.when(pl.program_id(0) == 0)
    def _():
        part_ref[...] = jnp.zeros_like(part_ref)

    zero = jnp.zeros((rows, cols), jnp.float32)
    first_lane = lax.broadcasted_iota(jnp.int32, (rows, cols), 1) == 0
    first_row = lax.broadcasted_iota(jnp.int32, (rows, cols), 0) == 0

    def forward(k, up, down, prev, elim):
        east = e_ref[k]
        north = n_ref[k]
        west = jnp.where(first_lane, jnp.broadcast_to(eleft_ref[k], (rows, cols)),
                         pltpu.roll(east, 1, 1))
        south = jnp.where(first_row, jnp.broadcast_to(nsouth_ref[k], (rows, cols)),
                          pltpu.roll(north, 1, 0))
        diag = h_ref[k] + east + west + north + south + up + down
        ratio = down / prev
        pivot = diag - down * ratio
        inv_ref[k] = 1.0 / pivot
        ratio_ref[k] = ratio
        elim = r_ref[k] + ratio * elim
        p_ref[k] = elim
        return pivot, elim

    carry = forward(0, v_ref[0], zero, jnp.ones_like(zero), zero)
    carry = lax.fori_loop(
        1, levels - 1, lambda k, c: forward(k, v_ref[k], v_ref[k - 1], *c), carry, unroll=4
    )
    forward(levels - 1, zero, v_ref[levels - 2], *carry)

    def backward(k, up, succ, acc):
        value = inv_ref[k] * (p_ref[k] + up * succ)
        p_ref[k] = value
        top_ref[k] = value[rows - 1:rows]
        bottom_ref[k] = value[:1]
        return value, acc + r_ref[k] * value

    carry = backward(levels - 1, zero, zero, zero)
    carry = lax.fori_loop(
        0, levels - 1, lambda i, c: backward(levels - 2 - i, v_ref[levels - 2 - i], *c), carry,
        unroll=4,
    )
    add_totals(part_ref, (0,), (carry[1],))


def factor_solve(helm_diag, east_coef, north_coef, vert_coef, rhs, east_left, north_south):
    levels, rows, cols = rhs.shape
    block = BLOCK_COLS if cols % BLOCK_COLS == 0 else cols
    full = column_spec(levels, rows, block)
    vspec = column_spec(levels - 1, rows, block)
    field = jax.ShapeDtypeStruct(rhs.shape, jnp.float32)
    return pl.pallas_call(
        factor_solve_kernel,
        grid=(cols // block,),
        in_specs=[full, full, full, vspec, full,
                  pl.BlockSpec((None, levels, rows, 1), lambda j: (j, 0, 0, 0)),
                  pl.BlockSpec((levels, 1, block), lambda j: (0, 0, j))],
        out_specs=[full, full, full, row_block(levels, block), row_block(levels, block),
                   tile_spec()],
        out_shape=[field, field, field, row_shape(levels, cols), row_shape(levels, cols),
                   tile_shape()],
    )(helm_diag, east_coef, north_coef, vert_coef, rhs, east_left, north_south)


def solve_kernel(slots, *refs):
    count = len(slots)
    val_ref, inv_ref, ratio_ref, v_ref = refs[:4]
    partner_refs = refs[4:4 + count - 1] + (val_ref,)
    p_ref, top_ref, bottom_ref, part_ref = refs[4 + count - 1:]
    levels = val_ref.shape[0]
    zero = jnp.zeros(val_ref.shape[1:], jnp.float32)

    @pl.when(pl.program_id(0) == 0)
    def _():
        part_ref[...] = jnp.zeros_like(part_ref)

    def forward(k, elim):
        elim = val_ref[k] + ratio_ref[k] * elim
        p_ref[k] = elim
        return elim

    lax.fori_loop(0, levels, forward, zero, unroll=4)

    def backward(k, up, succ, accs):
        value = inv_ref[k] * (p_ref[k] + up * succ)
        p_ref[k] = value
        top_ref[k] = value[value.shape[0] - 1:]
        bottom_ref[k] = value[:1]
        return value, tuple(acc + ref[k] * value for acc, ref in zip(accs, partner_refs))

    carry = backward(levels - 1, zero, zero, (zero,) * count)
    carry = lax.fori_loop(
        0, levels - 1, lambda i, c: backward(levels - 2 - i, v_ref[levels - 2 - i], *c), carry,
        unroll=4,
    )
    add_totals(part_ref, slots, carry[1])


def solve(values, inverse_pivot, ratio_values, vert_coef, partners, slots):
    levels, rows, cols = values.shape
    block = BLOCK_COLS if cols % BLOCK_COLS == 0 else cols
    full = column_spec(levels, rows, block)
    vspec = column_spec(levels - 1, rows, block)
    return pl.pallas_call(
        lambda *refs: solve_kernel(slots, *refs),
        grid=(cols // block,),
        in_specs=[full, full, full, vspec] + [full] * len(partners),
        out_specs=[full, row_block(levels, block), row_block(levels, block), tile_spec()],
        out_shape=[jax.ShapeDtypeStruct(values.shape, jnp.float32), row_shape(levels, cols),
                   row_shape(levels, cols), tile_shape()],
    )(values, inverse_pivot, ratio_values, vert_coef, *partners)


def edge_tables(edge_num, row_start, rows, weight_index, edge_map, mortar_weights):
    maps = lax.dynamic_slice_in_dim(edge_map[edge_num], row_start, rows, 0)
    picks = lax.dynamic_slice_in_dim(weight_index[edge_num], row_start, rows, 0)
    return (maps[:, 0], maps[:, 1], mortar_weights[picks, 0], mortar_weights[picks, 1])


def belt_cols(field):
    count = lax.axis_size("belt")
    first = jnp.transpose(field[:, :, 0])
    last = jnp.transpose(field[:, :, -1])
    west = lax.ppermute(last, "belt", [(i, (i + 1) % count) for i in range(count)])
    east = lax.ppermute(first, "belt", [((i + 1) % count, i) for i in range(count)])
    return west, east


def mer_rows(top, bottom):
    count = lax.axis_size("mer")
    south = lax.ppermute(top, "mer", [(i, i + 1) for i in range(count - 1)])
    north = lax.ppermute(bottom, "mer", [(i + 1, i) for i in range(count - 1)])
    return south, north


def gather_rows(column):
    count = lax.axis_size("mer")
    if count & (count - 1):
        return lax.all_gather(column, "mer", axis=0, tiled=True)
    me = lax.axis_index("mer")
    bit = 1
    while bit < count:
        other = lax.ppermute(column, "mer", [(i, i ^ bit) for i in range(count)])
        low_half = (me & bit) == 0
        column = jnp.concatenate(
            [jnp.where(low_half, column, other), jnp.where(low_half, other, column)], axis=0
        )
        bit *= 2
    return column


def as_lane_column(cols):
    return jnp.transpose(cols)[:, :, None]


def operator_kernel(slots, *refs):
    extra = len(slots) - 1
    (v_ref, vab_ref, vbe_ref, h_ref, e_ref, n_ref, up_ref, upb_ref, ew_ref, ns_ref,
     ve_ref, vw_ref, vn_ref, vs_ref) = refs[:14]
    partner_refs = (v_ref,) + refs[14:14 + extra]
    img_ref, part_ref = refs[14 + extra:]
    block, rows, cols = v_ref.shape
    i = pl.program_id(0)
    last_block = pl.num_programs(0) - 1
    lane = lax.broadcasted_iota(jnp.int32, (rows, cols), 1)
    row = lax.broadcasted_iota(jnp.int32, (rows, cols), 0)
    first_lane, last_lane = lane == 0, lane == cols - 1
    first_row, last_row = row == 0, row == rows - 1
    zero = jnp.zeros((rows, cols), jnp.float32)
    above = jnp.where(i == last_block, zero, vab_ref[0])
    below = jnp.where(i == 0, zero, vbe_ref[0])
    up_below = jnp.where(i == 0, zero, upb_ref[0])

    @pl.when(i == 0)
    def _():
        part_ref[...] = jnp.zeros_like(part_ref)

    edge = min(cols, 128)
    lane_e = lax.broadcasted_iota(jnp.int32, (rows, edge), 1)

    def first_tile(halo_ref, k, rolled):
        fixed = jnp.where(lane_e == 0, jnp.broadcast_to(halo_ref[k], (rows, edge)), rolled[:, :edge])
        return jnp.concatenate([fixed, rolled[:, edge:]], axis=1) if cols > edge else fixed

    def last_tile(halo_ref, k, rolled):
        fixed = jnp.where(lane_e == edge - 1, jnp.broadcast_to(halo_ref[k], (rows, edge)),
                          rolled[:, cols - edge:])
        return jnp.concatenate([rolled[:, :cols - edge], fixed], axis=1) if cols > edge else fixed

    def level(k, up_side, down_side, lower, accs):
        v = v_ref[k]
        east_side = last_tile(ve_ref, k, pltpu.roll(v, cols - 1, 1))
        west_side = first_tile(vw_ref, k, pltpu.roll(v, 1, 1))
        north_side = jnp.where(last_row, jnp.broadcast_to(vn_ref[k], (rows, cols)),
                               pltpu.roll(v, rows - 1, 0))
        south_side = jnp.where(first_row, jnp.broadcast_to(vs_ref[k], (rows, cols)),
                               pltpu.roll(v, 1, 0))
        east = e_ref[k]
        north = n_ref[k]
        west = first_tile(ew_ref, k, pltpu.roll(east, 1, 1))
        south = jnp.where(first_row, jnp.broadcast_to(ns_ref[k], (rows, cols)),
                          pltpu.roll(north, 1, 0))
        image = (
            h_ref[k] * v
            + east * (v - east_side)
            + west * (v - west_side)
            + north * (v - north_side)
            + south * (v - south_side)
            + up_ref[k] * (v - up_side)
            + lower * (v - down_side)
        )
        img_ref[k] = image
        return tuple(acc + ref[k] * image for acc, ref in zip(accs, partner_refs))

    accs = (zero,) * len(slots)
    if block == 1:
        accs = level(0, above, below, up_below, accs)
    else:
        accs = level(0, v_ref[1], below, up_below, accs)
        accs = lax.fori_loop(
            1, block - 1,
            lambda k, c: level(k, v_ref[k + 1], v_ref[k - 1], up_ref[k - 1], c), accs,
        )
        accs = level(block - 1, above, v_ref[block - 2], up_ref[block - 2], accs)
    add_totals(part_ref, slots, accs)


def apply_operator(direction, coefs, halos, slots, extra=()):
    helm_diag, east_coef, north_coef, upper, east_west, north_south = coefs
    east_halo, west_halo, north_halo, south_halo = halos
    levels, rows, cols = direction.shape
    block = LEVEL_BLOCK if levels % LEVEL_BLOCK == 0 else levels
    blocks = levels // block
    full = pl.BlockSpec((block, rows, cols), lambda i: (i, 0, 0))
    lane_col = pl.BlockSpec((block, rows, 1), lambda i: (i, 0, 0))
    first_col = pl.BlockSpec((None, block, rows, 1), lambda i: (0, i, 0, 0))
    row_spec = pl.BlockSpec((block, 1, cols), lambda i: (i, 0, 0))
    above = pl.BlockSpec((1, rows, cols), lambda i: (jnp.minimum((i + 1) * block, levels - 1), 0, 0))
    below = pl.BlockSpec((1, rows, cols), lambda i: (jnp.maximum(i * block - 1, 0), 0, 0))
    kernel = lambda *refs: operator_kernel(slots, *refs)
    image, part = pl.pallas_call(
        kernel,
        grid=(blocks,),
        in_specs=[full, above, below, full, full, full, full, below, first_col, row_spec,
                  lane_col, lane_col, row_spec, row_spec] + [full] * len(extra),
        out_specs=[full, tile_spec()],
        out_shape=[jax.ShapeDtypeStruct(direction.shape, jnp.float32), tile_shape()],
    )(direction, direction, direction, helm_diag, east_coef, north_coef, upper, upper,
      east_west, north_south, east_halo, west_halo, north_halo, south_halo, *extra)
    return image, part


def finish_kernel(sums_ref, p0_ref, q_ref, r0_ref, a0_ref, aq_ref, sol_ref, res_ref):
    block, rows, cols = p0_ref.shape
    sums = sums_ref[...]
    norm0, curv0, r0q, a0q, qaq, p0aq = (
        jnp.broadcast_to(sums[j:j + 1, :], sums.shape) for j in range(6)
    )
    step0 = norm0 / curv0
    norm1 = norm0 - step0 * (r0q + curv0) + step0 * step0 * a0q
    p1ap1 = curv0 - step0 * (p0aq + a0q) + step0 * step0 * qaq
    p1a0 = curv0 - step0 * a0q
    d0ap1 = curv0 - step0 * p0aq
    beta = norm1 / norm0
    curv1 = p1ap1 + beta * (p1a0 + d0ap1) + beta * beta * curv0
    step1 = norm1 / curv1
    widen = lambda x: jnp.concatenate([x[:rows]] * (cols // x.shape[1]), axis=1)
    step0, beta, step1 = widen(step0), widen(beta), widen(step1)

    def level(k, carry):
        p0 = p0_ref[k]
        a0 = a0_ref[k]
        precond1 = p0 - step0 * q_ref[k]
        direction1 = precond1 + beta * p0
        image1 = (a0 - step0 * aq_ref[k]) + beta * a0
        sol_ref[k] = step0 * p0 + step1 * direction1
        res_ref[k] = (r0_ref[k] - step0 * a0) - step1 * image1
        return carry

    lax.fori_loop(0, block, level, 0)


def finish(sums, precond0, basis, right_side, image0, image_q):
    levels, rows, cols = precond0.shape
    block = LEVEL_BLOCK if levels % LEVEL_BLOCK == 0 else levels
    full = pl.BlockSpec((block, rows, cols), lambda i: (i, 0, 0))
    field = jax.ShapeDtypeStruct(precond0.shape, jnp.float32)
    return pl.pallas_call(
        finish_kernel,
        grid=(levels // block,),
        in_specs=[tile_spec(), full, full, full, full, full],
        out_specs=[full, full],
        out_shape=[field, field],
    )(sums, precond0, basis, right_side, image0, image_q)


def exchange(direction, top, bottom, tables, use_mortar):
    west, east = belt_cols(direction)
    first_map, second_map, first_weight, second_weight = tables
    whole = gather_rows(east)
    arrived = first_weight[:, None] * whole[first_map] + second_weight[:, None] * whole[second_map]
    east = jnp.where(use_mortar, arrived, east)
    south, north = mer_rows(top, bottom)
    return as_lane_column(east), as_lane_column(west), north, south


def on_device(
    right_side,
    helm_diag,
    east_coef,
    north_coef,
    vert_coef,
    mortar_weights,
    weight_index,
    edge_map,
    refined,
):
    belt_index = lax.axis_index("belt")
    mer_index = lax.axis_index("mer")
    per_panel = lax.axis_size("belt") // 4
    rows = right_side.shape[1]
    row_start = mer_index * rows
    own_edge = belt_index // per_panel
    row_flags = lax.dynamic_slice_in_dim(refined[own_edge], row_start, rows, 0)
    at_edge = (belt_index + 1) % per_panel == 0
    use_mortar = jnp.logical_and(at_edge, row_flags == 1)[:, None]
    tables = edge_tables(own_edge, row_start, rows, weight_index, edge_map, mortar_weights)
    levels, _, cols = right_side.shape
    block = BLOCK_COLS if cols % BLOCK_COLS == 0 else cols
    coef_west, _ = belt_cols(east_coef)
    coef_south, _ = mer_rows(north_coef[:, -1:, :], north_coef[:, :1, :])
    east_left = jnp.stack(
        [jnp.transpose(coef_west)]
        + [east_coef[:, :, j * block - 1] for j in range(1, cols // block)],
        axis=0,
    )[..., None]
    upper = jnp.concatenate([vert_coef, jnp.zeros_like(vert_coef[:1])], axis=0)
    coefs = (helm_diag, east_coef, north_coef, upper, east_left, coef_south)

    inverse_pivot, ratio_values, precond0, top0, bottom0, part0 = factor_solve(
        helm_diag, east_coef, north_coef, vert_coef, right_side, east_left, coef_south
    )
    image0, curv_part0 = apply_operator(
        precond0, coefs, exchange(precond0, top0, bottom0, tables, use_mortar), (1,)
    )
    basis, top_q, bottom_q, basis_part = solve(
        image0, inverse_pivot, ratio_values, vert_coef, (right_side,), (2, 3)
    )
    image_q, image_q_part = apply_operator(
        basis, coefs, exchange(basis, top_q, bottom_q, tables, use_mortar), (4, 5), (precond0,)
    )
    sums = tree_sum(part0 + curv_part0 + basis_part + image_q_part)
    return finish(sums, precond0, basis, right_side, image0, image_q)


def solution(mesh):
    placed = (
        P(None, "mer", "belt"),
        P(None, "mer", "belt"),
        P(None, "mer", "belt"),
        P(None, "mer", "belt"),
        P(None, "mer", "belt"),
        P(),
        P(),
        P(),
        P(),
    )
    return jax.shard_map(
        on_device,
        mesh=mesh,
        in_specs=placed,
        out_specs=(P(None, "mer", "belt"), P(None, "mer", "belt")),
        check_vma=False,
    )
```

```python
import jax
import jax.numpy as jnp
from jax import lax
from jax.experimental import pallas as pl
from jax.experimental.pallas import tpu as pltpu
from jax.sharding import PartitionSpec as P

ITERS = 2
BLOCK_COLS = 384
LEVEL_BLOCK = 24


def tree_sum(values):
    for axis in ("mer", "belt"):
        count = lax.axis_size(axis)
        if count & (count - 1):
            values = lax.psum(values, axis)
            continue
        bit = 1
        while bit < count:
            values = values + lax.ppermute(values, axis, [(i, i ^ bit) for i in range(count)])
            bit *= 2
    return values


def add_totals(part_ref, slots, accs):
    row = lax.broadcasted_iota(jnp.int32, part_ref.shape, 0)
    tile = part_ref[...]
    for slot, acc in zip(slots, accs):
        tile = tile + jnp.where(row == slot, jnp.sum(acc), 0.0)
    part_ref[...] = tile


def tile_spec():
    return pl.BlockSpec((8, 128), lambda j: (0, 0))


def tile_shape():
    return jax.ShapeDtypeStruct((8, 128), jnp.float32)


def row_block(levels, block):
    return pl.BlockSpec((levels, 1, block), lambda j: (0, 0, j))


def row_shape(levels, cols):
    return jax.ShapeDtypeStruct((levels, 1, cols), jnp.float32)


def column_spec(levels, rows, cols):
    return pl.BlockSpec((levels, rows, cols), lambda j: (0, 0, j))


def factor_solve_kernel(h_ref, e_ref, n_ref, v_ref, r_ref, eleft_ref, nsouth_ref,
                        inv_ref, ratio_ref, p_ref, top_ref, bottom_ref, part_ref):
    levels, rows, cols = h_ref.shape

    @pl.when(pl.program_id(0) == 0)
    def _():
        part_ref[...] = jnp.zeros_like(part_ref)

    zero = jnp.zeros((rows, cols), jnp.float32)
    first_lane = lax.broadcasted_iota(jnp.int32, (rows, cols), 1) == 0
    first_row = lax.broadcasted_iota(jnp.int32, (rows, cols), 0) == 0

    def forward(k, up, down, prev, elim):
        east = e_ref[k]
        north = n_ref[k]
        west = jnp.where(first_lane, jnp.broadcast_to(eleft_ref[k], (rows, cols)),
                         pltpu.roll(east, 1, 1))
        south = jnp.where(first_row, jnp.broadcast_to(nsouth_ref[k], (rows, cols)),
                          pltpu.roll(north, 1, 0))
        diag = h_ref[k] + east + west + north + south + up + down
        ratio = down / prev
        pivot = diag - down * ratio
        inv_ref[k] = 1.0 / pivot
        ratio_ref[k] = ratio
        elim = r_ref[k] + ratio * elim
        p_ref[k] = elim
        return pivot, elim

    carry = forward(0, v_ref[0], zero, jnp.ones_like(zero), zero)
    carry = lax.fori_loop(
        1, levels - 1, lambda k, c: forward(k, v_ref[k], v_ref[k - 1], *c), carry, unroll=4
    )
    forward(levels - 1, zero, v_ref[levels - 2], *carry)

    def backward(k, up, succ, acc):
        value = inv_ref[k] * (p_ref[k] + up * succ)
        p_ref[k] = value
        top_ref[k] = value[rows - 1:rows]
        bottom_ref[k] = value[:1]
        return value, acc + r_ref[k] * value

    carry = backward(levels - 1, zero, zero, zero)
    carry = lax.fori_loop(
        0, levels - 1, lambda i, c: backward(levels - 2 - i, v_ref[levels - 2 - i], *c), carry,
        unroll=4,
    )
    add_totals(part_ref, (0,), (carry[1],))


def factor_solve(helm_diag, east_coef, north_coef, vert_coef, rhs, east_left, north_south):
    levels, rows, cols = rhs.shape
    block = BLOCK_COLS if cols % BLOCK_COLS == 0 else cols
    full = column_spec(levels, rows, block)
    vspec = column_spec(levels - 1, rows, block)
    field = jax.ShapeDtypeStruct(rhs.shape, jnp.float32)
    return pl.pallas_call(
        factor_solve_kernel,
        grid=(cols // block,),
        in_specs=[full, full, full, vspec, full,
                  pl.BlockSpec((None, levels, rows, 1), lambda j: (j, 0, 0, 0)),
                  pl.BlockSpec((levels, 1, block), lambda j: (0, 0, j))],
        out_specs=[full, full, full, row_block(levels, block), row_block(levels, block),
                   tile_spec()],
        out_shape=[field, field, field, row_shape(levels, cols), row_shape(levels, cols),
                   tile_shape()],
    )(helm_diag, east_coef, north_coef, vert_coef, rhs, east_left, north_south)


def solve_kernel(slots, *refs):
    count = len(slots)
    val_ref, inv_ref, ratio_ref, v_ref = refs[:4]
    partner_refs = refs[4:4 + count - 1] + (val_ref,)
    p_ref, top_ref, bottom_ref, part_ref = refs[4 + count - 1:]
    levels = val_ref.shape[0]
    zero = jnp.zeros(val_ref.shape[1:], jnp.float32)

    @pl.when(pl.program_id(0) == 0)
    def _():
        part_ref[...] = jnp.zeros_like(part_ref)

    def forward(k, elim):
        elim = val_ref[k] + ratio_ref[k] * elim
        p_ref[k] = elim
        return elim

    lax.fori_loop(0, levels, forward, zero, unroll=4)

    def backward(k, up, succ, accs):
        value = inv_ref[k] * (p_ref[k] + up * succ)
        p_ref[k] = value
        top_ref[k] = value[value.shape[0] - 1:]
        bottom_ref[k] = value[:1]
        return value, tuple(acc + ref[k] * value for acc, ref in zip(accs, partner_refs))

    carry = backward(levels - 1, zero, zero, (zero,) * count)
    carry = lax.fori_loop(
        0, levels - 1, lambda i, c: backward(levels - 2 - i, v_ref[levels - 2 - i], *c), carry,
        unroll=4,
    )
    add_totals(part_ref, slots, carry[1])


def solve(values, inverse_pivot, ratio_values, vert_coef, partners, slots):
    levels, rows, cols = values.shape
    block = BLOCK_COLS if cols % BLOCK_COLS == 0 else cols
    full = column_spec(levels, rows, block)
    vspec = column_spec(levels - 1, rows, block)
    return pl.pallas_call(
        lambda *refs: solve_kernel(slots, *refs),
        grid=(cols // block,),
        in_specs=[full, full, full, vspec] + [full] * len(partners),
        out_specs=[full, row_block(levels, block), row_block(levels, block), tile_spec()],
        out_shape=[jax.ShapeDtypeStruct(values.shape, jnp.float32), row_shape(levels, cols),
                   row_shape(levels, cols), tile_shape()],
    )(values, inverse_pivot, ratio_values, vert_coef, *partners)


def edge_tables(edge_num, row_start, rows, weight_index, edge_map, mortar_weights):
    maps = lax.dynamic_slice_in_dim(edge_map[edge_num], row_start, rows, 0)
    picks = lax.dynamic_slice_in_dim(weight_index[edge_num], row_start, rows, 0)
    return (maps[:, 0], maps[:, 1], mortar_weights[picks, 0], mortar_weights[picks, 1])


def belt_cols(field):
    count = lax.axis_size("belt")
    first = jnp.transpose(field[:, :, 0])
    last = jnp.transpose(field[:, :, -1])
    west = lax.ppermute(last, "belt", [(i, (i + 1) % count) for i in range(count)])
    east = lax.ppermute(first, "belt", [((i + 1) % count, i) for i in range(count)])
    return west, east


def mer_rows(top, bottom):
    count = lax.axis_size("mer")
    south = lax.ppermute(top, "mer", [(i, i + 1) for i in range(count - 1)])
    north = lax.ppermute(bottom, "mer", [(i + 1, i) for i in range(count - 1)])
    return south, north


def gather_rows(column):
    count = lax.axis_size("mer")
    if count & (count - 1):
        return lax.all_gather(column, "mer", axis=0, tiled=True)
    me = lax.axis_index("mer")
    bit = 1
    while bit < count:
        other = lax.ppermute(column, "mer", [(i, i ^ bit) for i in range(count)])
        low_half = (me & bit) == 0
        column = jnp.concatenate(
            [jnp.where(low_half, column, other), jnp.where(low_half, other, column)], axis=0
        )
        bit *= 2
    return column


def as_lane_column(cols):
    return jnp.transpose(cols)[:, :, None]


def operator_kernel(slots, *refs):
    extra = len(slots) - 1
    (v_ref, vab_ref, vbe_ref, h_ref, e_ref, n_ref, up_ref, upb_ref, ew_ref, ns_ref,
     ve_ref, vw_ref, vn_ref, vs_ref) = refs[:14]
    partner_refs = (v_ref,) + refs[14:14 + extra]
    img_ref, part_ref = refs[14 + extra:]
    block, rows, cols = v_ref.shape
    i = pl.program_id(0)
    last_block = pl.num_programs(0) - 1
    keep_above = jnp.where(i == last_block, 0.0, 1.0)
    keep_below = jnp.where(i == 0, 0.0, 1.0)

    @pl.when(i == 0)
    def _():
        part_ref[...] = jnp.zeros_like(part_ref)

    width = 128 if cols % 128 == 0 else cols
    tiles = cols // width
    lane_t = lax.broadcasted_iota(jnp.int32, (rows, width), 1)
    row_t = lax.broadcasted_iota(jnp.int32, (rows, width), 0)
    top_t, bottom_t = row_t == rows - 1, row_t == 0
    first_t, last_t = lane_t == 0, lane_t == width - 1

    def level(k, up_at, down_at, lower_at, accs):
        accs = list(accs)
        v_all = [v_ref[k, :, t * width:(t + 1) * width] for t in range(tiles)]
        e_all = [e_ref[k, :, t * width:(t + 1) * width] for t in range(tiles)]
        v_west = jnp.broadcast_to(vw_ref[k], (rows, width))
        v_east = jnp.broadcast_to(ve_ref[k], (rows, width))
        e_west = jnp.broadcast_to(ew_ref[k], (rows, width))
        for t in range(tiles):
            sl = slice(t * width, (t + 1) * width)
            v = v_all[t]
            v_next = v_all[t + 1] if t + 1 < tiles else v_east
            v_prev = v_all[t - 1] if t > 0 else v_west
            east = e_all[t]
            e_prev = e_all[t - 1] if t > 0 else e_west
            east_side = jnp.where(last_t, pltpu.roll(v_next, width - 1, 1),
                                  pltpu.roll(v, width - 1, 1))
            west_side = jnp.where(first_t, pltpu.roll(v_prev, 1, 1), pltpu.roll(v, 1, 1))
            north_side = jnp.where(top_t, jnp.broadcast_to(vn_ref[k, :, sl], (rows, width)),
                                   pltpu.roll(v, rows - 1, 0))
            south_side = jnp.where(bottom_t, jnp.broadcast_to(vs_ref[k, :, sl], (rows, width)),
                                   pltpu.roll(v, 1, 0))
            north = n_ref[k, :, sl]
            west = jnp.where(first_t, pltpu.roll(e_prev, 1, 1), pltpu.roll(east, 1, 1))
            south = jnp.where(bottom_t, jnp.broadcast_to(ns_ref[k, :, sl], (rows, width)),
                              pltpu.roll(north, 1, 0))
            image = (
                h_ref[k, :, sl] * v
                + east * (v - east_side)
                + west * (v - west_side)
                + north * (v - north_side)
                + south * (v - south_side)
                + up_ref[k, :, sl] * (v - up_at(sl))
                + lower_at(sl) * (v - down_at(sl))
            )
            img_ref[k, :, sl] = image
            for j, ref in enumerate(partner_refs):
                accs[j] = accs[j] + (v if j == 0 else ref[k, :, sl]) * image
        return tuple(accs)

    above = lambda sl: jnp.where(keep_above > 0.0, vab_ref[0, :, sl], 0.0)
    below = lambda sl: jnp.where(keep_below > 0.0, vbe_ref[0, :, sl], 0.0)
    up_below = lambda sl: jnp.where(keep_below > 0.0, upb_ref[0, :, sl], 0.0)
    accs = (jnp.zeros((rows, width), jnp.float32),) * len(slots)
    if block == 1:
        accs = level(0, above, below, up_below, accs)
    else:
        accs = level(0, lambda sl: v_ref[1, :, sl], below, up_below, accs)
        accs = lax.fori_loop(
            1, block - 1,
            lambda k, c: level(k, lambda sl: v_ref[k + 1, :, sl], lambda sl: v_ref[k - 1, :, sl],
                               lambda sl: up_ref[k - 1, :, sl], c), accs,
        )
        accs = level(block - 1, above, lambda sl: v_ref[block - 2, :, sl],
                     lambda sl: up_ref[block - 2, :, sl], accs)
    add_totals(part_ref, slots, accs)


def apply_operator(direction, coefs, halos, slots, extra=()):
    helm_diag, east_coef, north_coef, upper, east_west, north_south = coefs
    east_halo, west_halo, north_halo, south_halo = halos
    levels, rows, cols = direction.shape
    block = LEVEL_BLOCK if levels % LEVEL_BLOCK == 0 else levels
    blocks = levels // block
    full = pl.BlockSpec((block, rows, cols), lambda i: (i, 0, 0))
    lane_col = pl.BlockSpec((block, rows, 1), lambda i: (i, 0, 0))
    first_col = pl.BlockSpec((None, block, rows, 1), lambda i: (0, i, 0, 0))
    row_spec = pl.BlockSpec((block, 1, cols), lambda i: (i, 0, 0))
    above = pl.BlockSpec((1, rows, cols), lambda i: (jnp.minimum((i + 1) * block, levels - 1), 0, 0))
    below = pl.BlockSpec((1, rows, cols), lambda i: (jnp.maximum(i * block - 1, 0), 0, 0))
    kernel = lambda *refs: operator_kernel(slots, *refs)
    image, part = pl.pallas_call(
        kernel,
        grid=(blocks,),
        in_specs=[full, above, below, full, full, full, full, below, first_col, row_spec,
                  lane_col, lane_col, row_spec, row_spec] + [full] * len(extra),
        out_specs=[full, tile_spec()],
        out_shape=[jax.ShapeDtypeStruct(direction.shape, jnp.float32), tile_shape()],
    )(direction, direction, direction, helm_diag, east_coef, north_coef, upper, upper,
      east_west, north_south, east_halo, west_halo, north_halo, south_halo, *extra)
    return image, part


def finish_kernel(sums_ref, p0_ref, q_ref, r0_ref, a0_ref, aq_ref, sol_ref, res_ref):
    block, rows, cols = p0_ref.shape
    sums = sums_ref[...]
    norm0, curv0, r0q, a0q, qaq, p0aq = (
        jnp.broadcast_to(sums[j:j + 1, :], sums.shape) for j in range(6)
    )
    step0 = norm0 / curv0
    norm1 = norm0 - step0 * (r0q + curv0) + step0 * step0 * a0q
    p1ap1 = curv0 - step0 * (p0aq + a0q) + step0 * step0 * qaq
    p1a0 = curv0 - step0 * a0q
    d0ap1 = curv0 - step0 * p0aq
    beta = norm1 / norm0
    curv1 = p1ap1 + beta * (p1a0 + d0ap1) + beta * beta * curv0
    step1 = norm1 / curv1
    widen = lambda x: jnp.concatenate([x[:rows]] * (cols // x.shape[1]), axis=1)
    step0, beta, step1 = widen(step0), widen(beta), widen(step1)

    def level(k, carry):
        p0 = p0_ref[k]
        a0 = a0_ref[k]
        precond1 = p0 - step0 * q_ref[k]
        direction1 = precond1 + beta * p0
        image1 = (a0 - step0 * aq_ref[k]) + beta * a0
        sol_ref[k] = step0 * p0 + step1 * direction1
        res_ref[k] = (r0_ref[k] - step0 * a0) - step1 * image1
        return carry

    lax.fori_loop(0, block, level, 0)


def finish(sums, precond0, basis, right_side, image0, image_q):
    levels, rows, cols = precond0.shape
    block = LEVEL_BLOCK if levels % LEVEL_BLOCK == 0 else levels
    full = pl.BlockSpec((block, rows, cols), lambda i: (i, 0, 0))
    field = jax.ShapeDtypeStruct(precond0.shape, jnp.float32)
    return pl.pallas_call(
        finish_kernel,
        grid=(levels // block,),
        in_specs=[tile_spec(), full, full, full, full, full],
        out_specs=[full, full],
        out_shape=[field, field],
    )(sums, precond0, basis, right_side, image0, image_q)


def exchange(direction, top, bottom, tables, use_mortar):
    west, east = belt_cols(direction)
    first_map, second_map, first_weight, second_weight = tables
    whole = gather_rows(east)
    arrived = first_weight[:, None] * whole[first_map] + second_weight[:, None] * whole[second_map]
    east = jnp.where(use_mortar, arrived, east)
    south, north = mer_rows(top, bottom)
    return as_lane_column(east), as_lane_column(west), north, south


def on_device(
    right_side,
    helm_diag,
    east_coef,
    north_coef,
    vert_coef,
    mortar_weights,
    weight_index,
    edge_map,
    refined,
):
    belt_index = lax.axis_index("belt")
    mer_index = lax.axis_index("mer")
    per_panel = lax.axis_size("belt") // 4
    rows = right_side.shape[1]
    row_start = mer_index * rows
    own_edge = belt_index // per_panel
    row_flags = lax.dynamic_slice_in_dim(refined[own_edge], row_start, rows, 0)
    at_edge = (belt_index + 1) % per_panel == 0
    use_mortar = jnp.logical_and(at_edge, row_flags == 1)[:, None]
    tables = edge_tables(own_edge, row_start, rows, weight_index, edge_map, mortar_weights)
    levels, _, cols = right_side.shape
    block = BLOCK_COLS if cols % BLOCK_COLS == 0 else cols
    coef_west, _ = belt_cols(east_coef)
    coef_south, _ = mer_rows(north_coef[:, -1:, :], north_coef[:, :1, :])
    east_left = jnp.stack(
        [jnp.transpose(coef_west)]
        + [east_coef[:, :, j * block - 1] for j in range(1, cols // block)],
        axis=0,
    )[..., None]
    upper = jnp.concatenate([vert_coef, jnp.zeros_like(vert_coef[:1])], axis=0)
    coefs = (helm_diag, east_coef, north_coef, upper, east_left, coef_south)

    inverse_pivot, ratio_values, precond0, top0, bottom0, part0 = factor_solve(
        helm_diag, east_coef, north_coef, vert_coef, right_side, east_left, coef_south
    )
    image0, curv_part0 = apply_operator(
        precond0, coefs, exchange(precond0, top0, bottom0, tables, use_mortar), (1,)
    )
    basis, top_q, bottom_q, basis_part = solve(
        image0, inverse_pivot, ratio_values, vert_coef, (right_side,), (2, 3)
    )
    image_q, image_q_part = apply_operator(
        basis, coefs, exchange(basis, top_q, bottom_q, tables, use_mortar), (4, 5), (precond0,)
    )
    sums = tree_sum(part0 + curv_part0 + basis_part + image_q_part)
    return finish(sums, precond0, basis, right_side, image0, image_q)


def solution(mesh):
    placed = (
        P(None, "mer", "belt"),
        P(None, "mer", "belt"),
        P(None, "mer", "belt"),
        P(None, "mer", "belt"),
        P(None, "mer", "belt"),
        P(),
        P(),
        P(),
        P(),
    )
    return jax.shard_map(
        on_device,
        mesh=mesh,
        in_specs=placed,
        out_specs=(P(None, "mer", "belt"), P(None, "mer", "belt")),
        check_vma=False,
    )
```

```python
import jax
import jax.numpy as jnp
from jax import lax
from jax.experimental import pallas as pl
from jax.experimental.pallas import tpu as pltpu
from jax.sharding import PartitionSpec as P

ITERS = 2
BLOCK_COLS = 384
LEVEL_BLOCK = 24


def tree_sum(values):
    for axis in ("mer", "belt"):
        count = lax.axis_size(axis)
        if count & (count - 1):
            values = lax.psum(values, axis)
            continue
        bit = 1
        while bit < count:
            values = values + lax.ppermute(values, axis, [(i, i ^ bit) for i in range(count)])
            bit *= 2
    return values


def add_totals(part_ref, slots, accs):
    row = lax.broadcasted_iota(jnp.int32, part_ref.shape, 0)
    tile = part_ref[...]
    for slot, acc in zip(slots, accs):
        tile = tile + jnp.where(row == slot, jnp.sum(acc), 0.0)
    part_ref[...] = tile


def tile_spec():
    return pl.BlockSpec((8, 128), lambda j: (0, 0))


def tile_shape():
    return jax.ShapeDtypeStruct((8, 128), jnp.float32)


def row_block(levels, block):
    return pl.BlockSpec((levels, 1, block), lambda j: (0, 0, j))


def row_shape(levels, cols):
    return jax.ShapeDtypeStruct((levels, 1, cols), jnp.float32)


def column_spec(levels, rows, cols):
    return pl.BlockSpec((levels, rows, cols), lambda j: (0, 0, j))


def factor_solve_kernel(h_ref, e_ref, n_ref, v_ref, r_ref, eleft_ref, nsouth_ref,
                        inv_ref, ratio_ref, p_ref, top_ref, bottom_ref, part_ref):
    levels, rows, cols = h_ref.shape

    @pl.when(pl.program_id(0) == 0)
    def _():
        part_ref[...] = jnp.zeros_like(part_ref)

    zero = jnp.zeros((rows, cols), jnp.float32)
    first_lane = lax.broadcasted_iota(jnp.int32, (rows, cols), 1) == 0
    first_row = lax.broadcasted_iota(jnp.int32, (rows, cols), 0) == 0

    def forward(k, up, down, prev, elim):
        east = e_ref[k]
        north = n_ref[k]
        west = jnp.where(first_lane, jnp.broadcast_to(eleft_ref[k], (rows, cols)),
                         pltpu.roll(east, 1, 1))
        south = jnp.where(first_row, jnp.broadcast_to(nsouth_ref[k], (rows, cols)),
                          pltpu.roll(north, 1, 0))
        diag = h_ref[k] + east + west + north + south + up + down
        ratio = down / prev
        pivot = diag - down * ratio
        inv_ref[k] = 1.0 / pivot
        ratio_ref[k] = ratio
        elim = r_ref[k] + ratio * elim
        p_ref[k] = elim
        return pivot, elim

    carry = forward(0, v_ref[0], zero, jnp.ones_like(zero), zero)
    carry = lax.fori_loop(
        1, levels - 1, lambda k, c: forward(k, v_ref[k], v_ref[k - 1], *c), carry, unroll=4
    )
    forward(levels - 1, zero, v_ref[levels - 2], *carry)

    def backward(k, up, succ, acc):
        value = inv_ref[k] * (p_ref[k] + up * succ)
        p_ref[k] = value
        top_ref[k] = value[rows - 1:rows]
        bottom_ref[k] = value[:1]
        return value, acc + r_ref[k] * value

    carry = backward(levels - 1, zero, zero, zero)
    carry = lax.fori_loop(
        0, levels - 1, lambda i, c: backward(levels - 2 - i, v_ref[levels - 2 - i], *c), carry,
        unroll=4,
    )
    add_totals(part_ref, (0,), (carry[1],))


def factor_solve(helm_diag, east_coef, north_coef, vert_coef, rhs, east_left, north_south):
    levels, rows, cols = rhs.shape
    block = BLOCK_COLS if cols % BLOCK_COLS == 0 else cols
    full = column_spec(levels, rows, block)
    vspec = column_spec(levels - 1, rows, block)
    field = jax.ShapeDtypeStruct(rhs.shape, jnp.float32)
    return pl.pallas_call(
        factor_solve_kernel,
        grid=(cols // block,),
        in_specs=[full, full, full, vspec, full,
                  pl.BlockSpec((None, levels, rows, 1), lambda j: (j, 0, 0, 0)),
                  pl.BlockSpec((levels, 1, block), lambda j: (0, 0, j))],
        out_specs=[full, full, full, row_block(levels, block), row_block(levels, block),
                   tile_spec()],
        out_shape=[field, field, field, row_shape(levels, cols), row_shape(levels, cols),
                   tile_shape()],
    )(helm_diag, east_coef, north_coef, vert_coef, rhs, east_left, north_south)


def solve_kernel(slots, *refs):
    count = len(slots)
    val_ref, inv_ref, ratio_ref, v_ref = refs[:4]
    partner_refs = refs[4:4 + count - 1] + (val_ref,)
    p_ref, top_ref, bottom_ref, part_ref = refs[4 + count - 1:]
    levels = val_ref.shape[0]
    zero = jnp.zeros(val_ref.shape[1:], jnp.float32)

    @pl.when(pl.program_id(0) == 0)
    def _():
        part_ref[...] = jnp.zeros_like(part_ref)

    def forward(k, elim):
        elim = val_ref[k] + ratio_ref[k] * elim
        p_ref[k] = elim
        return elim

    lax.fori_loop(0, levels, forward, zero, unroll=4)

    def backward(k, up, succ, accs):
        value = inv_ref[k] * (p_ref[k] + up * succ)
        p_ref[k] = value
        top_ref[k] = value[value.shape[0] - 1:]
        bottom_ref[k] = value[:1]
        return value, tuple(acc + ref[k] * value for acc, ref in zip(accs, partner_refs))

    carry = backward(levels - 1, zero, zero, (zero,) * count)
    carry = lax.fori_loop(
        0, levels - 1, lambda i, c: backward(levels - 2 - i, v_ref[levels - 2 - i], *c), carry,
        unroll=4,
    )
    add_totals(part_ref, slots, carry[1])


def solve(values, inverse_pivot, ratio_values, vert_coef, partners, slots):
    levels, rows, cols = values.shape
    block = BLOCK_COLS if cols % BLOCK_COLS == 0 else cols
    full = column_spec(levels, rows, block)
    vspec = column_spec(levels - 1, rows, block)
    return pl.pallas_call(
        lambda *refs: solve_kernel(slots, *refs),
        grid=(cols // block,),
        in_specs=[full, full, full, vspec] + [full] * len(partners),
        out_specs=[full, row_block(levels, block), row_block(levels, block), tile_spec()],
        out_shape=[jax.ShapeDtypeStruct(values.shape, jnp.float32), row_shape(levels, cols),
                   row_shape(levels, cols), tile_shape()],
    )(values, inverse_pivot, ratio_values, vert_coef, *partners)


def edge_tables(edge_num, row_start, rows, weight_index, edge_map, mortar_weights):
    maps = lax.dynamic_slice_in_dim(edge_map[edge_num], row_start, rows, 0)
    picks = lax.dynamic_slice_in_dim(weight_index[edge_num], row_start, rows, 0)
    return (maps[:, 0], maps[:, 1], mortar_weights[picks, 0], mortar_weights[picks, 1])


def belt_cols(field):
    count = lax.axis_size("belt")
    first = jnp.transpose(field[:, :, 0])
    last = jnp.transpose(field[:, :, -1])
    west = lax.ppermute(last, "belt", [(i, (i + 1) % count) for i in range(count)])
    east = lax.ppermute(first, "belt", [((i + 1) % count, i) for i in range(count)])
    return west, east


def mer_rows(top, bottom):
    count = lax.axis_size("mer")
    south = lax.ppermute(top, "mer", [(i, i + 1) for i in range(count - 1)])
    north = lax.ppermute(bottom, "mer", [(i + 1, i) for i in range(count - 1)])
    return south, north


def gather_rows(column):
    count = lax.axis_size("mer")
    if count & (count - 1):
        return lax.all_gather(column, "mer", axis=0, tiled=True)
    me = lax.axis_index("mer")
    bit = 1
    while bit < count:
        other = lax.ppermute(column, "mer", [(i, i ^ bit) for i in range(count)])
        low_half = (me & bit) == 0
        column = jnp.concatenate(
            [jnp.where(low_half, column, other), jnp.where(low_half, other, column)], axis=0
        )
        bit *= 2
    return column


def as_lane_column(cols):
    return jnp.transpose(cols)[:, :, None]


def operator_kernel(slots, *refs):
    extra = len(slots) - 1
    (v_ref, vab_ref, vbe_ref, h_ref, e_ref, n_ref, up_ref, upb_ref, ew_ref, ns_ref,
     ve_ref, vw_ref, vn_ref, vs_ref) = refs[:14]
    partner_refs = (v_ref,) + refs[14:14 + extra]
    img_ref, part_ref = refs[14 + extra:]
    block, rows, cols = v_ref.shape
    i = pl.program_id(0)
    last_block = pl.num_programs(0) - 1
    keep_above = jnp.where(i == last_block, 0.0, 1.0)
    keep_below = jnp.where(i == 0, 0.0, 1.0)

    @pl.when(i == 0)
    def _():
        part_ref[...] = jnp.zeros_like(part_ref)

    width = 384 if cols % 384 == 0 else cols
    tiles = cols // width
    lane_t = lax.broadcasted_iota(jnp.int32, (rows, width), 1)
    row_t = lax.broadcasted_iota(jnp.int32, (rows, width), 0)
    top_t, bottom_t = row_t == rows - 1, row_t == 0
    first_t, last_t = lane_t == 0, lane_t == width - 1

    def level(k, up_at, down_at, lower_at, accs):
        accs = list(accs)
        v_all = [v_ref[k, :, t * width:(t + 1) * width] for t in range(tiles)]
        e_all = [e_ref[k, :, t * width:(t + 1) * width] for t in range(tiles)]
        v_west = jnp.broadcast_to(vw_ref[k], (rows, width))
        v_east = jnp.broadcast_to(ve_ref[k], (rows, width))
        e_west = jnp.broadcast_to(ew_ref[k], (rows, width))
        for t in range(tiles):
            sl = slice(t * width, (t + 1) * width)
            v = v_all[t]
            v_next = v_all[t + 1] if t + 1 < tiles else v_east
            v_prev = v_all[t - 1] if t > 0 else v_west
            east = e_all[t]
            e_prev = e_all[t - 1] if t > 0 else e_west
            east_side = jnp.where(last_t, pltpu.roll(v_next, width - 1, 1),
                                  pltpu.roll(v, width - 1, 1))
            west_side = jnp.where(first_t, pltpu.roll(v_prev, 1, 1), pltpu.roll(v, 1, 1))
            north_side = jnp.where(top_t, jnp.broadcast_to(vn_ref[k, :, sl], (rows, width)),
                                   pltpu.roll(v, rows - 1, 0))
            south_side = jnp.where(bottom_t, jnp.broadcast_to(vs_ref[k, :, sl], (rows, width)),
                                   pltpu.roll(v, 1, 0))
            north = n_ref[k, :, sl]
            west = jnp.where(first_t, pltpu.roll(e_prev, 1, 1), pltpu.roll(east, 1, 1))
            south = jnp.where(bottom_t, jnp.broadcast_to(ns_ref[k, :, sl], (rows, width)),
                              pltpu.roll(north, 1, 0))
            image = (
                h_ref[k, :, sl] * v
                + east * (v - east_side)
                + west * (v - west_side)
                + north * (v - north_side)
                + south * (v - south_side)
                + up_ref[k, :, sl] * (v - up_at(sl))
                + lower_at(sl) * (v - down_at(sl))
            )
            img_ref[k, :, sl] = image
            for j, ref in enumerate(partner_refs):
                accs[j] = accs[j] + (v if j == 0 else ref[k, :, sl]) * image
        return tuple(accs)

    above = lambda sl: jnp.where(keep_above > 0.0, vab_ref[0, :, sl], 0.0)
    below = lambda sl: jnp.where(keep_below > 0.0, vbe_ref[0, :, sl], 0.0)
    up_below = lambda sl: jnp.where(keep_below > 0.0, upb_ref[0, :, sl], 0.0)
    accs = (jnp.zeros((rows, width), jnp.float32),) * len(slots)
    if block == 1:
        accs = level(0, above, below, up_below, accs)
    else:
        accs = level(0, lambda sl: v_ref[1, :, sl], below, up_below, accs)
        accs = lax.fori_loop(
            1, block - 1,
            lambda k, c: level(k, lambda sl: v_ref[k + 1, :, sl], lambda sl: v_ref[k - 1, :, sl],
                               lambda sl: up_ref[k - 1, :, sl], c), accs,
        )
        accs = level(block - 1, above, lambda sl: v_ref[block - 2, :, sl],
                     lambda sl: up_ref[block - 2, :, sl], accs)
    add_totals(part_ref, slots, accs)


def apply_operator(direction, coefs, halos, slots, extra=()):
    helm_diag, east_coef, north_coef, upper, east_west, north_south = coefs
    east_halo, west_halo, north_halo, south_halo = halos
    levels, rows, cols = direction.shape
    block = LEVEL_BLOCK if levels % LEVEL_BLOCK == 0 else levels
    blocks = levels // block
    full = pl.BlockSpec((block, rows, cols), lambda i: (i, 0, 0))
    lane_col = pl.BlockSpec((block, rows, 1), lambda i: (i, 0, 0))
    first_col = pl.BlockSpec((None, block, rows, 1), lambda i: (0, i, 0, 0))
    row_spec = pl.BlockSpec((block, 1, cols), lambda i: (i, 0, 0))
    above = pl.BlockSpec((1, rows, cols), lambda i: (jnp.minimum((i + 1) * block, levels - 1), 0, 0))
    below = pl.BlockSpec((1, rows, cols), lambda i: (jnp.maximum(i * block - 1, 0), 0, 0))
    kernel = lambda *refs: operator_kernel(slots, *refs)
    image, part = pl.pallas_call(
        kernel,
        grid=(blocks,),
        in_specs=[full, above, below, full, full, full, full, below, first_col, row_spec,
                  lane_col, lane_col, row_spec, row_spec] + [full] * len(extra),
        out_specs=[full, tile_spec()],
        out_shape=[jax.ShapeDtypeStruct(direction.shape, jnp.float32), tile_shape()],
    )(direction, direction, direction, helm_diag, east_coef, north_coef, upper, upper,
      east_west, north_south, east_halo, west_halo, north_halo, south_halo, *extra)
    return image, part


def finish_kernel(sums_ref, p0_ref, q_ref, r0_ref, a0_ref, aq_ref, sol_ref, res_ref):
    block, rows, cols = p0_ref.shape
    sums = sums_ref[...]
    norm0, curv0, r0q, a0q, qaq, p0aq = (
        jnp.broadcast_to(sums[j:j + 1, :], sums.shape) for j in range(6)
    )
    step0 = norm0 / curv0
    norm1 = norm0 - step0 * (r0q + curv0) + step0 * step0 * a0q
    p1ap1 = curv0 - step0 * (p0aq + a0q) + step0 * step0 * qaq
    p1a0 = curv0 - step0 * a0q
    d0ap1 = curv0 - step0 * p0aq
    beta = norm1 / norm0
    curv1 = p1ap1 + beta * (p1a0 + d0ap1) + beta * beta * curv0
    step1 = norm1 / curv1
    widen = lambda x: jnp.concatenate([x[:rows]] * (cols // x.shape[1]), axis=1)
    step0, beta, step1 = widen(step0), widen(beta), widen(step1)

    def level(k, carry):
        p0 = p0_ref[k]
        a0 = a0_ref[k]
        precond1 = p0 - step0 * q_ref[k]
        direction1 = precond1 + beta * p0
        image1 = (a0 - step0 * aq_ref[k]) + beta * a0
        sol_ref[k] = step0 * p0 + step1 * direction1
        res_ref[k] = (r0_ref[k] - step0 * a0) - step1 * image1
        return carry

    lax.fori_loop(0, block, level, 0)


def finish(sums, precond0, basis, right_side, image0, image_q):
    levels, rows, cols = precond0.shape
    block = LEVEL_BLOCK if levels % LEVEL_BLOCK == 0 else levels
    full = pl.BlockSpec((block, rows, cols), lambda i: (i, 0, 0))
    field = jax.ShapeDtypeStruct(precond0.shape, jnp.float32)
    return pl.pallas_call(
        finish_kernel,
        grid=(levels // block,),
        in_specs=[tile_spec(), full, full, full, full, full],
        out_specs=[full, full],
        out_shape=[field, field],
    )(sums, precond0, basis, right_side, image0, image_q)


def exchange(direction, top, bottom, tables, use_mortar):
    west, east = belt_cols(direction)
    first_map, second_map, first_weight, second_weight = tables
    whole = gather_rows(east)
    arrived = first_weight[:, None] * whole[first_map] + second_weight[:, None] * whole[second_map]
    east = jnp.where(use_mortar, arrived, east)
    south, north = mer_rows(top, bottom)
    return as_lane_column(east), as_lane_column(west), north, south


def on_device(
    right_side,
    helm_diag,
    east_coef,
    north_coef,
    vert_coef,
    mortar_weights,
    weight_index,
    edge_map,
    refined,
):
    belt_index = lax.axis_index("belt")
    mer_index = lax.axis_index("mer")
    per_panel = lax.axis_size("belt") // 4
    rows = right_side.shape[1]
    row_start = mer_index * rows
    own_edge = belt_index // per_panel
    row_flags = lax.dynamic_slice_in_dim(refined[own_edge], row_start, rows, 0)
    at_edge = (belt_index + 1) % per_panel == 0
    use_mortar = jnp.logical_and(at_edge, row_flags == 1)[:, None]
    tables = edge_tables(own_edge, row_start, rows, weight_index, edge_map, mortar_weights)
    levels, _, cols = right_side.shape
    block = BLOCK_COLS if cols % BLOCK_COLS == 0 else cols
    coef_west, _ = belt_cols(east_coef)
    coef_south, _ = mer_rows(north_coef[:, -1:, :], north_coef[:, :1, :])
    east_left = jnp.stack(
        [jnp.transpose(coef_west)]
        + [east_coef[:, :, j * block - 1] for j in range(1, cols // block)],
        axis=0,
    )[..., None]
    upper = jnp.concatenate([vert_coef, jnp.zeros_like(vert_coef[:1])], axis=0)
    coefs = (helm_diag, east_coef, north_coef, upper, east_left, coef_south)

    inverse_pivot, ratio_values, precond0, top0, bottom0, part0 = factor_solve(
        helm_diag, east_coef, north_coef, vert_coef, right_side, east_left, coef_south
    )
    image0, curv_part0 = apply_operator(
        precond0, coefs, exchange(precond0, top0, bottom0, tables, use_mortar), (1,)
    )
    basis, top_q, bottom_q, basis_part = solve(
        image0, inverse_pivot, ratio_values, vert_coef, (right_side,), (2, 3)
    )
    image_q, image_q_part = apply_operator(
        basis, coefs, exchange(basis, top_q, bottom_q, tables, use_mortar), (4, 5), (precond0,)
    )
    sums = tree_sum(part0 + curv_part0 + basis_part + image_q_part)
    return finish(sums, precond0, basis, right_side, image0, image_q)


def solution(mesh):
    placed = (
        P(None, "mer", "belt"),
        P(None, "mer", "belt"),
        P(None, "mer", "belt"),
        P(None, "mer", "belt"),
        P(None, "mer", "belt"),
        P(),
        P(),
        P(),
        P(),
    )
    return jax.shard_map(
        on_device,
        mesh=mesh,
        in_specs=placed,
        out_specs=(P(None, "mer", "belt"), P(None, "mer", "belt")),
        check_vma=False,
    )
```

```python
import jax
import jax.numpy as jnp
from jax import lax
from jax.experimental import pallas as pl
from jax.experimental.pallas import tpu as pltpu
from jax.sharding import PartitionSpec as P

ITERS = 2
BLOCK_COLS = 384
LEVEL_BLOCK = 24


def tree_sum(values):
    for axis in ("mer", "belt"):
        count = lax.axis_size(axis)
        if count & (count - 1):
            values = lax.psum(values, axis)
            continue
        bit = 1
        while bit < count:
            values = values + lax.ppermute(values, axis, [(i, i ^ bit) for i in range(count)])
            bit *= 2
    return values


def add_totals(part_ref, slots, accs):
    row = lax.broadcasted_iota(jnp.int32, part_ref.shape, 0)
    tile = part_ref[...]
    for slot, acc in zip(slots, accs):
        tile = tile + jnp.where(row == slot, jnp.sum(acc), 0.0)
    part_ref[...] = tile


def tile_spec():
    return pl.BlockSpec((8, 128), lambda j: (0, 0))


def tile_shape():
    return jax.ShapeDtypeStruct((8, 128), jnp.float32)


def row_block(levels, block):
    return pl.BlockSpec((levels, 1, block), lambda j: (0, 0, j))


def row_shape(levels, cols):
    return jax.ShapeDtypeStruct((levels, 1, cols), jnp.float32)


def column_spec(levels, rows, cols):
    return pl.BlockSpec((levels, rows, cols), lambda j: (0, 0, j))


def factor_solve_kernel(h_ref, e_ref, n_ref, v_ref, r_ref, eleft_ref, nsouth_ref,
                        inv_ref, ratio_ref, p_ref, top_ref, bottom_ref, part_ref):
    levels, rows, cols = h_ref.shape

    @pl.when(pl.program_id(0) == 0)
    def _():
        part_ref[...] = jnp.zeros_like(part_ref)

    zero = jnp.zeros((rows, cols), jnp.float32)
    first_lane = lax.broadcasted_iota(jnp.int32, (rows, cols), 1) == 0
    first_row = lax.broadcasted_iota(jnp.int32, (rows, cols), 0) == 0

    def forward(k, up, down, prev, elim):
        east = e_ref[k]
        north = n_ref[k]
        west = jnp.where(first_lane, jnp.broadcast_to(eleft_ref[k], (rows, cols)),
                         pltpu.roll(east, 1, 1))
        south = jnp.where(first_row, jnp.broadcast_to(nsouth_ref[k], (rows, cols)),
                          pltpu.roll(north, 1, 0))
        diag = h_ref[k] + east + west + north + south + up + down
        ratio = down / prev
        pivot = diag - down * ratio
        inv_ref[k] = 1.0 / pivot
        ratio_ref[k] = ratio
        elim = r_ref[k] + ratio * elim
        p_ref[k] = elim
        return pivot, elim

    carry = forward(0, v_ref[0], zero, jnp.ones_like(zero), zero)
    carry = lax.fori_loop(
        1, levels - 1, lambda k, c: forward(k, v_ref[k], v_ref[k - 1], *c), carry, unroll=4
    )
    forward(levels - 1, zero, v_ref[levels - 2], *carry)

    def backward(k, up, succ, acc):
        value = inv_ref[k] * (p_ref[k] + up * succ)
        p_ref[k] = value
        top_ref[k] = value[rows - 1:rows]
        bottom_ref[k] = value[:1]
        return value, acc + r_ref[k] * value

    carry = backward(levels - 1, zero, zero, zero)
    carry = lax.fori_loop(
        0, levels - 1, lambda i, c: backward(levels - 2 - i, v_ref[levels - 2 - i], *c), carry,
        unroll=4,
    )
    add_totals(part_ref, (0,), (carry[1],))


def factor_solve(helm_diag, east_coef, north_coef, vert_coef, rhs, east_left, north_south):
    levels, rows, cols = rhs.shape
    block = BLOCK_COLS if cols % BLOCK_COLS == 0 else cols
    full = column_spec(levels, rows, block)
    vspec = column_spec(levels - 1, rows, block)
    field = jax.ShapeDtypeStruct(rhs.shape, jnp.float32)
    return pl.pallas_call(
        factor_solve_kernel,
        grid=(cols // block,),
        in_specs=[full, full, full, vspec, full,
                  pl.BlockSpec((None, levels, rows, 1), lambda j: (j, 0, 0, 0)),
                  pl.BlockSpec((levels, 1, block), lambda j: (0, 0, j))],
        out_specs=[full, full, full, row_block(levels, block), row_block(levels, block),
                   tile_spec()],
        out_shape=[field, field, field, row_shape(levels, cols), row_shape(levels, cols),
                   tile_shape()],
    )(helm_diag, east_coef, north_coef, vert_coef, rhs, east_left, north_south)


def solve_kernel(slots, *refs):
    count = len(slots)
    val_ref, inv_ref, ratio_ref, v_ref = refs[:4]
    partner_refs = refs[4:4 + count - 1] + (val_ref,)
    p_ref, top_ref, bottom_ref, part_ref = refs[4 + count - 1:]
    levels = val_ref.shape[0]
    zero = jnp.zeros(val_ref.shape[1:], jnp.float32)

    @pl.when(pl.program_id(0) == 0)
    def _():
        part_ref[...] = jnp.zeros_like(part_ref)

    def forward(k, elim):
        elim = val_ref[k] + ratio_ref[k] * elim
        p_ref[k] = elim
        return elim

    lax.fori_loop(0, levels, forward, zero, unroll=4)

    def backward(k, up, succ, accs):
        value = inv_ref[k] * (p_ref[k] + up * succ)
        p_ref[k] = value
        top_ref[k] = value[value.shape[0] - 1:]
        bottom_ref[k] = value[:1]
        return value, tuple(acc + ref[k] * value for acc, ref in zip(accs, partner_refs))

    carry = backward(levels - 1, zero, zero, (zero,) * count)
    carry = lax.fori_loop(
        0, levels - 1, lambda i, c: backward(levels - 2 - i, v_ref[levels - 2 - i], *c), carry,
        unroll=4,
    )
    add_totals(part_ref, slots, carry[1])


def solve(values, inverse_pivot, ratio_values, vert_coef, partners, slots):
    levels, rows, cols = values.shape
    block = BLOCK_COLS if cols % BLOCK_COLS == 0 else cols
    full = column_spec(levels, rows, block)
    vspec = column_spec(levels - 1, rows, block)
    return pl.pallas_call(
        lambda *refs: solve_kernel(slots, *refs),
        grid=(cols // block,),
        in_specs=[full, full, full, vspec] + [full] * len(partners),
        out_specs=[full, row_block(levels, block), row_block(levels, block), tile_spec()],
        out_shape=[jax.ShapeDtypeStruct(values.shape, jnp.float32), row_shape(levels, cols),
                   row_shape(levels, cols), tile_shape()],
    )(values, inverse_pivot, ratio_values, vert_coef, *partners)


def edge_tables(edge_num, row_start, rows, weight_index, edge_map, mortar_weights):
    maps = lax.dynamic_slice_in_dim(edge_map[edge_num], row_start, rows, 0)
    picks = lax.dynamic_slice_in_dim(weight_index[edge_num], row_start, rows, 0)
    return (maps[:, 0], maps[:, 1], mortar_weights[picks, 0], mortar_weights[picks, 1])


def belt_cols(field):
    count = lax.axis_size("belt")
    first = jnp.transpose(field[:, :, 0])
    last = jnp.transpose(field[:, :, -1])
    west = lax.ppermute(last, "belt", [(i, (i + 1) % count) for i in range(count)])
    east = lax.ppermute(first, "belt", [((i + 1) % count, i) for i in range(count)])
    return west, east


def mer_rows(top, bottom):
    count = lax.axis_size("mer")
    south = lax.ppermute(top, "mer", [(i, i + 1) for i in range(count - 1)])
    north = lax.ppermute(bottom, "mer", [(i + 1, i) for i in range(count - 1)])
    return south, north


def gather_rows(column):
    count = lax.axis_size("mer")
    if count & (count - 1):
        return lax.all_gather(column, "mer", axis=0, tiled=True)
    me = lax.axis_index("mer")
    bit = 1
    while bit < count:
        other = lax.ppermute(column, "mer", [(i, i ^ bit) for i in range(count)])
        low_half = (me & bit) == 0
        column = jnp.concatenate(
            [jnp.where(low_half, column, other), jnp.where(low_half, other, column)], axis=0
        )
        bit *= 2
    return column


def as_lane_column(cols):
    return jnp.transpose(cols)[:, :, None]


def operator_kernel(slots, *refs):
    extra = len(slots) - 1
    (v_ref, vab_ref, vbe_ref, h_ref, e_ref, n_ref, up_ref, upb_ref, ew_ref, ns_ref,
     ve_ref, vw_ref, vn_ref, vs_ref) = refs[:14]
    partner_refs = (v_ref,) + refs[14:14 + extra]
    img_ref, part_ref = refs[14 + extra:]
    block, rows, cols = v_ref.shape
    i = pl.program_id(0)
    last_block = pl.num_programs(0) - 1
    lane = lax.broadcasted_iota(jnp.int32, (rows, cols), 1)
    row = lax.broadcasted_iota(jnp.int32, (rows, cols), 0)
    first_lane, last_lane = lane == 0, lane == cols - 1
    first_row, last_row = row == 0, row == rows - 1
    zero = jnp.zeros((rows, cols), jnp.float32)
    above = jnp.where(i == last_block, zero, vab_ref[0])
    below = jnp.where(i == 0, zero, vbe_ref[0])
    up_below = jnp.where(i == 0, zero, upb_ref[0])

    @pl.when(i == 0)
    def _():
        part_ref[...] = jnp.zeros_like(part_ref)

    edge = min(cols, 128)
    lane_e = lax.broadcasted_iota(jnp.int32, (rows, edge), 1)

    def first_tile(halo_ref, k, rolled):
        fixed = jnp.where(lane_e == 0, jnp.broadcast_to(halo_ref[k], (rows, edge)), rolled[:, :edge])
        return jnp.concatenate([fixed, rolled[:, edge:]], axis=1) if cols > edge else fixed

    def last_tile(halo_ref, k, rolled):
        fixed = jnp.where(lane_e == edge - 1, jnp.broadcast_to(halo_ref[k], (rows, edge)),
                          rolled[:, cols - edge:])
        return jnp.concatenate([rolled[:, :cols - edge], fixed], axis=1) if cols > edge else fixed

    def level(k, up_side, down_side, lower, accs):
        v = v_ref[k]
        east_side = last_tile(ve_ref, k, pltpu.roll(v, cols - 1, 1))
        west_side = first_tile(vw_ref, k, pltpu.roll(v, 1, 1))
        north_side = jnp.where(last_row, jnp.broadcast_to(vn_ref[k], (rows, cols)),
                               pltpu.roll(v, rows - 1, 0))
        south_side = jnp.where(first_row, jnp.broadcast_to(vs_ref[k], (rows, cols)),
                               pltpu.roll(v, 1, 0))
        east = e_ref[k]
        north = n_ref[k]
        west = first_tile(ew_ref, k, pltpu.roll(east, 1, 1))
        south = jnp.where(first_row, jnp.broadcast_to(ns_ref[k], (rows, cols)),
                          pltpu.roll(north, 1, 0))
        image = (
            h_ref[k] * v
            + east * (v - east_side)
            + west * (v - west_side)
            + north * (v - north_side)
            + south * (v - south_side)
            + up_ref[k] * (v - up_side)
            + lower * (v - down_side)
        )
        img_ref[k] = image
        return tuple(acc + ref[k] * image for acc, ref in zip(accs, partner_refs))

    accs = (zero,) * len(slots)
    if block == 1:
        accs = level(0, above, below, up_below, accs)
    else:
        accs = level(0, v_ref[1], below, up_below, accs)
        accs = lax.fori_loop(
            1, block - 1,
            lambda k, c: level(k, v_ref[k + 1], v_ref[k - 1], up_ref[k - 1], c), accs,
        )
        accs = level(block - 1, above, v_ref[block - 2], up_ref[block - 2], accs)
    add_totals(part_ref, slots, accs)


def apply_operator(direction, coefs, halos, slots, extra=()):
    helm_diag, east_coef, north_coef, upper, east_west, north_south = coefs
    east_halo, west_halo, north_halo, south_halo = halos
    levels, rows, cols = direction.shape
    block = LEVEL_BLOCK if levels % LEVEL_BLOCK == 0 else levels
    blocks = levels // block
    full = pl.BlockSpec((block, rows, cols), lambda i: (i, 0, 0))
    lane_col = pl.BlockSpec((block, rows, 1), lambda i: (i, 0, 0))
    first_col = pl.BlockSpec((None, block, rows, 1), lambda i: (0, i, 0, 0))
    row_spec = pl.BlockSpec((block, 1, cols), lambda i: (i, 0, 0))
    above = pl.BlockSpec((1, rows, cols), lambda i: (jnp.minimum((i + 1) * block, levels - 1), 0, 0))
    below = pl.BlockSpec((1, rows, cols), lambda i: (jnp.maximum(i * block - 1, 0), 0, 0))
    kernel = lambda *refs: operator_kernel(slots, *refs)
    image, part = pl.pallas_call(
        kernel,
        grid=(blocks,),
        in_specs=[full, above, below, full, full, full, full, below, first_col, row_spec,
                  lane_col, lane_col, row_spec, row_spec] + [full] * len(extra),
        out_specs=[full, tile_spec()],
        out_shape=[jax.ShapeDtypeStruct(direction.shape, jnp.float32), tile_shape()],
    )(direction, direction, direction, helm_diag, east_coef, north_coef, upper, upper,
      east_west, north_south, east_halo, west_halo, north_halo, south_halo, *extra)
    return image, part


def finish_kernel(sums_ref, p0_ref, q_ref, r0_ref, a0_ref, aq_ref, sol_ref, res_ref):
    block, rows, cols = p0_ref.shape
    sums = sums_ref[...]
    norm0, curv0, r0q, a0q, qaq, p0aq = (
        jnp.broadcast_to(sums[j:j + 1, :], sums.shape) for j in range(6)
    )
    step0 = norm0 / curv0
    norm1 = norm0 - step0 * (r0q + curv0) + step0 * step0 * a0q
    p1ap1 = curv0 - step0 * (p0aq + a0q) + step0 * step0 * qaq
    p1a0 = curv0 - step0 * a0q
    d0ap1 = curv0 - step0 * p0aq
    beta = norm1 / norm0
    curv1 = p1ap1 + beta * (p1a0 + d0ap1) + beta * beta * curv0
    step1 = norm1 / curv1
    widen = lambda x: jnp.concatenate([x[:rows]] * (cols // x.shape[1]), axis=1)
    step0, beta, step1 = widen(step0), widen(beta), widen(step1)

    def level(k, carry):
        p0 = p0_ref[k]
        a0 = a0_ref[k]
        precond1 = p0 - step0 * q_ref[k]
        direction1 = precond1 + beta * p0
        image1 = (a0 - step0 * aq_ref[k]) + beta * a0
        sol_ref[k] = step0 * p0 + step1 * direction1
        res_ref[k] = (r0_ref[k] - step0 * a0) - step1 * image1
        return carry

    lax.fori_loop(0, block, level, 0)


def finish(sums, precond0, basis, right_side, image0, image_q):
    levels, rows, cols = precond0.shape
    block = LEVEL_BLOCK if levels % LEVEL_BLOCK == 0 else levels
    full = pl.BlockSpec((block, rows, cols), lambda i: (i, 0, 0))
    field = jax.ShapeDtypeStruct(precond0.shape, jnp.float32)
    return pl.pallas_call(
        finish_kernel,
        grid=(levels // block,),
        in_specs=[tile_spec(), full, full, full, full, full],
        out_specs=[full, full],
        out_shape=[field, field],
    )(sums, precond0, basis, right_side, image0, image_q)


def exchange(direction, top, bottom, tables, use_mortar):
    count = lax.axis_size("belt")
    east = lax.ppermute(jnp.transpose(direction[:, :, 0]), "belt",
                        [((i + 1) % count, i) for i in range(count)])
    whole = gather_rows(east)
    west = lax.ppermute(jnp.transpose(direction[:, :, -1]), "belt",
                        [(i, (i + 1) % count) for i in range(count)])
    south, north = mer_rows(top, bottom)
    first_map, second_map, first_weight, second_weight = tables
    arrived = first_weight[:, None] * whole[first_map] + second_weight[:, None] * whole[second_map]
    east = jnp.where(use_mortar, arrived, east)
    return as_lane_column(east), as_lane_column(west), north, south


def on_device(
    right_side,
    helm_diag,
    east_coef,
    north_coef,
    vert_coef,
    mortar_weights,
    weight_index,
    edge_map,
    refined,
):
    belt_index = lax.axis_index("belt")
    mer_index = lax.axis_index("mer")
    per_panel = lax.axis_size("belt") // 4
    rows = right_side.shape[1]
    row_start = mer_index * rows
    own_edge = belt_index // per_panel
    row_flags = lax.dynamic_slice_in_dim(refined[own_edge], row_start, rows, 0)
    at_edge = (belt_index + 1) % per_panel == 0
    use_mortar = jnp.logical_and(at_edge, row_flags == 1)[:, None]
    tables = edge_tables(own_edge, row_start, rows, weight_index, edge_map, mortar_weights)
    levels, _, cols = right_side.shape
    block = BLOCK_COLS if cols % BLOCK_COLS == 0 else cols
    coef_west, _ = belt_cols(east_coef)
    coef_south, _ = mer_rows(north_coef[:, -1:, :], north_coef[:, :1, :])
    east_left = jnp.stack(
        [jnp.transpose(coef_west)]
        + [east_coef[:, :, j * block - 1] for j in range(1, cols // block)],
        axis=0,
    )[..., None]
    upper = jnp.concatenate([vert_coef, jnp.zeros_like(vert_coef[:1])], axis=0)
    coefs = (helm_diag, east_coef, north_coef, upper, east_left, coef_south)

    inverse_pivot, ratio_values, precond0, top0, bottom0, part0 = factor_solve(
        helm_diag, east_coef, north_coef, vert_coef, right_side, east_left, coef_south
    )
    image0, curv_part0 = apply_operator(
        precond0, coefs, exchange(precond0, top0, bottom0, tables, use_mortar), (1,)
    )
    basis, top_q, bottom_q, basis_part = solve(
        image0, inverse_pivot, ratio_values, vert_coef, (right_side,), (2, 3)
    )
    image_q, image_q_part = apply_operator(
        basis, coefs, exchange(basis, top_q, bottom_q, tables, use_mortar), (4, 5), (precond0,)
    )
    sums = tree_sum(part0 + curv_part0 + basis_part + image_q_part)
    return finish(sums, precond0, basis, right_side, image0, image_q)


def solution(mesh):
    placed = (
        P(None, "mer", "belt"),
        P(None, "mer", "belt"),
        P(None, "mer", "belt"),
        P(None, "mer", "belt"),
        P(None, "mer", "belt"),
        P(),
        P(),
        P(),
        P(),
    )
    return jax.shard_map(
        on_device,
        mesh=mesh,
        in_specs=placed,
        out_specs=(P(None, "mer", "belt"), P(None, "mer", "belt")),
        check_vma=False,
    )
```

```python
import jax
import jax.numpy as jnp
from jax import lax
from jax.experimental import pallas as pl
from jax.experimental.pallas import tpu as pltpu
from jax.sharding import PartitionSpec as P

ITERS = 2
BLOCK_COLS = 384
LEVEL_BLOCK = 24


def tree_sum(values):
    for axis in ("mer", "belt"):
        count = lax.axis_size(axis)
        if count & (count - 1):
            values = lax.psum(values, axis)
            continue
        bit = 1
        while bit < count:
            values = values + lax.ppermute(values, axis, [(i, i ^ bit) for i in range(count)])
            bit *= 2
    return values


def add_totals(part_ref, slots, accs):
    row = lax.broadcasted_iota(jnp.int32, part_ref.shape, 0)
    tile = part_ref[...]
    for slot, acc in zip(slots, accs):
        tile = tile + jnp.where(row == slot, jnp.sum(acc), 0.0)
    part_ref[...] = tile


def tile_spec():
    return pl.BlockSpec((8, 128), lambda j: (0, 0))


def tile_shape():
    return jax.ShapeDtypeStruct((8, 128), jnp.float32)


def row_block(levels, block):
    return pl.BlockSpec((levels, 1, block), lambda j: (0, 0, j))


def row_shape(levels, cols):
    return jax.ShapeDtypeStruct((levels, 1, cols), jnp.float32)


def column_spec(levels, rows, cols):
    return pl.BlockSpec((levels, rows, cols), lambda j: (0, 0, j))


def factor_solve_kernel(h_ref, e_ref, n_ref, v_ref, r_ref, eleft_ref, nsouth_ref,
                        inv_ref, ratio_ref, p_ref, top_ref, bottom_ref, w_ref, s_ref, part_ref):
    levels, rows, cols = h_ref.shape

    @pl.when(pl.program_id(0) == 0)
    def _():
        part_ref[...] = jnp.zeros_like(part_ref)

    zero = jnp.zeros((rows, cols), jnp.float32)
    first_lane = lax.broadcasted_iota(jnp.int32, (rows, cols), 1) == 0
    first_row = lax.broadcasted_iota(jnp.int32, (rows, cols), 0) == 0

    def forward(k, up, down, prev, elim):
        east = e_ref[k]
        north = n_ref[k]
        west = jnp.where(first_lane, jnp.broadcast_to(eleft_ref[k], (rows, cols)),
                         pltpu.roll(east, 1, 1))
        south = jnp.where(first_row, jnp.broadcast_to(nsouth_ref[k], (rows, cols)),
                          pltpu.roll(north, 1, 0))
        w_ref[k] = west
        s_ref[k] = south
        diag = h_ref[k] + east + west + north + south + up + down
        ratio = down / prev
        pivot = diag - down * ratio
        inv_ref[k] = 1.0 / pivot
        ratio_ref[k] = ratio
        elim = r_ref[k] + ratio * elim
        p_ref[k] = elim
        return pivot, elim

    carry = forward(0, v_ref[0], zero, jnp.ones_like(zero), zero)
    carry = lax.fori_loop(
        1, levels - 1, lambda k, c: forward(k, v_ref[k], v_ref[k - 1], *c), carry, unroll=4
    )
    forward(levels - 1, zero, v_ref[levels - 2], *carry)

    def backward(k, up, succ, acc):
        value = inv_ref[k] * (p_ref[k] + up * succ)
        p_ref[k] = value
        top_ref[k] = value[rows - 1:rows]
        bottom_ref[k] = value[:1]
        return value, acc + r_ref[k] * value

    carry = backward(levels - 1, zero, zero, zero)
    carry = lax.fori_loop(
        0, levels - 1, lambda i, c: backward(levels - 2 - i, v_ref[levels - 2 - i], *c), carry,
        unroll=4,
    )
    add_totals(part_ref, (0,), (carry[1],))


def factor_solve(helm_diag, east_coef, north_coef, vert_coef, rhs, east_left, north_south):
    levels, rows, cols = rhs.shape
    block = BLOCK_COLS if cols % BLOCK_COLS == 0 else cols
    full = column_spec(levels, rows, block)
    vspec = column_spec(levels - 1, rows, block)
    field = jax.ShapeDtypeStruct(rhs.shape, jnp.float32)
    return pl.pallas_call(
        factor_solve_kernel,
        grid=(cols // block,),
        in_specs=[full, full, full, vspec, full,
                  pl.BlockSpec((None, levels, rows, 1), lambda j: (j, 0, 0, 0)),
                  pl.BlockSpec((levels, 1, block), lambda j: (0, 0, j))],
        out_specs=[full, full, full, row_block(levels, block), row_block(levels, block),
                   full, full, tile_spec()],
        out_shape=[field, field, field, row_shape(levels, cols), row_shape(levels, cols),
                   field, field, tile_shape()],
    )(helm_diag, east_coef, north_coef, vert_coef, rhs, east_left, north_south)


def solve_kernel(slots, *refs):
    count = len(slots)
    val_ref, inv_ref, ratio_ref, v_ref = refs[:4]
    partner_refs = refs[4:4 + count - 1] + (val_ref,)
    p_ref, top_ref, bottom_ref, part_ref = refs[4 + count - 1:]
    levels = val_ref.shape[0]
    zero = jnp.zeros(val_ref.shape[1:], jnp.float32)

    @pl.when(pl.program_id(0) == 0)
    def _():
        part_ref[...] = jnp.zeros_like(part_ref)

    def forward(k, elim):
        elim = val_ref[k] + ratio_ref[k] * elim
        p_ref[k] = elim
        return elim

    lax.fori_loop(0, levels, forward, zero, unroll=4)

    def backward(k, up, succ, accs):
        value = inv_ref[k] * (p_ref[k] + up * succ)
        p_ref[k] = value
        top_ref[k] = value[value.shape[0] - 1:]
        bottom_ref[k] = value[:1]
        return value, tuple(acc + ref[k] * value for acc, ref in zip(accs, partner_refs))

    carry = backward(levels - 1, zero, zero, (zero,) * count)
    carry = lax.fori_loop(
        0, levels - 1, lambda i, c: backward(levels - 2 - i, v_ref[levels - 2 - i], *c), carry,
        unroll=4,
    )
    add_totals(part_ref, slots, carry[1])


def solve(values, inverse_pivot, ratio_values, vert_coef, partners, slots):
    levels, rows, cols = values.shape
    block = BLOCK_COLS if cols % BLOCK_COLS == 0 else cols
    full = column_spec(levels, rows, block)
    vspec = column_spec(levels - 1, rows, block)
    return pl.pallas_call(
        lambda *refs: solve_kernel(slots, *refs),
        grid=(cols // block,),
        in_specs=[full, full, full, vspec] + [full] * len(partners),
        out_specs=[full, row_block(levels, block), row_block(levels, block), tile_spec()],
        out_shape=[jax.ShapeDtypeStruct(values.shape, jnp.float32), row_shape(levels, cols),
                   row_shape(levels, cols), tile_shape()],
    )(values, inverse_pivot, ratio_values, vert_coef, *partners)


def edge_tables(edge_num, row_start, rows, weight_index, edge_map, mortar_weights):
    maps = lax.dynamic_slice_in_dim(edge_map[edge_num], row_start, rows, 0)
    picks = lax.dynamic_slice_in_dim(weight_index[edge_num], row_start, rows, 0)
    return (maps[:, 0], maps[:, 1], mortar_weights[picks, 0], mortar_weights[picks, 1])


def belt_cols(field):
    count = lax.axis_size("belt")
    first = jnp.transpose(field[:, :, 0])
    last = jnp.transpose(field[:, :, -1])
    west = lax.ppermute(last, "belt", [(i, (i + 1) % count) for i in range(count)])
    east = lax.ppermute(first, "belt", [((i + 1) % count, i) for i in range(count)])
    return west, east


def mer_rows(top, bottom):
    count = lax.axis_size("mer")
    south = lax.ppermute(top, "mer", [(i, i + 1) for i in range(count - 1)])
    north = lax.ppermute(bottom, "mer", [(i + 1, i) for i in range(count - 1)])
    return south, north


def gather_rows(column):
    count = lax.axis_size("mer")
    if count & (count - 1):
        return lax.all_gather(column, "mer", axis=0, tiled=True)
    me = lax.axis_index("mer")
    bit = 1
    while bit < count:
        other = lax.ppermute(column, "mer", [(i, i ^ bit) for i in range(count)])
        low_half = (me & bit) == 0
        column = jnp.concatenate(
            [jnp.where(low_half, column, other), jnp.where(low_half, other, column)], axis=0
        )
        bit *= 2
    return column


def as_lane_column(cols):
    return jnp.transpose(cols)[:, :, None]


def operator_kernel(slots, *refs):
    extra = len(slots) - 1
    (v_ref, vab_ref, vbe_ref, h_ref, e_ref, n_ref, up_ref, upb_ref, ew_ref, ns_ref,
     ve_ref, vw_ref, vn_ref, vs_ref) = refs[:14]
    partner_refs = (v_ref,) + refs[14:14 + extra]
    img_ref, part_ref = refs[14 + extra:]
    block, rows, cols = v_ref.shape
    i = pl.program_id(0)
    last_block = pl.num_programs(0) - 1
    lane = lax.broadcasted_iota(jnp.int32, (rows, cols), 1)
    row = lax.broadcasted_iota(jnp.int32, (rows, cols), 0)
    first_lane, last_lane = lane == 0, lane == cols - 1
    first_row, last_row = row == 0, row == rows - 1
    zero = jnp.zeros((rows, cols), jnp.float32)
    above = jnp.where(i == last_block, zero, vab_ref[0])
    below = jnp.where(i == 0, zero, vbe_ref[0])
    up_below = jnp.where(i == 0, zero, upb_ref[0])

    @pl.when(i == 0)
    def _():
        part_ref[...] = jnp.zeros_like(part_ref)

    edge = min(cols, 128)
    lane_e = lax.broadcasted_iota(jnp.int32, (rows, edge), 1)

    def first_tile(halo_ref, k, rolled):
        fixed = jnp.where(lane_e == 0, jnp.broadcast_to(halo_ref[k], (rows, edge)), rolled[:, :edge])
        return jnp.concatenate([fixed, rolled[:, edge:]], axis=1) if cols > edge else fixed

    def last_tile(halo_ref, k, rolled):
        fixed = jnp.where(lane_e == edge - 1, jnp.broadcast_to(halo_ref[k], (rows, edge)),
                          rolled[:, cols - edge:])
        return jnp.concatenate([rolled[:, :cols - edge], fixed], axis=1) if cols > edge else fixed

    def level(k, up_side, down_side, lower, accs):
        v = v_ref[k]
        east_side = last_tile(ve_ref, k, pltpu.roll(v, cols - 1, 1))
        west_side = first_tile(vw_ref, k, pltpu.roll(v, 1, 1))
        north_side = jnp.where(last_row, jnp.broadcast_to(vn_ref[k], (rows, cols)),
                               pltpu.roll(v, rows - 1, 0))
        south_side = jnp.where(first_row, jnp.broadcast_to(vs_ref[k], (rows, cols)),
                               pltpu.roll(v, 1, 0))
        east = e_ref[k]
        north = n_ref[k]
        west = ew_ref[k]
        south = ns_ref[k]
        image = (
            h_ref[k] * v
            + east * (v - east_side)
            + west * (v - west_side)
            + north * (v - north_side)
            + south * (v - south_side)
            + up_ref[k] * (v - up_side)
            + lower * (v - down_side)
        )
        img_ref[k] = image
        return tuple(acc + ref[k] * image for acc, ref in zip(accs, partner_refs))

    accs = (zero,) * len(slots)
    if block == 1:
        accs = level(0, above, below, up_below, accs)
    else:
        accs = level(0, v_ref[1], below, up_below, accs)
        accs = lax.fori_loop(
            1, block - 1,
            lambda k, c: level(k, v_ref[k + 1], v_ref[k - 1], up_ref[k - 1], c), accs,
        )
        accs = level(block - 1, above, v_ref[block - 2], up_ref[block - 2], accs)
    add_totals(part_ref, slots, accs)


def apply_operator(direction, coefs, halos, slots, extra=()):
    helm_diag, east_coef, north_coef, upper, east_west, north_south = coefs
    east_halo, west_halo, north_halo, south_halo = halos
    levels, rows, cols = direction.shape
    block = LEVEL_BLOCK if levels % LEVEL_BLOCK == 0 else levels
    blocks = levels // block
    full = pl.BlockSpec((block, rows, cols), lambda i: (i, 0, 0))
    lane_col = pl.BlockSpec((block, rows, 1), lambda i: (i, 0, 0))
    row_spec = pl.BlockSpec((block, 1, cols), lambda i: (i, 0, 0))
    above = pl.BlockSpec((1, rows, cols), lambda i: (jnp.minimum((i + 1) * block, levels - 1), 0, 0))
    below = pl.BlockSpec((1, rows, cols), lambda i: (jnp.maximum(i * block - 1, 0), 0, 0))
    kernel = lambda *refs: operator_kernel(slots, *refs)
    image, part = pl.pallas_call(
        kernel,
        grid=(blocks,),
        in_specs=[full, above, below, full, full, full, full, below, full, full,
                  lane_col, lane_col, row_spec, row_spec] + [full] * len(extra),
        out_specs=[full, tile_spec()],
        out_shape=[jax.ShapeDtypeStruct(direction.shape, jnp.float32), tile_shape()],
    )(direction, direction, direction, helm_diag, east_coef, north_coef, upper, upper,
      east_west, north_south, east_halo, west_halo, north_halo, south_halo, *extra)
    return image, part


def finish_kernel(sums_ref, p0_ref, q_ref, r0_ref, a0_ref, aq_ref, sol_ref, res_ref):
    block, rows, cols = p0_ref.shape
    sums = sums_ref[...]
    norm0, curv0, r0q, a0q, qaq, p0aq = (
        jnp.broadcast_to(sums[j:j + 1, :], sums.shape) for j in range(6)
    )
    step0 = norm0 / curv0
    norm1 = norm0 - step0 * (r0q + curv0) + step0 * step0 * a0q
    p1ap1 = curv0 - step0 * (p0aq + a0q) + step0 * step0 * qaq
    p1a0 = curv0 - step0 * a0q
    d0ap1 = curv0 - step0 * p0aq
    beta = norm1 / norm0
    curv1 = p1ap1 + beta * (p1a0 + d0ap1) + beta * beta * curv0
    step1 = norm1 / curv1
    widen = lambda x: jnp.concatenate([x[:rows]] * (cols // x.shape[1]), axis=1)
    step0, beta, step1 = widen(step0), widen(beta), widen(step1)

    def level(k, carry):
        p0 = p0_ref[k]
        a0 = a0_ref[k]
        precond1 = p0 - step0 * q_ref[k]
        direction1 = precond1 + beta * p0
        image1 = (a0 - step0 * aq_ref[k]) + beta * a0
        sol_ref[k] = step0 * p0 + step1 * direction1
        res_ref[k] = (r0_ref[k] - step0 * a0) - step1 * image1
        return carry

    lax.fori_loop(0, block, level, 0)


def finish(sums, precond0, basis, right_side, image0, image_q):
    levels, rows, cols = precond0.shape
    block = LEVEL_BLOCK if levels % LEVEL_BLOCK == 0 else levels
    full = pl.BlockSpec((block, rows, cols), lambda i: (i, 0, 0))
    field = jax.ShapeDtypeStruct(precond0.shape, jnp.float32)
    return pl.pallas_call(
        finish_kernel,
        grid=(levels // block,),
        in_specs=[tile_spec(), full, full, full, full, full],
        out_specs=[full, full],
        out_shape=[field, field],
    )(sums, precond0, basis, right_side, image0, image_q)


def exchange(direction, top, bottom, tables, use_mortar):
    count = lax.axis_size("belt")
    east = lax.ppermute(jnp.transpose(direction[:, :, 0]), "belt",
                        [((i + 1) % count, i) for i in range(count)])
    whole = gather_rows(east)
    west = lax.ppermute(jnp.transpose(direction[:, :, -1]), "belt",
                        [(i, (i + 1) % count) for i in range(count)])
    south, north = mer_rows(top, bottom)
    first_map, second_map, first_weight, second_weight = tables
    arrived = first_weight[:, None] * whole[first_map] + second_weight[:, None] * whole[second_map]
    east = jnp.where(use_mortar, arrived, east)
    return as_lane_column(east), as_lane_column(west), north, south


def on_device(
    right_side,
    helm_diag,
    east_coef,
    north_coef,
    vert_coef,
    mortar_weights,
    weight_index,
    edge_map,
    refined,
):
    belt_index = lax.axis_index("belt")
    mer_index = lax.axis_index("mer")
    per_panel = lax.axis_size("belt") // 4
    rows = right_side.shape[1]
    row_start = mer_index * rows
    own_edge = belt_index // per_panel
    row_flags = lax.dynamic_slice_in_dim(refined[own_edge], row_start, rows, 0)
    at_edge = (belt_index + 1) % per_panel == 0
    use_mortar = jnp.logical_and(at_edge, row_flags == 1)[:, None]
    tables = edge_tables(own_edge, row_start, rows, weight_index, edge_map, mortar_weights)
    levels, _, cols = right_side.shape
    block = BLOCK_COLS if cols % BLOCK_COLS == 0 else cols
    coef_west, _ = belt_cols(east_coef)
    coef_south, _ = mer_rows(north_coef[:, -1:, :], north_coef[:, :1, :])
    east_left = jnp.stack(
        [jnp.transpose(coef_west)]
        + [east_coef[:, :, j * block - 1] for j in range(1, cols // block)],
        axis=0,
    )[..., None]
    upper = jnp.concatenate([vert_coef, jnp.zeros_like(vert_coef[:1])], axis=0)

    inverse_pivot, ratio_values, precond0, top0, bottom0, west_coef, south_coef, part0 = (
        factor_solve(helm_diag, east_coef, north_coef, vert_coef, right_side, east_left, coef_south)
    )
    coefs = (helm_diag, east_coef, north_coef, upper, west_coef, south_coef)
    image0, curv_part0 = apply_operator(
        precond0, coefs, exchange(precond0, top0, bottom0, tables, use_mortar), (1,)
    )
    basis, top_q, bottom_q, basis_part = solve(
        image0, inverse_pivot, ratio_values, vert_coef, (right_side,), (2, 3)
    )
    image_q, image_q_part = apply_operator(
        basis, coefs, exchange(basis, top_q, bottom_q, tables, use_mortar), (4, 5), (precond0,)
    )
    sums = tree_sum(part0 + curv_part0 + basis_part + image_q_part)
    return finish(sums, precond0, basis, right_side, image0, image_q)


def solution(mesh):
    placed = (
        P(None, "mer", "belt"),
        P(None, "mer", "belt"),
        P(None, "mer", "belt"),
        P(None, "mer", "belt"),
        P(None, "mer", "belt"),
        P(),
        P(),
        P(),
        P(),
    )
    return jax.shard_map(
        on_device,
        mesh=mesh,
        in_specs=placed,
        out_specs=(P(None, "mer", "belt"), P(None, "mer", "belt")),
        check_vma=False,
    )
```

```python
import jax
import jax.numpy as jnp
from jax import lax
from jax.experimental import pallas as pl
from jax.experimental.pallas import tpu as pltpu
from jax.sharding import PartitionSpec as P

ITERS = 2
BLOCK_COLS = 384
LEVEL_BLOCK = 24


def tree_sum(values):
    for axis in ("mer", "belt"):
        count = lax.axis_size(axis)
        if count & (count - 1):
            values = lax.psum(values, axis)
            continue
        bit = 1
        while bit < count:
            values = values + lax.ppermute(values, axis, [(i, i ^ bit) for i in range(count)])
            bit *= 2
    return values


def add_totals(part_ref, slots, accs):
    row = lax.broadcasted_iota(jnp.int32, part_ref.shape, 0)
    tile = part_ref[...]
    for slot, acc in zip(slots, accs):
        tile = tile + jnp.where(row == slot, jnp.sum(acc), 0.0)
    part_ref[...] = tile


def tile_spec():
    return pl.BlockSpec((8, 128), lambda j: (0, 0))


def tile_shape():
    return jax.ShapeDtypeStruct((8, 128), jnp.float32)


def row_block(levels, block):
    return pl.BlockSpec((levels, 1, block), lambda j: (0, 0, j))


def row_shape(levels, cols):
    return jax.ShapeDtypeStruct((levels, 1, cols), jnp.float32)


def column_spec(levels, rows, cols):
    return pl.BlockSpec((levels, rows, cols), lambda j: (0, 0, j))


def factor_solve_kernel(h_ref, e_ref, n_ref, v_ref, r_ref, eleft_ref, nsouth_ref,
                        inv_ref, ratio_ref, p_ref, top_ref, bottom_ref, w_ref, s_ref, part_ref):
    levels, rows, cols = h_ref.shape

    @pl.when(pl.program_id(0) == 0)
    def _():
        part_ref[...] = jnp.zeros_like(part_ref)

    zero = jnp.zeros((rows, cols), jnp.float32)
    first_lane = lax.broadcasted_iota(jnp.int32, (rows, cols), 1) == 0
    first_row = lax.broadcasted_iota(jnp.int32, (rows, cols), 0) == 0

    def forward(k, up, down, prev, elim):
        east = e_ref[k]
        north = n_ref[k]
        west = jnp.where(first_lane, jnp.broadcast_to(eleft_ref[k], (rows, cols)),
                         pltpu.roll(east, 1, 1))
        south = jnp.where(first_row, jnp.broadcast_to(nsouth_ref[k], (rows, cols)),
                          pltpu.roll(north, 1, 0))
        w_ref[k] = west
        s_ref[k] = south
        diag = h_ref[k] + east + west + north + south + up + down
        ratio = down / prev
        pivot = diag - down * ratio
        inv_ref[k] = 1.0 / pivot
        ratio_ref[k] = ratio
        elim = r_ref[k] + ratio * elim
        p_ref[k] = elim
        return pivot, elim

    carry = forward(0, v_ref[0], zero, jnp.ones_like(zero), zero)
    carry = lax.fori_loop(
        1, levels - 1, lambda k, c: forward(k, v_ref[k], v_ref[k - 1], *c), carry, unroll=4
    )
    forward(levels - 1, zero, v_ref[levels - 2], *carry)

    def backward(k, up, succ, acc):
        value = inv_ref[k] * (p_ref[k] + up * succ)
        p_ref[k] = value
        top_ref[k] = value[rows - 1:rows]
        bottom_ref[k] = value[:1]
        return value, acc + r_ref[k] * value

    carry = backward(levels - 1, zero, zero, zero)
    carry = lax.fori_loop(
        0, levels - 1, lambda i, c: backward(levels - 2 - i, v_ref[levels - 2 - i], *c), carry,
        unroll=4,
    )
    add_totals(part_ref, (0,), (carry[1],))


def factor_solve(helm_diag, east_coef, north_coef, vert_coef, rhs, east_left, north_south):
    levels, rows, cols = rhs.shape
    block = BLOCK_COLS if cols % BLOCK_COLS == 0 else cols
    full = column_spec(levels, rows, block)
    vspec = column_spec(levels - 1, rows, block)
    field = jax.ShapeDtypeStruct(rhs.shape, jnp.float32)
    return pl.pallas_call(
        factor_solve_kernel,
        grid=(cols // block,),
        in_specs=[full, full, full, vspec, full,
                  pl.BlockSpec((None, levels, rows, 1), lambda j: (j, 0, 0, 0)),
                  pl.BlockSpec((levels, 1, block), lambda j: (0, 0, j))],
        out_specs=[full, full, full, row_block(levels, block), row_block(levels, block),
                   full, full, tile_spec()],
        out_shape=[field, field, field, row_shape(levels, cols), row_shape(levels, cols),
                   field, field, tile_shape()],
    )(helm_diag, east_coef, north_coef, vert_coef, rhs, east_left, north_south)


def solve_kernel(slots, *refs):
    count = len(slots)
    val_ref, inv_ref, ratio_ref, v_ref = refs[:4]
    partner_refs = refs[4:4 + count - 1] + (val_ref,)
    p_ref, top_ref, bottom_ref, part_ref = refs[4 + count - 1:]
    levels = val_ref.shape[0]
    zero = jnp.zeros(val_ref.shape[1:], jnp.float32)

    @pl.when(pl.program_id(0) == 0)
    def _():
        part_ref[...] = jnp.zeros_like(part_ref)

    def forward(k, elim):
        elim = val_ref[k] + ratio_ref[k] * elim
        p_ref[k] = elim
        return elim

    lax.fori_loop(0, levels, forward, zero, unroll=4)

    def backward(k, up, succ, accs):
        value = inv_ref[k] * (p_ref[k] + up * succ)
        p_ref[k] = value
        top_ref[k] = value[value.shape[0] - 1:]
        bottom_ref[k] = value[:1]
        return value, tuple(acc + ref[k] * value for acc, ref in zip(accs, partner_refs))

    carry = backward(levels - 1, zero, zero, (zero,) * count)
    carry = lax.fori_loop(
        0, levels - 1, lambda i, c: backward(levels - 2 - i, v_ref[levels - 2 - i], *c), carry,
        unroll=4,
    )
    add_totals(part_ref, slots, carry[1])


def solve(values, inverse_pivot, ratio_values, vert_coef, partners, slots):
    levels, rows, cols = values.shape
    block = BLOCK_COLS if cols % BLOCK_COLS == 0 else cols
    full = column_spec(levels, rows, block)
    vspec = column_spec(levels - 1, rows, block)
    return pl.pallas_call(
        lambda *refs: solve_kernel(slots, *refs),
        grid=(cols // block,),
        in_specs=[full, full, full, vspec] + [full] * len(partners),
        out_specs=[full, row_block(levels, block), row_block(levels, block), tile_spec()],
        out_shape=[jax.ShapeDtypeStruct(values.shape, jnp.float32), row_shape(levels, cols),
                   row_shape(levels, cols), tile_shape()],
    )(values, inverse_pivot, ratio_values, vert_coef, *partners)


def edge_tables(edge_num, row_start, rows, weight_index, edge_map, mortar_weights):
    maps = lax.dynamic_slice_in_dim(edge_map[edge_num], row_start, rows, 0)
    picks = lax.dynamic_slice_in_dim(weight_index[edge_num], row_start, rows, 0)
    return (maps[:, 0], maps[:, 1], mortar_weights[picks, 0], mortar_weights[picks, 1])


def belt_cols(field):
    count = lax.axis_size("belt")
    first = jnp.transpose(field[:, :, 0])
    last = jnp.transpose(field[:, :, -1])
    west = lax.ppermute(last, "belt", [(i, (i + 1) % count) for i in range(count)])
    east = lax.ppermute(first, "belt", [((i + 1) % count, i) for i in range(count)])
    return west, east


def mer_rows(top, bottom):
    count = lax.axis_size("mer")
    south = lax.ppermute(top, "mer", [(i, i + 1) for i in range(count - 1)])
    north = lax.ppermute(bottom, "mer", [(i + 1, i) for i in range(count - 1)])
    return south, north


def gather_rows(column):
    count = lax.axis_size("mer")
    if count & (count - 1):
        return lax.all_gather(column, "mer", axis=0, tiled=True)
    me = lax.axis_index("mer")
    bit = 1
    while bit < count:
        other = lax.ppermute(column, "mer", [(i, i ^ bit) for i in range(count)])
        low_half = (me & bit) == 0
        column = jnp.concatenate(
            [jnp.where(low_half, column, other), jnp.where(low_half, other, column)], axis=0
        )
        bit *= 2
    return column


def as_lane_column(cols):
    return jnp.transpose(cols)[:, :, None]


def operator_kernel(slots, *refs):
    extra = len(slots) - 1
    (v_ref, vab_ref, vbe_ref, h_ref, e_ref, n_ref, up_ref, upb_ref, ew_ref, ns_ref,
     ve_ref, vw_ref, vn_ref, vs_ref) = refs[:14]
    partner_refs = (v_ref,) + refs[14:14 + extra]
    img_ref, part_ref = refs[14 + extra:]
    block, rows, cols = v_ref.shape
    i = pl.program_id(0)
    last_block = pl.num_programs(0) - 1
    lane = lax.broadcasted_iota(jnp.int32, (rows, cols), 1)
    row = lax.broadcasted_iota(jnp.int32, (rows, cols), 0)
    first_lane, last_lane = lane == 0, lane == cols - 1
    first_row, last_row = row == 0, row == rows - 1
    zero = jnp.zeros((rows, cols), jnp.float32)
    above = jnp.where(i == last_block, zero, vab_ref[0])
    below = jnp.where(i == 0, zero, vbe_ref[0])
    up_below = jnp.where(i == 0, zero, upb_ref[0])

    @pl.when(i == 0)
    def _():
        part_ref[...] = jnp.zeros_like(part_ref)

    edge = min(cols, 128)
    lane_e = lax.broadcasted_iota(jnp.int32, (rows, edge), 1)

    def first_tile(halo_ref, k, rolled):
        fixed = jnp.where(lane_e == 0, jnp.broadcast_to(halo_ref[k], (rows, edge)), rolled[:, :edge])
        return jnp.concatenate([fixed, rolled[:, edge:]], axis=1) if cols > edge else fixed

    def last_tile(halo_ref, k, rolled):
        fixed = jnp.where(lane_e == edge - 1, jnp.broadcast_to(halo_ref[k], (rows, edge)),
                          rolled[:, cols - edge:])
        return jnp.concatenate([rolled[:, :cols - edge], fixed], axis=1) if cols > edge else fixed

    def level(k, up_side, down_side, lower, accs):
        v = v_ref[k]
        east_side = last_tile(ve_ref, k, pltpu.roll(v, cols - 1, 1))
        west_side = first_tile(vw_ref, k, pltpu.roll(v, 1, 1))
        north_side = jnp.where(last_row, jnp.broadcast_to(vn_ref[k], (rows, cols)),
                               pltpu.roll(v, rows - 1, 0))
        south_side = jnp.where(first_row, jnp.broadcast_to(vs_ref[k], (rows, cols)),
                               pltpu.roll(v, 1, 0))
        east = e_ref[k]
        north = n_ref[k]
        west = ew_ref[k]
        south = ns_ref[k]
        image = (
            h_ref[k] * v
            + east * (v - east_side)
            + west * (v - west_side)
            + north * (v - north_side)
            + south * (v - south_side)
            + up_ref[k] * (v - up_side)
            + lower * (v - down_side)
        )
        img_ref[k] = image
        return tuple(acc + ref[k] * image for acc, ref in zip(accs, partner_refs))

    accs = (zero,) * len(slots)
    if block == 1:
        accs = level(0, above, below, up_below, accs)
    else:
        accs = level(0, v_ref[1], below, up_below, accs)
        accs = lax.fori_loop(
            1, block - 1,
            lambda k, c: level(k, v_ref[k + 1], v_ref[k - 1], up_ref[k - 1], c), accs,
            unroll=2,
        )
        accs = level(block - 1, above, v_ref[block - 2], up_ref[block - 2], accs)
    add_totals(part_ref, slots, accs)


def apply_operator(direction, coefs, halos, slots, extra=()):
    helm_diag, east_coef, north_coef, upper, east_west, north_south = coefs
    east_halo, west_halo, north_halo, south_halo = halos
    levels, rows, cols = direction.shape
    block = LEVEL_BLOCK if levels % LEVEL_BLOCK == 0 else levels
    blocks = levels // block
    full = pl.BlockSpec((block, rows, cols), lambda i: (i, 0, 0))
    lane_col = pl.BlockSpec((block, rows, 1), lambda i: (i, 0, 0))
    row_spec = pl.BlockSpec((block, 1, cols), lambda i: (i, 0, 0))
    above = pl.BlockSpec((1, rows, cols), lambda i: (jnp.minimum((i + 1) * block, levels - 1), 0, 0))
    below = pl.BlockSpec((1, rows, cols), lambda i: (jnp.maximum(i * block - 1, 0), 0, 0))
    kernel = lambda *refs: operator_kernel(slots, *refs)
    image, part = pl.pallas_call(
        kernel,
        grid=(blocks,),
        in_specs=[full, above, below, full, full, full, full, below, full, full,
                  lane_col, lane_col, row_spec, row_spec] + [full] * len(extra),
        out_specs=[full, tile_spec()],
        out_shape=[jax.ShapeDtypeStruct(direction.shape, jnp.float32), tile_shape()],
    )(direction, direction, direction, helm_diag, east_coef, north_coef, upper, upper,
      east_west, north_south, east_halo, west_halo, north_halo, south_halo, *extra)
    return image, part


def finish_kernel(sums_ref, p0_ref, q_ref, r0_ref, a0_ref, aq_ref, sol_ref, res_ref):
    block, rows, cols = p0_ref.shape
    sums = sums_ref[...]
    norm0, curv0, r0q, a0q, qaq, p0aq = (
        jnp.broadcast_to(sums[j:j + 1, :], sums.shape) for j in range(6)
    )
    step0 = norm0 / curv0
    norm1 = norm0 - step0 * (r0q + curv0) + step0 * step0 * a0q
    p1ap1 = curv0 - step0 * (p0aq + a0q) + step0 * step0 * qaq
    p1a0 = curv0 - step0 * a0q
    d0ap1 = curv0 - step0 * p0aq
    beta = norm1 / norm0
    curv1 = p1ap1 + beta * (p1a0 + d0ap1) + beta * beta * curv0
    step1 = norm1 / curv1
    widen = lambda x: jnp.concatenate([x[:rows]] * (cols // x.shape[1]), axis=1)
    step0, beta, step1 = widen(step0), widen(beta), widen(step1)

    def level(k, carry):
        p0 = p0_ref[k]
        a0 = a0_ref[k]
        precond1 = p0 - step0 * q_ref[k]
        direction1 = precond1 + beta * p0
        image1 = (a0 - step0 * aq_ref[k]) + beta * a0
        sol_ref[k] = step0 * p0 + step1 * direction1
        res_ref[k] = (r0_ref[k] - step0 * a0) - step1 * image1
        return carry

    lax.fori_loop(0, block, level, 0)


def finish(sums, precond0, basis, right_side, image0, image_q):
    levels, rows, cols = precond0.shape
    block = LEVEL_BLOCK if levels % LEVEL_BLOCK == 0 else levels
    full = pl.BlockSpec((block, rows, cols), lambda i: (i, 0, 0))
    field = jax.ShapeDtypeStruct(precond0.shape, jnp.float32)
    return pl.pallas_call(
        finish_kernel,
        grid=(levels // block,),
        in_specs=[tile_spec(), full, full, full, full, full],
        out_specs=[full, full],
        out_shape=[field, field],
    )(sums, precond0, basis, right_side, image0, image_q)


def exchange(direction, top, bottom, tables, use_mortar):
    count = lax.axis_size("belt")
    east = lax.ppermute(jnp.transpose(direction[:, :, 0]), "belt",
                        [((i + 1) % count, i) for i in range(count)])
    whole = gather_rows(east)
    west = lax.ppermute(jnp.transpose(direction[:, :, -1]), "belt",
                        [(i, (i + 1) % count) for i in range(count)])
    south, north = mer_rows(top, bottom)
    first_map, second_map, first_weight, second_weight = tables
    arrived = first_weight[:, None] * whole[first_map] + second_weight[:, None] * whole[second_map]
    east = jnp.where(use_mortar, arrived, east)
    return as_lane_column(east), as_lane_column(west), north, south


def on_device(
    right_side,
    helm_diag,
    east_coef,
    north_coef,
    vert_coef,
    mortar_weights,
    weight_index,
    edge_map,
    refined,
):
    belt_index = lax.axis_index("belt")
    mer_index = lax.axis_index("mer")
    per_panel = lax.axis_size("belt") // 4
    rows = right_side.shape[1]
    row_start = mer_index * rows
    own_edge = belt_index // per_panel
    row_flags = lax.dynamic_slice_in_dim(refined[own_edge], row_start, rows, 0)
    at_edge = (belt_index + 1) % per_panel == 0
    use_mortar = jnp.logical_and(at_edge, row_flags == 1)[:, None]
    tables = edge_tables(own_edge, row_start, rows, weight_index, edge_map, mortar_weights)
    levels, _, cols = right_side.shape
    block = BLOCK_COLS if cols % BLOCK_COLS == 0 else cols
    coef_west, _ = belt_cols(east_coef)
    coef_south, _ = mer_rows(north_coef[:, -1:, :], north_coef[:, :1, :])
    east_left = jnp.stack(
        [jnp.transpose(coef_west)]
        + [east_coef[:, :, j * block - 1] for j in range(1, cols // block)],
        axis=0,
    )[..., None]
    upper = jnp.concatenate([vert_coef, jnp.zeros_like(vert_coef[:1])], axis=0)

    inverse_pivot, ratio_values, precond0, top0, bottom0, west_coef, south_coef, part0 = (
        factor_solve(helm_diag, east_coef, north_coef, vert_coef, right_side, east_left, coef_south)
    )
    coefs = (helm_diag, east_coef, north_coef, upper, west_coef, south_coef)
    image0, curv_part0 = apply_operator(
        precond0, coefs, exchange(precond0, top0, bottom0, tables, use_mortar), (1,)
    )
    basis, top_q, bottom_q, basis_part = solve(
        image0, inverse_pivot, ratio_values, vert_coef, (right_side,), (2, 3)
    )
    image_q, image_q_part = apply_operator(
        basis, coefs, exchange(basis, top_q, bottom_q, tables, use_mortar), (4, 5), (precond0,)
    )
    sums = tree_sum(part0 + curv_part0 + basis_part + image_q_part)
    return finish(sums, precond0, basis, right_side, image0, image_q)


def solution(mesh):
    placed = (
        P(None, "mer", "belt"),
        P(None, "mer", "belt"),
        P(None, "mer", "belt"),
        P(None, "mer", "belt"),
        P(None, "mer", "belt"),
        P(),
        P(),
        P(),
        P(),
    )
    return jax.shard_map(
        on_device,
        mesh=mesh,
        in_specs=placed,
        out_specs=(P(None, "mer", "belt"), P(None, "mer", "belt")),
        check_vma=False,
    )
```

```python
import jax
import jax.numpy as jnp
from jax import lax
from jax.experimental import pallas as pl
from jax.experimental.pallas import tpu as pltpu
from jax.sharding import PartitionSpec as P

ITERS = 2
BLOCK_COLS = 384
LEVEL_BLOCK = 24


def tree_sum(values):
    for axis in ("mer", "belt"):
        count = lax.axis_size(axis)
        if count & (count - 1):
            values = lax.psum(values, axis)
            continue
        bit = 1
        while bit < count:
            values = values + lax.ppermute(values, axis, [(i, i ^ bit) for i in range(count)])
            bit *= 2
    return values


def add_totals(part_ref, slots, accs):
    row = lax.broadcasted_iota(jnp.int32, part_ref.shape, 0)
    tile = part_ref[...]
    for slot, acc in zip(slots, accs):
        tile = tile + jnp.where(row == slot, jnp.sum(acc), 0.0)
    part_ref[...] = tile


def tile_spec():
    return pl.BlockSpec((8, 128), lambda j: (0, 0))


def tile_shape():
    return jax.ShapeDtypeStruct((8, 128), jnp.float32)


def row_block(levels, block):
    return pl.BlockSpec((levels, 1, block), lambda j: (0, 0, j))


def row_shape(levels, cols):
    return jax.ShapeDtypeStruct((levels, 1, cols), jnp.float32)


def column_spec(levels, rows, cols):
    return pl.BlockSpec((levels, rows, cols), lambda j: (0, 0, j))


def factor_solve_kernel(h_ref, e_ref, n_ref, v_ref, r_ref, eleft_ref, nsouth_ref,
                        inv_ref, ratio_ref, p_ref, top_ref, bottom_ref, w_ref, s_ref, part_ref):
    levels, rows, cols = h_ref.shape

    @pl.when(pl.program_id(0) == 0)
    def _():
        part_ref[...] = jnp.zeros_like(part_ref)

    zero = jnp.zeros((rows, cols), jnp.float32)
    first_lane = lax.broadcasted_iota(jnp.int32, (rows, cols), 1) == 0
    first_row = lax.broadcasted_iota(jnp.int32, (rows, cols), 0) == 0

    def forward(k, up, down, prev, elim):
        east = e_ref[k]
        north = n_ref[k]
        west = jnp.where(first_lane, jnp.broadcast_to(eleft_ref[k], (rows, cols)),
                         pltpu.roll(east, 1, 1))
        south = jnp.where(first_row, jnp.broadcast_to(nsouth_ref[k], (rows, cols)),
                          pltpu.roll(north, 1, 0))
        w_ref[k] = west
        s_ref[k] = south
        diag = h_ref[k] + east + west + north + south + up + down
        ratio = down / prev
        pivot = diag - down * ratio
        inv_ref[k] = 1.0 / pivot
        ratio_ref[k] = ratio
        elim = r_ref[k] + ratio * elim
        p_ref[k] = elim
        return pivot, elim

    carry = forward(0, v_ref[0], zero, jnp.ones_like(zero), zero)
    carry = lax.fori_loop(
        1, levels - 1, lambda k, c: forward(k, v_ref[k], v_ref[k - 1], *c), carry, unroll=4
    )
    forward(levels - 1, zero, v_ref[levels - 2], *carry)

    def backward(k, up, succ, acc):
        value = inv_ref[k] * (p_ref[k] + up * succ)
        p_ref[k] = value
        top_ref[k] = value[rows - 1:rows]
        bottom_ref[k] = value[:1]
        return value, acc + r_ref[k] * value

    carry = backward(levels - 1, zero, zero, zero)
    carry = lax.fori_loop(
        0, levels - 1, lambda i, c: backward(levels - 2 - i, v_ref[levels - 2 - i], *c), carry,
        unroll=4,
    )
    add_totals(part_ref, (0,), (carry[1],))


def factor_solve(helm_diag, east_coef, north_coef, vert_coef, rhs, east_left, north_south):
    levels, rows, cols = rhs.shape
    block = BLOCK_COLS if cols % BLOCK_COLS == 0 else cols
    full = column_spec(levels, rows, block)
    vspec = column_spec(levels - 1, rows, block)
    field = jax.ShapeDtypeStruct(rhs.shape, jnp.float32)
    return pl.pallas_call(
        factor_solve_kernel,
        grid=(cols // block,),
        in_specs=[full, full, full, vspec, full,
                  pl.BlockSpec((None, levels, rows, 1), lambda j: (j, 0, 0, 0)),
                  pl.BlockSpec((levels, 1, block), lambda j: (0, 0, j))],
        out_specs=[full, full, full, row_block(levels, block), row_block(levels, block),
                   full, full, tile_spec()],
        out_shape=[field, field, field, row_shape(levels, cols), row_shape(levels, cols),
                   field, field, tile_shape()],
    )(helm_diag, east_coef, north_coef, vert_coef, rhs, east_left, north_south)


def solve_kernel(slots, *refs):
    count = len(slots)
    val_ref, inv_ref, ratio_ref, v_ref = refs[:4]
    partner_refs = refs[4:4 + count - 1] + (val_ref,)
    p_ref, top_ref, bottom_ref, part_ref = refs[4 + count - 1:]
    levels = val_ref.shape[0]
    zero = jnp.zeros(val_ref.shape[1:], jnp.float32)

    @pl.when(pl.program_id(0) == 0)
    def _():
        part_ref[...] = jnp.zeros_like(part_ref)

    def forward(k, elim):
        elim = val_ref[k] + ratio_ref[k] * elim
        p_ref[k] = elim
        return elim

    lax.fori_loop(0, levels, forward, zero, unroll=4)

    def backward(k, up, succ, accs):
        value = inv_ref[k] * (p_ref[k] + up * succ)
        p_ref[k] = value
        top_ref[k] = value[value.shape[0] - 1:]
        bottom_ref[k] = value[:1]
        return value, tuple(acc + ref[k] * value for acc, ref in zip(accs, partner_refs))

    carry = backward(levels - 1, zero, zero, (zero,) * count)
    carry = lax.fori_loop(
        0, levels - 1, lambda i, c: backward(levels - 2 - i, v_ref[levels - 2 - i], *c), carry,
        unroll=4,
    )
    add_totals(part_ref, slots, carry[1])


def solve(values, inverse_pivot, ratio_values, vert_coef, partners, slots):
    levels, rows, cols = values.shape
    block = BLOCK_COLS if cols % BLOCK_COLS == 0 else cols
    full = column_spec(levels, rows, block)
    vspec = column_spec(levels - 1, rows, block)
    return pl.pallas_call(
        lambda *refs: solve_kernel(slots, *refs),
        grid=(cols // block,),
        in_specs=[full, full, full, vspec] + [full] * len(partners),
        out_specs=[full, row_block(levels, block), row_block(levels, block), tile_spec()],
        out_shape=[jax.ShapeDtypeStruct(values.shape, jnp.float32), row_shape(levels, cols),
                   row_shape(levels, cols), tile_shape()],
    )(values, inverse_pivot, ratio_values, vert_coef, *partners)


def edge_tables(edge_num, row_start, rows, weight_index, edge_map, mortar_weights):
    maps = lax.dynamic_slice_in_dim(edge_map[edge_num], row_start, rows, 0)
    picks = lax.dynamic_slice_in_dim(weight_index[edge_num], row_start, rows, 0)
    return (maps[:, 0], maps[:, 1], mortar_weights[picks, 0], mortar_weights[picks, 1])


def belt_cols(field):
    count = lax.axis_size("belt")
    first = jnp.transpose(field[:, :, 0])
    last = jnp.transpose(field[:, :, -1])
    west = lax.ppermute(last, "belt", [(i, (i + 1) % count) for i in range(count)])
    east = lax.ppermute(first, "belt", [((i + 1) % count, i) for i in range(count)])
    return west, east


def mer_rows(top, bottom):
    count = lax.axis_size("mer")
    south = lax.ppermute(top, "mer", [(i, i + 1) for i in range(count - 1)])
    north = lax.ppermute(bottom, "mer", [(i + 1, i) for i in range(count - 1)])
    return south, north


def gather_rows(column):
    count = lax.axis_size("mer")
    if count & (count - 1):
        return lax.all_gather(column, "mer", axis=0, tiled=True)
    me = lax.axis_index("mer")
    bit = 1
    while bit < count:
        other = lax.ppermute(column, "mer", [(i, i ^ bit) for i in range(count)])
        low_half = (me & bit) == 0
        column = jnp.concatenate(
            [jnp.where(low_half, column, other), jnp.where(low_half, other, column)], axis=0
        )
        bit *= 2
    return column


def as_lane_column(cols):
    return jnp.transpose(cols)[:, :, None]


def operator_kernel(slots, *refs):
    extra = len(slots) - 1
    (v_ref, vab_ref, vbe_ref, h_ref, e_ref, n_ref, up_ref, upb_ref, ew_ref, ns_ref,
     ve_ref, vw_ref, vn_ref, vs_ref) = refs[:14]
    partner_refs = (v_ref,) + refs[14:14 + extra]
    img_ref, part_ref = refs[14 + extra:]
    block, rows, cols = v_ref.shape
    i = pl.program_id(0)
    last_block = pl.num_programs(0) - 1
    lane = lax.broadcasted_iota(jnp.int32, (rows, cols), 1)
    row = lax.broadcasted_iota(jnp.int32, (rows, cols), 0)
    first_lane, last_lane = lane == 0, lane == cols - 1
    first_row, last_row = row == 0, row == rows - 1
    zero = jnp.zeros((rows, cols), jnp.float32)
    above = jnp.where(i == last_block, zero, vab_ref[0])
    below = jnp.where(i == 0, zero, vbe_ref[0])
    up_below = jnp.where(i == 0, zero, upb_ref[0])

    @pl.when(i == 0)
    def _():
        part_ref[...] = jnp.zeros_like(part_ref)

    edge = min(cols, 128)
    lane_e = lax.broadcasted_iota(jnp.int32, (rows, edge), 1)

    def first_tile(halo_ref, k, rolled):
        fixed = jnp.where(lane_e == 0, jnp.broadcast_to(halo_ref[k], (rows, edge)), rolled[:, :edge])
        return jnp.concatenate([fixed, rolled[:, edge:]], axis=1) if cols > edge else fixed

    def last_tile(halo_ref, k, rolled):
        fixed = jnp.where(lane_e == edge - 1, jnp.broadcast_to(halo_ref[k], (rows, edge)),
                          rolled[:, cols - edge:])
        return jnp.concatenate([rolled[:, :cols - edge], fixed], axis=1) if cols > edge else fixed

    def level(k, up_side, down_side, lower, accs):
        v = v_ref[k]
        east_side = last_tile(ve_ref, k, pltpu.roll(v, cols - 1, 1))
        west_side = first_tile(vw_ref, k, pltpu.roll(v, 1, 1))
        north_side = jnp.where(last_row, jnp.broadcast_to(vn_ref[k], (rows, cols)),
                               pltpu.roll(v, rows - 1, 0))
        south_side = jnp.where(first_row, jnp.broadcast_to(vs_ref[k], (rows, cols)),
                               pltpu.roll(v, 1, 0))
        east = e_ref[k]
        north = n_ref[k]
        west = ew_ref[k]
        south = ns_ref[k]
        image = (
            h_ref[k] * v
            + east * (v - east_side)
            + west * (v - west_side)
            + north * (v - north_side)
            + south * (v - south_side)
            + up_ref[k] * (v - up_side)
            + lower * (v - down_side)
        )
        img_ref[k] = image
        return tuple(acc + ref[k] * image for acc, ref in zip(accs, partner_refs))

    accs = (zero,) * len(slots)
    if block == 1:
        accs = level(0, above, below, up_below, accs)
    else:
        accs = level(0, v_ref[1], below, up_below, accs)
        accs = lax.fori_loop(
            1, block - 1,
            lambda k, c: level(k, v_ref[k + 1], v_ref[k - 1], up_ref[k - 1], c), accs,
            unroll=4,
        )
        accs = level(block - 1, above, v_ref[block - 2], up_ref[block - 2], accs)
    add_totals(part_ref, slots, accs)


def apply_operator(direction, coefs, halos, slots, extra=()):
    helm_diag, east_coef, north_coef, upper, east_west, north_south = coefs
    east_halo, west_halo, north_halo, south_halo = halos
    levels, rows, cols = direction.shape
    block = LEVEL_BLOCK if levels % LEVEL_BLOCK == 0 else levels
    blocks = levels // block
    full = pl.BlockSpec((block, rows, cols), lambda i: (i, 0, 0))
    lane_col = pl.BlockSpec((block, rows, 1), lambda i: (i, 0, 0))
    row_spec = pl.BlockSpec((block, 1, cols), lambda i: (i, 0, 0))
    above = pl.BlockSpec((1, rows, cols), lambda i: (jnp.minimum((i + 1) * block, levels - 1), 0, 0))
    below = pl.BlockSpec((1, rows, cols), lambda i: (jnp.maximum(i * block - 1, 0), 0, 0))
    kernel = lambda *refs: operator_kernel(slots, *refs)
    image, part = pl.pallas_call(
        kernel,
        grid=(blocks,),
        in_specs=[full, above, below, full, full, full, full, below, full, full,
                  lane_col, lane_col, row_spec, row_spec] + [full] * len(extra),
        out_specs=[full, tile_spec()],
        out_shape=[jax.ShapeDtypeStruct(direction.shape, jnp.float32), tile_shape()],
    )(direction, direction, direction, helm_diag, east_coef, north_coef, upper, upper,
      east_west, north_south, east_halo, west_halo, north_halo, south_halo, *extra)
    return image, part


def finish_kernel(sums_ref, p0_ref, q_ref, r0_ref, a0_ref, aq_ref, sol_ref, res_ref):
    block, rows, cols = p0_ref.shape
    sums = sums_ref[...]
    norm0, curv0, r0q, a0q, qaq, p0aq = (
        jnp.broadcast_to(sums[j:j + 1, :], sums.shape) for j in range(6)
    )
    step0 = norm0 / curv0
    norm1 = norm0 - step0 * (r0q + curv0) + step0 * step0 * a0q
    p1ap1 = curv0 - step0 * (p0aq + a0q) + step0 * step0 * qaq
    p1a0 = curv0 - step0 * a0q
    d0ap1 = curv0 - step0 * p0aq
    beta = norm1 / norm0
    curv1 = p1ap1 + beta * (p1a0 + d0ap1) + beta * beta * curv0
    step1 = norm1 / curv1
    widen = lambda x: jnp.concatenate([x[:rows]] * (cols // x.shape[1]), axis=1)
    step0, beta, step1 = widen(step0), widen(beta), widen(step1)

    def level(k, carry):
        p0 = p0_ref[k]
        a0 = a0_ref[k]
        precond1 = p0 - step0 * q_ref[k]
        direction1 = precond1 + beta * p0
        image1 = (a0 - step0 * aq_ref[k]) + beta * a0
        sol_ref[k] = step0 * p0 + step1 * direction1
        res_ref[k] = (r0_ref[k] - step0 * a0) - step1 * image1
        return carry

    lax.fori_loop(0, block, level, 0, unroll=2)


def finish(sums, precond0, basis, right_side, image0, image_q):
    levels, rows, cols = precond0.shape
    block = LEVEL_BLOCK if levels % LEVEL_BLOCK == 0 else levels
    full = pl.BlockSpec((block, rows, cols), lambda i: (i, 0, 0))
    field = jax.ShapeDtypeStruct(precond0.shape, jnp.float32)
    return pl.pallas_call(
        finish_kernel,
        grid=(levels // block,),
        in_specs=[tile_spec(), full, full, full, full, full],
        out_specs=[full, full],
        out_shape=[field, field],
    )(sums, precond0, basis, right_side, image0, image_q)


def exchange(direction, top, bottom, tables, use_mortar):
    count = lax.axis_size("belt")
    east = lax.ppermute(jnp.transpose(direction[:, :, 0]), "belt",
                        [((i + 1) % count, i) for i in range(count)])
    whole = gather_rows(east)
    west = lax.ppermute(jnp.transpose(direction[:, :, -1]), "belt",
                        [(i, (i + 1) % count) for i in range(count)])
    south, north = mer_rows(top, bottom)
    first_map, second_map, first_weight, second_weight = tables
    arrived = first_weight[:, None] * whole[first_map] + second_weight[:, None] * whole[second_map]
    east = jnp.where(use_mortar, arrived, east)
    return as_lane_column(east), as_lane_column(west), north, south


def on_device(
    right_side,
    helm_diag,
    east_coef,
    north_coef,
    vert_coef,
    mortar_weights,
    weight_index,
    edge_map,
    refined,
):
    belt_index = lax.axis_index("belt")
    mer_index = lax.axis_index("mer")
    per_panel = lax.axis_size("belt") // 4
    rows = right_side.shape[1]
    row_start = mer_index * rows
    own_edge = belt_index // per_panel
    row_flags = lax.dynamic_slice_in_dim(refined[own_edge], row_start, rows, 0)
    at_edge = (belt_index + 1) % per_panel == 0
    use_mortar = jnp.logical_and(at_edge, row_flags == 1)[:, None]
    tables = edge_tables(own_edge, row_start, rows, weight_index, edge_map, mortar_weights)
    levels, _, cols = right_side.shape
    block = BLOCK_COLS if cols % BLOCK_COLS == 0 else cols
    coef_west, _ = belt_cols(east_coef)
    coef_south, _ = mer_rows(north_coef[:, -1:, :], north_coef[:, :1, :])
    east_left = jnp.stack(
        [jnp.transpose(coef_west)]
        + [east_coef[:, :, j * block - 1] for j in range(1, cols // block)],
        axis=0,
    )[..., None]
    upper = jnp.concatenate([vert_coef, jnp.zeros_like(vert_coef[:1])], axis=0)

    inverse_pivot, ratio_values, precond0, top0, bottom0, west_coef, south_coef, part0 = (
        factor_solve(helm_diag, east_coef, north_coef, vert_coef, right_side, east_left, coef_south)
    )
    coefs = (helm_diag, east_coef, north_coef, upper, west_coef, south_coef)
    image0, curv_part0 = apply_operator(
        precond0, coefs, exchange(precond0, top0, bottom0, tables, use_mortar), (1,)
    )
    basis, top_q, bottom_q, basis_part = solve(
        image0, inverse_pivot, ratio_values, vert_coef, (right_side,), (2, 3)
    )
    image_q, image_q_part = apply_operator(
        basis, coefs, exchange(basis, top_q, bottom_q, tables, use_mortar), (4, 5), (precond0,)
    )
    sums = tree_sum(part0 + curv_part0 + basis_part + image_q_part)
    return finish(sums, precond0, basis, right_side, image0, image_q)


def solution(mesh):
    placed = (
        P(None, "mer", "belt"),
        P(None, "mer", "belt"),
        P(None, "mer", "belt"),
        P(None, "mer", "belt"),
        P(None, "mer", "belt"),
        P(),
        P(),
        P(),
        P(),
    )
    return jax.shard_map(
        on_device,
        mesh=mesh,
        in_specs=placed,
        out_specs=(P(None, "mer", "belt"), P(None, "mer", "belt")),
        check_vma=False,
    )
```

```python
import jax
import jax.numpy as jnp
from jax import lax
from jax.experimental import pallas as pl
from jax.experimental.pallas import tpu as pltpu
from jax.sharding import PartitionSpec as P

ITERS = 2
BLOCK_COLS = 384
LEVEL_BLOCK = 24


def tree_sum(values):
    for axis in ("mer", "belt"):
        count = lax.axis_size(axis)
        if count & (count - 1):
            values = lax.psum(values, axis)
            continue
        bit = 1
        while bit < count:
            values = values + lax.ppermute(values, axis, [(i, i ^ bit) for i in range(count)])
            bit *= 2
    return values


def add_totals(part_ref, slots, accs):
    row = lax.broadcasted_iota(jnp.int32, part_ref.shape, 0)
    tile = part_ref[...]
    for slot, acc in zip(slots, accs):
        tile = tile + jnp.where(row == slot, jnp.sum(acc), 0.0)
    part_ref[...] = tile


def tile_spec():
    return pl.BlockSpec((8, 128), lambda j: (0, 0))


def tile_shape():
    return jax.ShapeDtypeStruct((8, 128), jnp.float32)


def row_block(levels, block):
    return pl.BlockSpec((levels, 1, block), lambda j: (0, 0, j))


def row_shape(levels, cols):
    return jax.ShapeDtypeStruct((levels, 1, cols), jnp.float32)


def column_spec(levels, rows, cols):
    return pl.BlockSpec((levels, rows, cols), lambda j: (0, 0, j))


def factor_solve_kernel(h_ref, e_ref, n_ref, v_ref, r_ref, eleft_ref, nsouth_ref,
                        inv_ref, ratio_ref, p_ref, top_ref, bottom_ref, w_ref, s_ref, part_ref):
    levels, rows, cols = h_ref.shape

    @pl.when(pl.program_id(0) == 0)
    def _():
        part_ref[...] = jnp.zeros_like(part_ref)

    zero = jnp.zeros((rows, cols), jnp.float32)
    first_lane = lax.broadcasted_iota(jnp.int32, (rows, cols), 1) == 0
    first_row = lax.broadcasted_iota(jnp.int32, (rows, cols), 0) == 0

    def forward(k, up, down, prev, elim):
        east = e_ref[k]
        north = n_ref[k]
        west = jnp.where(first_lane, jnp.broadcast_to(eleft_ref[k], (rows, cols)),
                         pltpu.roll(east, 1, 1))
        south = jnp.where(first_row, jnp.broadcast_to(nsouth_ref[k], (rows, cols)),
                          pltpu.roll(north, 1, 0))
        w_ref[k] = west
        s_ref[k] = south
        diag = h_ref[k] + east + west + north + south + up + down
        ratio = down / prev
        pivot = diag - down * ratio
        inv_ref[k] = 1.0 / pivot
        ratio_ref[k] = ratio
        elim = r_ref[k] + ratio * elim
        p_ref[k] = elim
        return pivot, elim

    carry = forward(0, v_ref[0], zero, jnp.ones_like(zero), zero)
    carry = lax.fori_loop(
        1, levels - 1, lambda k, c: forward(k, v_ref[k], v_ref[k - 1], *c), carry, unroll=8
    )
    forward(levels - 1, zero, v_ref[levels - 2], *carry)

    def backward(k, up, succ, acc):
        value = inv_ref[k] * (p_ref[k] + up * succ)
        p_ref[k] = value
        top_ref[k] = value[rows - 1:rows]
        bottom_ref[k] = value[:1]
        return value, acc + r_ref[k] * value

    carry = backward(levels - 1, zero, zero, zero)
    carry = lax.fori_loop(
        0, levels - 1, lambda i, c: backward(levels - 2 - i, v_ref[levels - 2 - i], *c), carry,
        unroll=8,
    )
    add_totals(part_ref, (0,), (carry[1],))


def factor_solve(helm_diag, east_coef, north_coef, vert_coef, rhs, east_left, north_south):
    levels, rows, cols = rhs.shape
    block = BLOCK_COLS if cols % BLOCK_COLS == 0 else cols
    full = column_spec(levels, rows, block)
    vspec = column_spec(levels - 1, rows, block)
    field = jax.ShapeDtypeStruct(rhs.shape, jnp.float32)
    return pl.pallas_call(
        factor_solve_kernel,
        grid=(cols // block,),
        in_specs=[full, full, full, vspec, full,
                  pl.BlockSpec((None, levels, rows, 1), lambda j: (j, 0, 0, 0)),
                  pl.BlockSpec((levels, 1, block), lambda j: (0, 0, j))],
        out_specs=[full, full, full, row_block(levels, block), row_block(levels, block),
                   full, full, tile_spec()],
        out_shape=[field, field, field, row_shape(levels, cols), row_shape(levels, cols),
                   field, field, tile_shape()],
    )(helm_diag, east_coef, north_coef, vert_coef, rhs, east_left, north_south)


def solve_kernel(slots, *refs):
    count = len(slots)
    val_ref, inv_ref, ratio_ref, v_ref = refs[:4]
    partner_refs = refs[4:4 + count - 1] + (val_ref,)
    p_ref, top_ref, bottom_ref, part_ref = refs[4 + count - 1:]
    levels = val_ref.shape[0]
    zero = jnp.zeros(val_ref.shape[1:], jnp.float32)

    @pl.when(pl.program_id(0) == 0)
    def _():
        part_ref[...] = jnp.zeros_like(part_ref)

    def forward(k, elim):
        elim = val_ref[k] + ratio_ref[k] * elim
        p_ref[k] = elim
        return elim

    lax.fori_loop(0, levels, forward, zero, unroll=8)

    def backward(k, up, succ, accs):
        value = inv_ref[k] * (p_ref[k] + up * succ)
        p_ref[k] = value
        top_ref[k] = value[value.shape[0] - 1:]
        bottom_ref[k] = value[:1]
        return value, tuple(acc + ref[k] * value for acc, ref in zip(accs, partner_refs))

    carry = backward(levels - 1, zero, zero, (zero,) * count)
    carry = lax.fori_loop(
        0, levels - 1, lambda i, c: backward(levels - 2 - i, v_ref[levels - 2 - i], *c), carry,
        unroll=8,
    )
    add_totals(part_ref, slots, carry[1])


def solve(values, inverse_pivot, ratio_values, vert_coef, partners, slots):
    levels, rows, cols = values.shape
    block = BLOCK_COLS if cols % BLOCK_COLS == 0 else cols
    full = column_spec(levels, rows, block)
    vspec = column_spec(levels - 1, rows, block)
    return pl.pallas_call(
        lambda *refs: solve_kernel(slots, *refs),
        grid=(cols // block,),
        in_specs=[full, full, full, vspec] + [full] * len(partners),
        out_specs=[full, row_block(levels, block), row_block(levels, block), tile_spec()],
        out_shape=[jax.ShapeDtypeStruct(values.shape, jnp.float32), row_shape(levels, cols),
                   row_shape(levels, cols), tile_shape()],
    )(values, inverse_pivot, ratio_values, vert_coef, *partners)


def edge_tables(edge_num, row_start, rows, weight_index, edge_map, mortar_weights):
    maps = lax.dynamic_slice_in_dim(edge_map[edge_num], row_start, rows, 0)
    picks = lax.dynamic_slice_in_dim(weight_index[edge_num], row_start, rows, 0)
    return (maps[:, 0], maps[:, 1], mortar_weights[picks, 0], mortar_weights[picks, 1])


def belt_cols(field):
    count = lax.axis_size("belt")
    first = jnp.transpose(field[:, :, 0])
    last = jnp.transpose(field[:, :, -1])
    west = lax.ppermute(last, "belt", [(i, (i + 1) % count) for i in range(count)])
    east = lax.ppermute(first, "belt", [((i + 1) % count, i) for i in range(count)])
    return west, east


def mer_rows(top, bottom):
    count = lax.axis_size("mer")
    south = lax.ppermute(top, "mer", [(i, i + 1) for i in range(count - 1)])
    north = lax.ppermute(bottom, "mer", [(i + 1, i) for i in range(count - 1)])
    return south, north


def gather_rows(column):
    count = lax.axis_size("mer")
    if count & (count - 1):
        return lax.all_gather(column, "mer", axis=0, tiled=True)
    me = lax.axis_index("mer")
    bit = 1
    while bit < count:
        other = lax.ppermute(column, "mer", [(i, i ^ bit) for i in range(count)])
        low_half = (me & bit) == 0
        column = jnp.concatenate(
            [jnp.where(low_half, column, other), jnp.where(low_half, other, column)], axis=0
        )
        bit *= 2
    return column


def as_lane_column(cols):
    return jnp.transpose(cols)[:, :, None]


def operator_kernel(slots, *refs):
    extra = len(slots) - 1
    (v_ref, vab_ref, vbe_ref, h_ref, e_ref, n_ref, up_ref, upb_ref, ew_ref, ns_ref,
     ve_ref, vw_ref, vn_ref, vs_ref) = refs[:14]
    partner_refs = (v_ref,) + refs[14:14 + extra]
    img_ref, part_ref = refs[14 + extra:]
    block, rows, cols = v_ref.shape
    i = pl.program_id(0)
    last_block = pl.num_programs(0) - 1
    lane = lax.broadcasted_iota(jnp.int32, (rows, cols), 1)
    row = lax.broadcasted_iota(jnp.int32, (rows, cols), 0)
    first_lane, last_lane = lane == 0, lane == cols - 1
    first_row, last_row = row == 0, row == rows - 1
    zero = jnp.zeros((rows, cols), jnp.float32)
    above = jnp.where(i == last_block, zero, vab_ref[0])
    below = jnp.where(i == 0, zero, vbe_ref[0])
    up_below = jnp.where(i == 0, zero, upb_ref[0])

    @pl.when(i == 0)
    def _():
        part_ref[...] = jnp.zeros_like(part_ref)

    edge = min(cols, 128)
    lane_e = lax.broadcasted_iota(jnp.int32, (rows, edge), 1)

    def first_tile(halo_ref, k, rolled):
        fixed = jnp.where(lane_e == 0, jnp.broadcast_to(halo_ref[k], (rows, edge)), rolled[:, :edge])
        return jnp.concatenate([fixed, rolled[:, edge:]], axis=1) if cols > edge else fixed

    def last_tile(halo_ref, k, rolled):
        fixed = jnp.where(lane_e == edge - 1, jnp.broadcast_to(halo_ref[k], (rows, edge)),
                          rolled[:, cols - edge:])
        return jnp.concatenate([rolled[:, :cols - edge], fixed], axis=1) if cols > edge else fixed

    def level(k, up_side, down_side, lower, accs):
        v = v_ref[k]
        east_side = last_tile(ve_ref, k, pltpu.roll(v, cols - 1, 1))
        west_side = first_tile(vw_ref, k, pltpu.roll(v, 1, 1))
        north_side = jnp.where(last_row, jnp.broadcast_to(vn_ref[k], (rows, cols)),
                               pltpu.roll(v, rows - 1, 0))
        south_side = jnp.where(first_row, jnp.broadcast_to(vs_ref[k], (rows, cols)),
                               pltpu.roll(v, 1, 0))
        east = e_ref[k]
        north = n_ref[k]
        west = ew_ref[k]
        south = ns_ref[k]
        image = (
            h_ref[k] * v
            + east * (v - east_side)
            + west * (v - west_side)
            + north * (v - north_side)
            + south * (v - south_side)
            + up_ref[k] * (v - up_side)
            + lower * (v - down_side)
        )
        img_ref[k] = image
        return tuple(acc + ref[k] * image for acc, ref in zip(accs, partner_refs))

    accs = (zero,) * len(slots)
    if block == 1:
        accs = level(0, above, below, up_below, accs)
    else:
        accs = level(0, v_ref[1], below, up_below, accs)
        accs = lax.fori_loop(
            1, block - 1,
            lambda k, c: level(k, v_ref[k + 1], v_ref[k - 1], up_ref[k - 1], c), accs,
            unroll=4,
        )
        accs = level(block - 1, above, v_ref[block - 2], up_ref[block - 2], accs)
    add_totals(part_ref, slots, accs)


def apply_operator(direction, coefs, halos, slots, extra=()):
    helm_diag, east_coef, north_coef, upper, east_west, north_south = coefs
    east_halo, west_halo, north_halo, south_halo = halos
    levels, rows, cols = direction.shape
    block = LEVEL_BLOCK if levels % LEVEL_BLOCK == 0 else levels
    blocks = levels // block
    full = pl.BlockSpec((block, rows, cols), lambda i: (i, 0, 0))
    lane_col = pl.BlockSpec((block, rows, 1), lambda i: (i, 0, 0))
    row_spec = pl.BlockSpec((block, 1, cols), lambda i: (i, 0, 0))
    above = pl.BlockSpec((1, rows, cols), lambda i: (jnp.minimum((i + 1) * block, levels - 1), 0, 0))
    below = pl.BlockSpec((1, rows, cols), lambda i: (jnp.maximum(i * block - 1, 0), 0, 0))
    kernel = lambda *refs: operator_kernel(slots, *refs)
    image, part = pl.pallas_call(
        kernel,
        grid=(blocks,),
        in_specs=[full, above, below, full, full, full, full, below, full, full,
                  lane_col, lane_col, row_spec, row_spec] + [full] * len(extra),
        out_specs=[full, tile_spec()],
        out_shape=[jax.ShapeDtypeStruct(direction.shape, jnp.float32), tile_shape()],
    )(direction, direction, direction, helm_diag, east_coef, north_coef, upper, upper,
      east_west, north_south, east_halo, west_halo, north_halo, south_halo, *extra)
    return image, part


def finish_kernel(sums_ref, p0_ref, q_ref, r0_ref, a0_ref, aq_ref, sol_ref, res_ref):
    block, rows, cols = p0_ref.shape
    sums = sums_ref[...]
    norm0, curv0, r0q, a0q, qaq, p0aq = (
        jnp.broadcast_to(sums[j:j + 1, :], sums.shape) for j in range(6)
    )
    step0 = norm0 / curv0
    norm1 = norm0 - step0 * (r0q + curv0) + step0 * step0 * a0q
    p1ap1 = curv0 - step0 * (p0aq + a0q) + step0 * step0 * qaq
    p1a0 = curv0 - step0 * a0q
    d0ap1 = curv0 - step0 * p0aq
    beta = norm1 / norm0
    curv1 = p1ap1 + beta * (p1a0 + d0ap1) + beta * beta * curv0
    step1 = norm1 / curv1
    widen = lambda x: jnp.concatenate([x[:rows]] * (cols // x.shape[1]), axis=1)
    step0, beta, step1 = widen(step0), widen(beta), widen(step1)

    def level(k, carry):
        p0 = p0_ref[k]
        a0 = a0_ref[k]
        precond1 = p0 - step0 * q_ref[k]
        direction1 = precond1 + beta * p0
        image1 = (a0 - step0 * aq_ref[k]) + beta * a0
        sol_ref[k] = step0 * p0 + step1 * direction1
        res_ref[k] = (r0_ref[k] - step0 * a0) - step1 * image1
        return carry

    lax.fori_loop(0, block, level, 0, unroll=2)


def finish(sums, precond0, basis, right_side, image0, image_q):
    levels, rows, cols = precond0.shape
    block = LEVEL_BLOCK if levels % LEVEL_BLOCK == 0 else levels
    full = pl.BlockSpec((block, rows, cols), lambda i: (i, 0, 0))
    field = jax.ShapeDtypeStruct(precond0.shape, jnp.float32)
    return pl.pallas_call(
        finish_kernel,
        grid=(levels // block,),
        in_specs=[tile_spec(), full, full, full, full, full],
        out_specs=[full, full],
        out_shape=[field, field],
    )(sums, precond0, basis, right_side, image0, image_q)


def exchange(direction, top, bottom, tables, use_mortar):
    count = lax.axis_size("belt")
    east = lax.ppermute(jnp.transpose(direction[:, :, 0]), "belt",
                        [((i + 1) % count, i) for i in range(count)])
    whole = gather_rows(east)
    west = lax.ppermute(jnp.transpose(direction[:, :, -1]), "belt",
                        [(i, (i + 1) % count) for i in range(count)])
    south, north = mer_rows(top, bottom)
    first_map, second_map, first_weight, second_weight = tables
    arrived = first_weight[:, None] * whole[first_map] + second_weight[:, None] * whole[second_map]
    east = jnp.where(use_mortar, arrived, east)
    return as_lane_column(east), as_lane_column(west), north, south


def on_device(
    right_side,
    helm_diag,
    east_coef,
    north_coef,
    vert_coef,
    mortar_weights,
    weight_index,
    edge_map,
    refined,
):
    belt_index = lax.axis_index("belt")
    mer_index = lax.axis_index("mer")
    per_panel = lax.axis_size("belt") // 4
    rows = right_side.shape[1]
    row_start = mer_index * rows
    own_edge = belt_index // per_panel
    row_flags = lax.dynamic_slice_in_dim(refined[own_edge], row_start, rows, 0)
    at_edge = (belt_index + 1) % per_panel == 0
    use_mortar = jnp.logical_and(at_edge, row_flags == 1)[:, None]
    tables = edge_tables(own_edge, row_start, rows, weight_index, edge_map, mortar_weights)
    levels, _, cols = right_side.shape
    block = BLOCK_COLS if cols % BLOCK_COLS == 0 else cols
    coef_west, _ = belt_cols(east_coef)
    coef_south, _ = mer_rows(north_coef[:, -1:, :], north_coef[:, :1, :])
    east_left = jnp.stack(
        [jnp.transpose(coef_west)]
        + [east_coef[:, :, j * block - 1] for j in range(1, cols // block)],
        axis=0,
    )[..., None]
    upper = jnp.concatenate([vert_coef, jnp.zeros_like(vert_coef[:1])], axis=0)

    inverse_pivot, ratio_values, precond0, top0, bottom0, west_coef, south_coef, part0 = (
        factor_solve(helm_diag, east_coef, north_coef, vert_coef, right_side, east_left, coef_south)
    )
    coefs = (helm_diag, east_coef, north_coef, upper, west_coef, south_coef)
    image0, curv_part0 = apply_operator(
        precond0, coefs, exchange(precond0, top0, bottom0, tables, use_mortar), (1,)
    )
    basis, top_q, bottom_q, basis_part = solve(
        image0, inverse_pivot, ratio_values, vert_coef, (right_side,), (2, 3)
    )
    image_q, image_q_part = apply_operator(
        basis, coefs, exchange(basis, top_q, bottom_q, tables, use_mortar), (4, 5), (precond0,)
    )
    sums = tree_sum(part0 + curv_part0 + basis_part + image_q_part)
    return finish(sums, precond0, basis, right_side, image0, image_q)


def solution(mesh):
    placed = (
        P(None, "mer", "belt"),
        P(None, "mer", "belt"),
        P(None, "mer", "belt"),
        P(None, "mer", "belt"),
        P(None, "mer", "belt"),
        P(),
        P(),
        P(),
        P(),
    )
    return jax.shard_map(
        on_device,
        mesh=mesh,
        in_specs=placed,
        out_specs=(P(None, "mer", "belt"), P(None, "mer", "belt")),
        check_vma=False,
    )
```

```python
import jax
import jax.numpy as jnp
from jax import lax
from jax.experimental import pallas as pl
from jax.experimental.pallas import tpu as pltpu
from jax.sharding import PartitionSpec as P

ITERS = 2
BLOCK_COLS = 384
LEVEL_BLOCK = 24


def tree_sum(values):
    for axis in ("mer", "belt"):
        count = lax.axis_size(axis)
        if count & (count - 1):
            values = lax.psum(values, axis)
            continue
        bit = 1
        while bit < count:
            values = values + lax.ppermute(values, axis, [(i, i ^ bit) for i in range(count)])
            bit *= 2
    return values


def add_totals(part_ref, slots, accs):
    row = lax.broadcasted_iota(jnp.int32, part_ref.shape, 0)
    tile = part_ref[...]
    for slot, acc in zip(slots, accs):
        tile = tile + jnp.where(row == slot, jnp.sum(acc), 0.0)
    part_ref[...] = tile


def tile_spec():
    return pl.BlockSpec((8, 128), lambda j: (0, 0))


def tile_shape():
    return jax.ShapeDtypeStruct((8, 128), jnp.float32)


def row_block(levels, block):
    return pl.BlockSpec((levels, 1, block), lambda j: (0, 0, j))


def row_shape(levels, cols):
    return jax.ShapeDtypeStruct((levels, 1, cols), jnp.float32)


def column_spec(levels, rows, cols):
    return pl.BlockSpec((levels, rows, cols), lambda j: (0, 0, j))


def factor_solve_kernel(h_ref, e_ref, n_ref, v_ref, r_ref, eleft_ref, nsouth_ref,
                        inv_ref, ratio_ref, p_ref, top_ref, bottom_ref, w_ref, s_ref, part_ref):
    levels, rows, cols = h_ref.shape

    @pl.when(pl.program_id(0) == 0)
    def _():
        part_ref[...] = jnp.zeros_like(part_ref)

    zero = jnp.zeros((rows, cols), jnp.float32)
    first_lane = lax.broadcasted_iota(jnp.int32, (rows, cols), 1) == 0
    first_row = lax.broadcasted_iota(jnp.int32, (rows, cols), 0) == 0

    def forward(k, up, down, prev, elim):
        east = e_ref[k]
        north = n_ref[k]
        west = jnp.where(first_lane, jnp.broadcast_to(eleft_ref[k], (rows, cols)),
                         pltpu.roll(east, 1, 1))
        south = jnp.where(first_row, jnp.broadcast_to(nsouth_ref[k], (rows, cols)),
                          pltpu.roll(north, 1, 0))
        w_ref[k] = west
        s_ref[k] = south
        diag = h_ref[k] + east + west + north + south + up + down
        ratio = down / prev
        pivot = diag - down * ratio
        inv_ref[k] = 1.0 / pivot
        ratio_ref[k] = ratio
        elim = r_ref[k] + ratio * elim
        p_ref[k] = elim
        return pivot, elim

    carry = forward(0, v_ref[0], zero, jnp.ones_like(zero), zero)
    carry = lax.fori_loop(
        1, levels - 1, lambda k, c: forward(k, v_ref[k], v_ref[k - 1], *c), carry, unroll=16
    )
    forward(levels - 1, zero, v_ref[levels - 2], *carry)

    def backward(k, up, succ, acc):
        value = inv_ref[k] * (p_ref[k] + up * succ)
        p_ref[k] = value
        top_ref[k] = value[rows - 1:rows]
        bottom_ref[k] = value[:1]
        return value, acc + r_ref[k] * value

    carry = backward(levels - 1, zero, zero, zero)
    carry = lax.fori_loop(
        0, levels - 1, lambda i, c: backward(levels - 2 - i, v_ref[levels - 2 - i], *c), carry,
        unroll=16,
    )
    add_totals(part_ref, (0,), (carry[1],))


def factor_solve(helm_diag, east_coef, north_coef, vert_coef, rhs, east_left, north_south):
    levels, rows, cols = rhs.shape
    block = BLOCK_COLS if cols % BLOCK_COLS == 0 else cols
    full = column_spec(levels, rows, block)
    vspec = column_spec(levels - 1, rows, block)
    field = jax.ShapeDtypeStruct(rhs.shape, jnp.float32)
    return pl.pallas_call(
        factor_solve_kernel,
        grid=(cols // block,),
        in_specs=[full, full, full, vspec, full,
                  pl.BlockSpec((None, levels, rows, 1), lambda j: (j, 0, 0, 0)),
                  pl.BlockSpec((levels, 1, block), lambda j: (0, 0, j))],
        out_specs=[full, full, full, row_block(levels, block), row_block(levels, block),
                   full, full, tile_spec()],
        out_shape=[field, field, field, row_shape(levels, cols), row_shape(levels, cols),
                   field, field, tile_shape()],
    )(helm_diag, east_coef, north_coef, vert_coef, rhs, east_left, north_south)


def solve_kernel(slots, *refs):
    count = len(slots)
    val_ref, inv_ref, ratio_ref, v_ref = refs[:4]
    partner_refs = refs[4:4 + count - 1] + (val_ref,)
    p_ref, top_ref, bottom_ref, part_ref = refs[4 + count - 1:]
    levels = val_ref.shape[0]
    zero = jnp.zeros(val_ref.shape[1:], jnp.float32)

    @pl.when(pl.program_id(0) == 0)
    def _():
        part_ref[...] = jnp.zeros_like(part_ref)

    def forward(k, elim):
        elim = val_ref[k] + ratio_ref[k] * elim
        p_ref[k] = elim
        return elim

    lax.fori_loop(0, levels, forward, zero, unroll=8)

    def backward(k, up, succ, accs):
        value = inv_ref[k] * (p_ref[k] + up * succ)
        p_ref[k] = value
        top_ref[k] = value[value.shape[0] - 1:]
        bottom_ref[k] = value[:1]
        return value, tuple(acc + ref[k] * value for acc, ref in zip(accs, partner_refs))

    carry = backward(levels - 1, zero, zero, (zero,) * count)
    carry = lax.fori_loop(
        0, levels - 1, lambda i, c: backward(levels - 2 - i, v_ref[levels - 2 - i], *c), carry,
        unroll=8,
    )
    add_totals(part_ref, slots, carry[1])


def solve(values, inverse_pivot, ratio_values, vert_coef, partners, slots):
    levels, rows, cols = values.shape
    block = BLOCK_COLS if cols % BLOCK_COLS == 0 else cols
    full = column_spec(levels, rows, block)
    vspec = column_spec(levels - 1, rows, block)
    return pl.pallas_call(
        lambda *refs: solve_kernel(slots, *refs),
        grid=(cols // block,),
        in_specs=[full, full, full, vspec] + [full] * len(partners),
        out_specs=[full, row_block(levels, block), row_block(levels, block), tile_spec()],
        out_shape=[jax.ShapeDtypeStruct(values.shape, jnp.float32), row_shape(levels, cols),
                   row_shape(levels, cols), tile_shape()],
    )(values, inverse_pivot, ratio_values, vert_coef, *partners)


def edge_tables(edge_num, row_start, rows, weight_index, edge_map, mortar_weights):
    maps = lax.dynamic_slice_in_dim(edge_map[edge_num], row_start, rows, 0)
    picks = lax.dynamic_slice_in_dim(weight_index[edge_num], row_start, rows, 0)
    return (maps[:, 0], maps[:, 1], mortar_weights[picks, 0], mortar_weights[picks, 1])


def belt_cols(field):
    count = lax.axis_size("belt")
    first = jnp.transpose(field[:, :, 0])
    last = jnp.transpose(field[:, :, -1])
    west = lax.ppermute(last, "belt", [(i, (i + 1) % count) for i in range(count)])
    east = lax.ppermute(first, "belt", [((i + 1) % count, i) for i in range(count)])
    return west, east


def mer_rows(top, bottom):
    count = lax.axis_size("mer")
    south = lax.ppermute(top, "mer", [(i, i + 1) for i in range(count - 1)])
    north = lax.ppermute(bottom, "mer", [(i + 1, i) for i in range(count - 1)])
    return south, north


def gather_rows(column):
    count = lax.axis_size("mer")
    if count & (count - 1):
        return lax.all_gather(column, "mer", axis=0, tiled=True)
    me = lax.axis_index("mer")
    bit = 1
    while bit < count:
        other = lax.ppermute(column, "mer", [(i, i ^ bit) for i in range(count)])
        low_half = (me & bit) == 0
        column = jnp.concatenate(
            [jnp.where(low_half, column, other), jnp.where(low_half, other, column)], axis=0
        )
        bit *= 2
    return column


def as_lane_column(cols):
    return jnp.transpose(cols)[:, :, None]


def operator_kernel(slots, *refs):
    extra = len(slots) - 1
    (v_ref, vab_ref, vbe_ref, h_ref, e_ref, n_ref, up_ref, upb_ref, ew_ref, ns_ref,
     ve_ref, vw_ref, vn_ref, vs_ref) = refs[:14]
    partner_refs = (v_ref,) + refs[14:14 + extra]
    img_ref, part_ref = refs[14 + extra:]
    block, rows, cols = v_ref.shape
    i = pl.program_id(0)
    last_block = pl.num_programs(0) - 1
    lane = lax.broadcasted_iota(jnp.int32, (rows, cols), 1)
    row = lax.broadcasted_iota(jnp.int32, (rows, cols), 0)
    first_lane, last_lane = lane == 0, lane == cols - 1
    first_row, last_row = row == 0, row == rows - 1
    zero = jnp.zeros((rows, cols), jnp.float32)
    above = jnp.where(i == last_block, zero, vab_ref[0])
    below = jnp.where(i == 0, zero, vbe_ref[0])
    up_below = jnp.where(i == 0, zero, upb_ref[0])

    @pl.when(i == 0)
    def _():
        part_ref[...] = jnp.zeros_like(part_ref)

    edge = min(cols, 128)
    lane_e = lax.broadcasted_iota(jnp.int32, (rows, edge), 1)

    def first_tile(halo_ref, k, rolled):
        fixed = jnp.where(lane_e == 0, jnp.broadcast_to(halo_ref[k], (rows, edge)), rolled[:, :edge])
        return jnp.concatenate([fixed, rolled[:, edge:]], axis=1) if cols > edge else fixed

    def last_tile(halo_ref, k, rolled):
        fixed = jnp.where(lane_e == edge - 1, jnp.broadcast_to(halo_ref[k], (rows, edge)),
                          rolled[:, cols - edge:])
        return jnp.concatenate([rolled[:, :cols - edge], fixed], axis=1) if cols > edge else fixed

    def level(k, up_side, down_side, lower, accs):
        v = v_ref[k]
        east_side = last_tile(ve_ref, k, pltpu.roll(v, cols - 1, 1))
        west_side = first_tile(vw_ref, k, pltpu.roll(v, 1, 1))
        north_side = jnp.where(last_row, jnp.broadcast_to(vn_ref[k], (rows, cols)),
                               pltpu.roll(v, rows - 1, 0))
        south_side = jnp.where(first_row, jnp.broadcast_to(vs_ref[k], (rows, cols)),
                               pltpu.roll(v, 1, 0))
        east = e_ref[k]
        north = n_ref[k]
        west = ew_ref[k]
        south = ns_ref[k]
        image = (
            h_ref[k] * v
            + east * (v - east_side)
            + west * (v - west_side)
            + north * (v - north_side)
            + south * (v - south_side)
            + up_ref[k] * (v - up_side)
            + lower * (v - down_side)
        )
        img_ref[k] = image
        return tuple(acc + ref[k] * image for acc, ref in zip(accs, partner_refs))

    accs = (zero,) * len(slots)
    if block == 1:
        accs = level(0, above, below, up_below, accs)
    else:
        accs = level(0, v_ref[1], below, up_below, accs)
        accs = lax.fori_loop(
            1, block - 1,
            lambda k, c: level(k, v_ref[k + 1], v_ref[k - 1], up_ref[k - 1], c), accs,
            unroll=8,
        )
        accs = level(block - 1, above, v_ref[block - 2], up_ref[block - 2], accs)
    add_totals(part_ref, slots, accs)


def apply_operator(direction, coefs, halos, slots, extra=()):
    helm_diag, east_coef, north_coef, upper, east_west, north_south = coefs
    east_halo, west_halo, north_halo, south_halo = halos
    levels, rows, cols = direction.shape
    block = LEVEL_BLOCK if levels % LEVEL_BLOCK == 0 else levels
    blocks = levels // block
    full = pl.BlockSpec((block, rows, cols), lambda i: (i, 0, 0))
    lane_col = pl.BlockSpec((block, rows, 1), lambda i: (i, 0, 0))
    row_spec = pl.BlockSpec((block, 1, cols), lambda i: (i, 0, 0))
    above = pl.BlockSpec((1, rows, cols), lambda i: (jnp.minimum((i + 1) * block, levels - 1), 0, 0))
    below = pl.BlockSpec((1, rows, cols), lambda i: (jnp.maximum(i * block - 1, 0), 0, 0))
    kernel = lambda *refs: operator_kernel(slots, *refs)
    image, part = pl.pallas_call(
        kernel,
        grid=(blocks,),
        in_specs=[full, above, below, full, full, full, full, below, full, full,
                  lane_col, lane_col, row_spec, row_spec] + [full] * len(extra),
        out_specs=[full, tile_spec()],
        out_shape=[jax.ShapeDtypeStruct(direction.shape, jnp.float32), tile_shape()],
    )(direction, direction, direction, helm_diag, east_coef, north_coef, upper, upper,
      east_west, north_south, east_halo, west_halo, north_halo, south_halo, *extra)
    return image, part


def finish_kernel(sums_ref, p0_ref, q_ref, r0_ref, a0_ref, aq_ref, sol_ref, res_ref):
    block, rows, cols = p0_ref.shape
    sums = sums_ref[...]
    norm0, curv0, r0q, a0q, qaq, p0aq = (
        jnp.broadcast_to(sums[j:j + 1, :], sums.shape) for j in range(6)
    )
    step0 = norm0 / curv0
    norm1 = norm0 - step0 * (r0q + curv0) + step0 * step0 * a0q
    p1ap1 = curv0 - step0 * (p0aq + a0q) + step0 * step0 * qaq
    p1a0 = curv0 - step0 * a0q
    d0ap1 = curv0 - step0 * p0aq
    beta = norm1 / norm0
    curv1 = p1ap1 + beta * (p1a0 + d0ap1) + beta * beta * curv0
    step1 = norm1 / curv1
    widen = lambda x: jnp.concatenate([x[:rows]] * (cols // x.shape[1]), axis=1)
    step0, beta, step1 = widen(step0), widen(beta), widen(step1)

    def level(k, carry):
        p0 = p0_ref[k]
        a0 = a0_ref[k]
        precond1 = p0 - step0 * q_ref[k]
        direction1 = precond1 + beta * p0
        image1 = (a0 - step0 * aq_ref[k]) + beta * a0
        sol_ref[k] = step0 * p0 + step1 * direction1
        res_ref[k] = (r0_ref[k] - step0 * a0) - step1 * image1
        return carry

    lax.fori_loop(0, block, level, 0, unroll=2)


def finish(sums, precond0, basis, right_side, image0, image_q):
    levels, rows, cols = precond0.shape
    block = LEVEL_BLOCK if levels % LEVEL_BLOCK == 0 else levels
    full = pl.BlockSpec((block, rows, cols), lambda i: (i, 0, 0))
    field = jax.ShapeDtypeStruct(precond0.shape, jnp.float32)
    return pl.pallas_call(
        finish_kernel,
        grid=(levels // block,),
        in_specs=[tile_spec(), full, full, full, full, full],
        out_specs=[full, full],
        out_shape=[field, field],
    )(sums, precond0, basis, right_side, image0, image_q)


def exchange(direction, top, bottom, tables, use_mortar):
    count = lax.axis_size("belt")
    east = lax.ppermute(jnp.transpose(direction[:, :, 0]), "belt",
                        [((i + 1) % count, i) for i in range(count)])
    whole = gather_rows(east)
    west = lax.ppermute(jnp.transpose(direction[:, :, -1]), "belt",
                        [(i, (i + 1) % count) for i in range(count)])
    south, north = mer_rows(top, bottom)
    first_map, second_map, first_weight, second_weight = tables
    arrived = first_weight[:, None] * whole[first_map] + second_weight[:, None] * whole[second_map]
    east = jnp.where(use_mortar, arrived, east)
    return as_lane_column(east), as_lane_column(west), north, south


def on_device(
    right_side,
    helm_diag,
    east_coef,
    north_coef,
    vert_coef,
    mortar_weights,
    weight_index,
    edge_map,
    refined,
):
    belt_index = lax.axis_index("belt")
    mer_index = lax.axis_index("mer")
    per_panel = lax.axis_size("belt") // 4
    rows = right_side.shape[1]
    row_start = mer_index * rows
    own_edge = belt_index // per_panel
    row_flags = lax.dynamic_slice_in_dim(refined[own_edge], row_start, rows, 0)
    at_edge = (belt_index + 1) % per_panel == 0
    use_mortar = jnp.logical_and(at_edge, row_flags == 1)[:, None]
    tables = edge_tables(own_edge, row_start, rows, weight_index, edge_map, mortar_weights)
    levels, _, cols = right_side.shape
    block = BLOCK_COLS if cols % BLOCK_COLS == 0 else cols
    coef_west, _ = belt_cols(east_coef)
    coef_south, _ = mer_rows(north_coef[:, -1:, :], north_coef[:, :1, :])
    east_left = jnp.stack(
        [jnp.transpose(coef_west)]
        + [east_coef[:, :, j * block - 1] for j in range(1, cols // block)],
        axis=0,
    )[..., None]
    upper = jnp.concatenate([vert_coef, jnp.zeros_like(vert_coef[:1])], axis=0)

    inverse_pivot, ratio_values, precond0, top0, bottom0, west_coef, south_coef, part0 = (
        factor_solve(helm_diag, east_coef, north_coef, vert_coef, right_side, east_left, coef_south)
    )
    coefs = (helm_diag, east_coef, north_coef, upper, west_coef, south_coef)
    image0, curv_part0 = apply_operator(
        precond0, coefs, exchange(precond0, top0, bottom0, tables, use_mortar), (1,)
    )
    basis, top_q, bottom_q, basis_part = solve(
        image0, inverse_pivot, ratio_values, vert_coef, (right_side,), (2, 3)
    )
    image_q, image_q_part = apply_operator(
        basis, coefs, exchange(basis, top_q, bottom_q, tables, use_mortar), (4, 5), (precond0,)
    )
    sums = tree_sum(part0 + curv_part0 + basis_part + image_q_part)
    return finish(sums, precond0, basis, right_side, image0, image_q)


def solution(mesh):
    placed = (
        P(None, "mer", "belt"),
        P(None, "mer", "belt"),
        P(None, "mer", "belt"),
        P(None, "mer", "belt"),
        P(None, "mer", "belt"),
        P(),
        P(),
        P(),
        P(),
    )
    return jax.shard_map(
        on_device,
        mesh=mesh,
        in_specs=placed,
        out_specs=(P(None, "mer", "belt"), P(None, "mer", "belt")),
        check_vma=False,
    )
```

```python
import jax
import jax.numpy as jnp
from jax import lax
from jax.experimental import pallas as pl
from jax.experimental.pallas import tpu as pltpu
from jax.sharding import PartitionSpec as P

ITERS = 2
BLOCK_COLS = 384
LEVEL_BLOCK = 24


def tree_sum(values):
    for axis in ("mer", "belt"):
        count = lax.axis_size(axis)
        if count & (count - 1):
            values = lax.psum(values, axis)
            continue
        bit = 1
        while bit < count:
            values = values + lax.ppermute(values, axis, [(i, i ^ bit) for i in range(count)])
            bit *= 2
    return values


def add_totals(part_ref, slots, accs):
    row = lax.broadcasted_iota(jnp.int32, part_ref.shape, 0)
    tile = part_ref[...]
    for slot, acc in zip(slots, accs):
        tile = tile + jnp.where(row == slot, jnp.sum(acc), 0.0)
    part_ref[...] = tile


def tile_spec():
    return pl.BlockSpec((8, 128), lambda j: (0, 0))


def tile_shape():
    return jax.ShapeDtypeStruct((8, 128), jnp.float32)


def row_block(levels, block):
    return pl.BlockSpec((levels, 1, block), lambda j: (0, 0, j))


def row_shape(levels, cols):
    return jax.ShapeDtypeStruct((levels, 1, cols), jnp.float32)


def column_spec(levels, rows, cols):
    return pl.BlockSpec((levels, rows, cols), lambda j: (0, 0, j))


def factor_solve_kernel(h_ref, e_ref, n_ref, v_ref, r_ref, eleft_ref, nsouth_ref,
                        inv_ref, ratio_ref, p_ref, top_ref, bottom_ref, w_ref, s_ref, part_ref):
    levels, rows, cols = h_ref.shape

    @pl.when(pl.program_id(0) == 0)
    def _():
        part_ref[...] = jnp.zeros_like(part_ref)

    zero = jnp.zeros((rows, cols), jnp.float32)
    first_lane = lax.broadcasted_iota(jnp.int32, (rows, cols), 1) == 0
    first_row = lax.broadcasted_iota(jnp.int32, (rows, cols), 0) == 0

    def forward(k, up, down, prev, elim):
        east = e_ref[k]
        north = n_ref[k]
        west = jnp.where(first_lane, jnp.broadcast_to(eleft_ref[k], (rows, cols)),
                         pltpu.roll(east, 1, 1))
        south = jnp.where(first_row, jnp.broadcast_to(nsouth_ref[k], (rows, cols)),
                          pltpu.roll(north, 1, 0))
        w_ref[k] = west
        s_ref[k] = south
        diag = h_ref[k] + east + west + north + south + up + down
        ratio = down / prev
        pivot = diag - down * ratio
        inv_ref[k] = 1.0 / pivot
        ratio_ref[k] = ratio
        elim = r_ref[k] + ratio * elim
        p_ref[k] = elim
        return pivot, elim

    carry = forward(0, v_ref[0], zero, jnp.ones_like(zero), zero)
    carry = lax.fori_loop(
        1, levels - 1, lambda k, c: forward(k, v_ref[k], v_ref[k - 1], *c), carry, unroll=16
    )
    forward(levels - 1, zero, v_ref[levels - 2], *carry)

    def backward(k, up, succ, acc):
        value = inv_ref[k] * (p_ref[k] + up * succ)
        p_ref[k] = value
        top_ref[k] = value[rows - 1:rows]
        bottom_ref[k] = value[:1]
        return value, acc + r_ref[k] * value

    carry = backward(levels - 1, zero, zero, zero)
    carry = lax.fori_loop(
        0, levels - 1, lambda i, c: backward(levels - 2 - i, v_ref[levels - 2 - i], *c), carry,
        unroll=16,
    )
    add_totals(part_ref, (0,), (carry[1],))


def factor_solve(helm_diag, east_coef, north_coef, vert_coef, rhs, east_left, north_south):
    levels, rows, cols = rhs.shape
    block = BLOCK_COLS if cols % BLOCK_COLS == 0 else cols
    full = column_spec(levels, rows, block)
    vspec = column_spec(levels - 1, rows, block)
    field = jax.ShapeDtypeStruct(rhs.shape, jnp.float32)
    return pl.pallas_call(
        factor_solve_kernel,
        grid=(cols // block,),
        in_specs=[full, full, full, vspec, full,
                  pl.BlockSpec((None, levels, rows, 1), lambda j: (j, 0, 0, 0)),
                  pl.BlockSpec((levels, 1, block), lambda j: (0, 0, j))],
        out_specs=[full, full, full, row_block(levels, block), row_block(levels, block),
                   full, full, tile_spec()],
        out_shape=[field, field, field, row_shape(levels, cols), row_shape(levels, cols),
                   field, field, tile_shape()],
    )(helm_diag, east_coef, north_coef, vert_coef, rhs, east_left, north_south)


def solve_kernel(slots, *refs):
    count = len(slots)
    val_ref, inv_ref, ratio_ref, v_ref = refs[:4]
    partner_refs = refs[4:4 + count - 1] + (val_ref,)
    p_ref, top_ref, bottom_ref, part_ref = refs[4 + count - 1:]
    levels = val_ref.shape[0]
    zero = jnp.zeros(val_ref.shape[1:], jnp.float32)

    @pl.when(pl.program_id(0) == 0)
    def _():
        part_ref[...] = jnp.zeros_like(part_ref)

    def forward(k, elim):
        elim = val_ref[k] + ratio_ref[k] * elim
        p_ref[k] = elim
        return elim

    lax.fori_loop(0, levels, forward, zero, unroll=16)

    def backward(k, up, succ, accs):
        value = inv_ref[k] * (p_ref[k] + up * succ)
        p_ref[k] = value
        top_ref[k] = value[value.shape[0] - 1:]
        bottom_ref[k] = value[:1]
        return value, tuple(acc + ref[k] * value for acc, ref in zip(accs, partner_refs))

    carry = backward(levels - 1, zero, zero, (zero,) * count)
    carry = lax.fori_loop(
        0, levels - 1, lambda i, c: backward(levels - 2 - i, v_ref[levels - 2 - i], *c), carry,
        unroll=16,
    )
    add_totals(part_ref, slots, carry[1])


def solve(values, inverse_pivot, ratio_values, vert_coef, partners, slots):
    levels, rows, cols = values.shape
    block = BLOCK_COLS if cols % BLOCK_COLS == 0 else cols
    full = column_spec(levels, rows, block)
    vspec = column_spec(levels - 1, rows, block)
    return pl.pallas_call(
        lambda *refs: solve_kernel(slots, *refs),
        grid=(cols // block,),
        in_specs=[full, full, full, vspec] + [full] * len(partners),
        out_specs=[full, row_block(levels, block), row_block(levels, block), tile_spec()],
        out_shape=[jax.ShapeDtypeStruct(values.shape, jnp.float32), row_shape(levels, cols),
                   row_shape(levels, cols), tile_shape()],
    )(values, inverse_pivot, ratio_values, vert_coef, *partners)


def edge_tables(edge_num, row_start, rows, weight_index, edge_map, mortar_weights):
    maps = lax.dynamic_slice_in_dim(edge_map[edge_num], row_start, rows, 0)
    picks = lax.dynamic_slice_in_dim(weight_index[edge_num], row_start, rows, 0)
    return (maps[:, 0], maps[:, 1], mortar_weights[picks, 0], mortar_weights[picks, 1])


def belt_cols(field):
    count = lax.axis_size("belt")
    first = jnp.transpose(field[:, :, 0])
    last = jnp.transpose(field[:, :, -1])
    west = lax.ppermute(last, "belt", [(i, (i + 1) % count) for i in range(count)])
    east = lax.ppermute(first, "belt", [((i + 1) % count, i) for i in range(count)])
    return west, east


def mer_rows(top, bottom):
    count = lax.axis_size("mer")
    south = lax.ppermute(top, "mer", [(i, i + 1) for i in range(count - 1)])
    north = lax.ppermute(bottom, "mer", [(i + 1, i) for i in range(count - 1)])
    return south, north


def gather_rows(column):
    count = lax.axis_size("mer")
    if count & (count - 1):
        return lax.all_gather(column, "mer", axis=0, tiled=True)
    me = lax.axis_index("mer")
    bit = 1
    while bit < count:
        other = lax.ppermute(column, "mer", [(i, i ^ bit) for i in range(count)])
        low_half = (me & bit) == 0
        column = jnp.concatenate(
            [jnp.where(low_half, column, other), jnp.where(low_half, other, column)], axis=0
        )
        bit *= 2
    return column


def as_lane_column(cols):
    return jnp.transpose(cols)[:, :, None]


def operator_kernel(slots, *refs):
    extra = len(slots) - 1
    (v_ref, vab_ref, vbe_ref, h_ref, e_ref, n_ref, up_ref, upb_ref, ew_ref, ns_ref,
     ve_ref, vw_ref, vn_ref, vs_ref) = refs[:14]
    partner_refs = (v_ref,) + refs[14:14 + extra]
    img_ref, part_ref = refs[14 + extra:]
    block, rows, cols = v_ref.shape
    i = pl.program_id(0)
    last_block = pl.num_programs(0) - 1
    lane = lax.broadcasted_iota(jnp.int32, (rows, cols), 1)
    row = lax.broadcasted_iota(jnp.int32, (rows, cols), 0)
    first_lane, last_lane = lane == 0, lane == cols - 1
    first_row, last_row = row == 0, row == rows - 1
    zero = jnp.zeros((rows, cols), jnp.float32)
    above = jnp.where(i == last_block, zero, vab_ref[0])
    below = jnp.where(i == 0, zero, vbe_ref[0])
    up_below = jnp.where(i == 0, zero, upb_ref[0])

    @pl.when(i == 0)
    def _():
        part_ref[...] = jnp.zeros_like(part_ref)

    edge = min(cols, 128)
    lane_e = lax.broadcasted_iota(jnp.int32, (rows, edge), 1)

    def first_tile(halo_ref, k, rolled):
        fixed = jnp.where(lane_e == 0, jnp.broadcast_to(halo_ref[k], (rows, edge)), rolled[:, :edge])
        return jnp.concatenate([fixed, rolled[:, edge:]], axis=1) if cols > edge else fixed

    def last_tile(halo_ref, k, rolled):
        fixed = jnp.where(lane_e == edge - 1, jnp.broadcast_to(halo_ref[k], (rows, edge)),
                          rolled[:, cols - edge:])
        return jnp.concatenate([rolled[:, :cols - edge], fixed], axis=1) if cols > edge else fixed

    def level(k, up_side, down_side, lower, accs):
        v = v_ref[k]
        east_side = last_tile(ve_ref, k, pltpu.roll(v, cols - 1, 1))
        west_side = first_tile(vw_ref, k, pltpu.roll(v, 1, 1))
        north_side = jnp.where(last_row, jnp.broadcast_to(vn_ref[k], (rows, cols)),
                               pltpu.roll(v, rows - 1, 0))
        south_side = jnp.where(first_row, jnp.broadcast_to(vs_ref[k], (rows, cols)),
                               pltpu.roll(v, 1, 0))
        east = e_ref[k]
        north = n_ref[k]
        west = ew_ref[k]
        south = ns_ref[k]
        image = (
            h_ref[k] * v
            + east * (v - east_side)
            + west * (v - west_side)
            + north * (v - north_side)
            + south * (v - south_side)
            + up_ref[k] * (v - up_side)
            + lower * (v - down_side)
        )
        img_ref[k] = image
        return tuple(acc + ref[k] * image for acc, ref in zip(accs, partner_refs))

    accs = (zero,) * len(slots)
    if block == 1:
        accs = level(0, above, below, up_below, accs)
    else:
        accs = level(0, v_ref[1], below, up_below, accs)
        accs = lax.fori_loop(
            1, block - 1,
            lambda k, c: level(k, v_ref[k + 1], v_ref[k - 1], up_ref[k - 1], c), accs,
            unroll=4,
        )
        accs = level(block - 1, above, v_ref[block - 2], up_ref[block - 2], accs)
    add_totals(part_ref, slots, accs)


def apply_operator(direction, coefs, halos, slots, extra=()):
    helm_diag, east_coef, north_coef, upper, east_west, north_south = coefs
    east_halo, west_halo, north_halo, south_halo = halos
    levels, rows, cols = direction.shape
    block = LEVEL_BLOCK if levels % LEVEL_BLOCK == 0 else levels
    blocks = levels // block
    full = pl.BlockSpec((block, rows, cols), lambda i: (i, 0, 0))
    lane_col = pl.BlockSpec((block, rows, 1), lambda i: (i, 0, 0))
    row_spec = pl.BlockSpec((block, 1, cols), lambda i: (i, 0, 0))
    above = pl.BlockSpec((1, rows, cols), lambda i: (jnp.minimum((i + 1) * block, levels - 1), 0, 0))
    below = pl.BlockSpec((1, rows, cols), lambda i: (jnp.maximum(i * block - 1, 0), 0, 0))
    kernel = lambda *refs: operator_kernel(slots, *refs)
    image, part = pl.pallas_call(
        kernel,
        grid=(blocks,),
        in_specs=[full, above, below, full, full, full, full, below, full, full,
                  lane_col, lane_col, row_spec, row_spec] + [full] * len(extra),
        out_specs=[full, tile_spec()],
        out_shape=[jax.ShapeDtypeStruct(direction.shape, jnp.float32), tile_shape()],
    )(direction, direction, direction, helm_diag, east_coef, north_coef, upper, upper,
      east_west, north_south, east_halo, west_halo, north_halo, south_halo, *extra)
    return image, part


def finish_kernel(sums_ref, p0_ref, q_ref, r0_ref, a0_ref, aq_ref, sol_ref, res_ref):
    block, rows, cols = p0_ref.shape
    sums = sums_ref[...]
    norm0, curv0, r0q, a0q, qaq, p0aq = (
        jnp.broadcast_to(sums[j:j + 1, :], sums.shape) for j in range(6)
    )
    step0 = norm0 / curv0
    norm1 = norm0 - step0 * (r0q + curv0) + step0 * step0 * a0q
    p1ap1 = curv0 - step0 * (p0aq + a0q) + step0 * step0 * qaq
    p1a0 = curv0 - step0 * a0q
    d0ap1 = curv0 - step0 * p0aq
    beta = norm1 / norm0
    curv1 = p1ap1 + beta * (p1a0 + d0ap1) + beta * beta * curv0
    step1 = norm1 / curv1
    widen = lambda x: jnp.concatenate([x[:rows]] * (cols // x.shape[1]), axis=1)
    step0, beta, step1 = widen(step0), widen(beta), widen(step1)

    def level(k, carry):
        p0 = p0_ref[k]
        a0 = a0_ref[k]
        precond1 = p0 - step0 * q_ref[k]
        direction1 = precond1 + beta * p0
        image1 = (a0 - step0 * aq_ref[k]) + beta * a0
        sol_ref[k] = step0 * p0 + step1 * direction1
        res_ref[k] = (r0_ref[k] - step0 * a0) - step1 * image1
        return carry

    lax.fori_loop(0, block, level, 0, unroll=2)


def finish(sums, precond0, basis, right_side, image0, image_q):
    levels, rows, cols = precond0.shape
    block = LEVEL_BLOCK if levels % LEVEL_BLOCK == 0 else levels
    full = pl.BlockSpec((block, rows, cols), lambda i: (i, 0, 0))
    field = jax.ShapeDtypeStruct(precond0.shape, jnp.float32)
    return pl.pallas_call(
        finish_kernel,
        grid=(levels // block,),
        in_specs=[tile_spec(), full, full, full, full, full],
        out_specs=[full, full],
        out_shape=[field, field],
    )(sums, precond0, basis, right_side, image0, image_q)


def exchange(direction, top, bottom, tables, use_mortar):
    count = lax.axis_size("belt")
    east = lax.ppermute(jnp.transpose(direction[:, :, 0]), "belt",
                        [((i + 1) % count, i) for i in range(count)])
    whole = gather_rows(east)
    west = lax.ppermute(jnp.transpose(direction[:, :, -1]), "belt",
                        [(i, (i + 1) % count) for i in range(count)])
    south, north = mer_rows(top, bottom)
    first_map, second_map, first_weight, second_weight = tables
    arrived = first_weight[:, None] * whole[first_map] + second_weight[:, None] * whole[second_map]
    east = jnp.where(use_mortar, arrived, east)
    return as_lane_column(east), as_lane_column(west), north, south


def on_device(
    right_side,
    helm_diag,
    east_coef,
    north_coef,
    vert_coef,
    mortar_weights,
    weight_index,
    edge_map,
    refined,
):
    belt_index = lax.axis_index("belt")
    mer_index = lax.axis_index("mer")
    per_panel = lax.axis_size("belt") // 4
    rows = right_side.shape[1]
    row_start = mer_index * rows
    own_edge = belt_index // per_panel
    row_flags = lax.dynamic_slice_in_dim(refined[own_edge], row_start, rows, 0)
    at_edge = (belt_index + 1) % per_panel == 0
    use_mortar = jnp.logical_and(at_edge, row_flags == 1)[:, None]
    tables = edge_tables(own_edge, row_start, rows, weight_index, edge_map, mortar_weights)
    levels, _, cols = right_side.shape
    block = BLOCK_COLS if cols % BLOCK_COLS == 0 else cols
    coef_west, _ = belt_cols(east_coef)
    coef_south, _ = mer_rows(north_coef[:, -1:, :], north_coef[:, :1, :])
    east_left = jnp.stack(
        [jnp.transpose(coef_west)]
        + [east_coef[:, :, j * block - 1] for j in range(1, cols // block)],
        axis=0,
    )[..., None]
    upper = jnp.concatenate([vert_coef, jnp.zeros_like(vert_coef[:1])], axis=0)

    inverse_pivot, ratio_values, precond0, top0, bottom0, west_coef, south_coef, part0 = (
        factor_solve(helm_diag, east_coef, north_coef, vert_coef, right_side, east_left, coef_south)
    )
    coefs = (helm_diag, east_coef, north_coef, upper, west_coef, south_coef)
    image0, curv_part0 = apply_operator(
        precond0, coefs, exchange(precond0, top0, bottom0, tables, use_mortar), (1,)
    )
    basis, top_q, bottom_q, basis_part = solve(
        image0, inverse_pivot, ratio_values, vert_coef, (right_side,), (2, 3)
    )
    image_q, image_q_part = apply_operator(
        basis, coefs, exchange(basis, top_q, bottom_q, tables, use_mortar), (4, 5), (precond0,)
    )
    sums = tree_sum(part0 + curv_part0 + basis_part + image_q_part)
    return finish(sums, precond0, basis, right_side, image0, image_q)


def solution(mesh):
    placed = (
        P(None, "mer", "belt"),
        P(None, "mer", "belt"),
        P(None, "mer", "belt"),
        P(None, "mer", "belt"),
        P(None, "mer", "belt"),
        P(),
        P(),
        P(),
        P(),
    )
    return jax.shard_map(
        on_device,
        mesh=mesh,
        in_specs=placed,
        out_specs=(P(None, "mer", "belt"), P(None, "mer", "belt")),
        check_vma=False,
    )
```

```python
import jax
import jax.numpy as jnp
from jax import lax
from jax.experimental import pallas as pl
from jax.experimental.pallas import tpu as pltpu
from jax.sharding import PartitionSpec as P

ITERS = 2
BLOCK_COLS = 384
LEVEL_BLOCK = 40


def tree_sum(values):
    for axis in ("mer", "belt"):
        count = lax.axis_size(axis)
        if count & (count - 1):
            values = lax.psum(values, axis)
            continue
        bit = 1
        while bit < count:
            values = values + lax.ppermute(values, axis, [(i, i ^ bit) for i in range(count)])
            bit *= 2
    return values


def add_totals(part_ref, slots, accs):
    row = lax.broadcasted_iota(jnp.int32, part_ref.shape, 0)
    tile = part_ref[...]
    for slot, acc in zip(slots, accs):
        tile = tile + jnp.where(row == slot, jnp.sum(acc), 0.0)
    part_ref[...] = tile


def tile_spec():
    return pl.BlockSpec((8, 128), lambda j: (0, 0))


def tile_shape():
    return jax.ShapeDtypeStruct((8, 128), jnp.float32)


def row_block(levels, block):
    return pl.BlockSpec((levels, 1, block), lambda j: (0, 0, j))


def row_shape(levels, cols):
    return jax.ShapeDtypeStruct((levels, 1, cols), jnp.float32)


def column_spec(levels, rows, cols):
    return pl.BlockSpec((levels, rows, cols), lambda j: (0, 0, j))


def factor_solve_kernel(h_ref, e_ref, n_ref, v_ref, r_ref, eleft_ref, nsouth_ref,
                        inv_ref, ratio_ref, p_ref, top_ref, bottom_ref, w_ref, s_ref, part_ref):
    levels, rows, cols = h_ref.shape

    @pl.when(pl.program_id(0) == 0)
    def _():
        part_ref[...] = jnp.zeros_like(part_ref)

    zero = jnp.zeros((rows, cols), jnp.float32)
    first_lane = lax.broadcasted_iota(jnp.int32, (rows, cols), 1) == 0
    first_row = lax.broadcasted_iota(jnp.int32, (rows, cols), 0) == 0

    def forward(k, up, down, prev, elim):
        east = e_ref[k]
        north = n_ref[k]
        west = jnp.where(first_lane, jnp.broadcast_to(eleft_ref[k], (rows, cols)),
                         pltpu.roll(east, 1, 1))
        south = jnp.where(first_row, jnp.broadcast_to(nsouth_ref[k], (rows, cols)),
                          pltpu.roll(north, 1, 0))
        w_ref[k] = west
        s_ref[k] = south
        diag = h_ref[k] + east + west + north + south + up + down
        ratio = down / prev
        pivot = diag - down * ratio
        inv_ref[k] = 1.0 / pivot
        ratio_ref[k] = ratio
        elim = r_ref[k] + ratio * elim
        p_ref[k] = elim
        return pivot, elim

    carry = forward(0, v_ref[0], zero, jnp.ones_like(zero), zero)
    carry = lax.fori_loop(
        1, levels - 1, lambda k, c: forward(k, v_ref[k], v_ref[k - 1], *c), carry, unroll=16
    )
    forward(levels - 1, zero, v_ref[levels - 2], *carry)

    def backward(k, up, succ, acc):
        value = inv_ref[k] * (p_ref[k] + up * succ)
        p_ref[k] = value
        top_ref[k] = value[rows - 1:rows]
        bottom_ref[k] = value[:1]
        return value, acc + r_ref[k] * value

    carry = backward(levels - 1, zero, zero, zero)
    carry = lax.fori_loop(
        0, levels - 1, lambda i, c: backward(levels - 2 - i, v_ref[levels - 2 - i], *c), carry,
        unroll=16,
    )
    add_totals(part_ref, (0,), (carry[1],))


def factor_solve(helm_diag, east_coef, north_coef, vert_coef, rhs, east_left, north_south):
    levels, rows, cols = rhs.shape
    block = BLOCK_COLS if cols % BLOCK_COLS == 0 else cols
    full = column_spec(levels, rows, block)
    vspec = column_spec(levels - 1, rows, block)
    field = jax.ShapeDtypeStruct(rhs.shape, jnp.float32)
    return pl.pallas_call(
        factor_solve_kernel,
        grid=(cols // block,),
        in_specs=[full, full, full, vspec, full,
                  pl.BlockSpec((None, levels, rows, 1), lambda j: (j, 0, 0, 0)),
                  pl.BlockSpec((levels, 1, block), lambda j: (0, 0, j))],
        out_specs=[full, full, full, row_block(levels, block), row_block(levels, block),
                   full, full, tile_spec()],
        out_shape=[field, field, field, row_shape(levels, cols), row_shape(levels, cols),
                   field, field, tile_shape()],
    )(helm_diag, east_coef, north_coef, vert_coef, rhs, east_left, north_south)


def solve_kernel(slots, *refs):
    count = len(slots)
    val_ref, inv_ref, ratio_ref, v_ref = refs[:4]
    partner_refs = refs[4:4 + count - 1] + (val_ref,)
    p_ref, top_ref, bottom_ref, part_ref = refs[4 + count - 1:]
    levels = val_ref.shape[0]
    zero = jnp.zeros(val_ref.shape[1:], jnp.float32)

    @pl.when(pl.program_id(0) == 0)
    def _():
        part_ref[...] = jnp.zeros_like(part_ref)

    def forward(k, elim):
        elim = val_ref[k] + ratio_ref[k] * elim
        p_ref[k] = elim
        return elim

    lax.fori_loop(0, levels, forward, zero, unroll=16)

    def backward(k, up, succ, accs):
        value = inv_ref[k] * (p_ref[k] + up * succ)
        p_ref[k] = value
        top_ref[k] = value[value.shape[0] - 1:]
        bottom_ref[k] = value[:1]
        return value, tuple(acc + ref[k] * value for acc, ref in zip(accs, partner_refs))

    carry = backward(levels - 1, zero, zero, (zero,) * count)
    carry = lax.fori_loop(
        0, levels - 1, lambda i, c: backward(levels - 2 - i, v_ref[levels - 2 - i], *c), carry,
        unroll=16,
    )
    add_totals(part_ref, slots, carry[1])


def solve(values, inverse_pivot, ratio_values, vert_coef, partners, slots):
    levels, rows, cols = values.shape
    block = BLOCK_COLS if cols % BLOCK_COLS == 0 else cols
    full = column_spec(levels, rows, block)
    vspec = column_spec(levels - 1, rows, block)
    return pl.pallas_call(
        lambda *refs: solve_kernel(slots, *refs),
        grid=(cols // block,),
        in_specs=[full, full, full, vspec] + [full] * len(partners),
        out_specs=[full, row_block(levels, block), row_block(levels, block), tile_spec()],
        out_shape=[jax.ShapeDtypeStruct(values.shape, jnp.float32), row_shape(levels, cols),
                   row_shape(levels, cols), tile_shape()],
    )(values, inverse_pivot, ratio_values, vert_coef, *partners)


def edge_tables(edge_num, row_start, rows, weight_index, edge_map, mortar_weights):
    maps = lax.dynamic_slice_in_dim(edge_map[edge_num], row_start, rows, 0)
    picks = lax.dynamic_slice_in_dim(weight_index[edge_num], row_start, rows, 0)
    return (maps[:, 0], maps[:, 1], mortar_weights[picks, 0], mortar_weights[picks, 1])


def belt_cols(field):
    count = lax.axis_size("belt")
    first = jnp.transpose(field[:, :, 0])
    last = jnp.transpose(field[:, :, -1])
    west = lax.ppermute(last, "belt", [(i, (i + 1) % count) for i in range(count)])
    east = lax.ppermute(first, "belt", [((i + 1) % count, i) for i in range(count)])
    return west, east


def mer_rows(top, bottom):
    count = lax.axis_size("mer")
    south = lax.ppermute(top, "mer", [(i, i + 1) for i in range(count - 1)])
    north = lax.ppermute(bottom, "mer", [(i + 1, i) for i in range(count - 1)])
    return south, north


def gather_rows(column):
    count = lax.axis_size("mer")
    if count & (count - 1):
        return lax.all_gather(column, "mer", axis=0, tiled=True)
    me = lax.axis_index("mer")
    bit = 1
    while bit < count:
        other = lax.ppermute(column, "mer", [(i, i ^ bit) for i in range(count)])
        low_half = (me & bit) == 0
        column = jnp.concatenate(
            [jnp.where(low_half, column, other), jnp.where(low_half, other, column)], axis=0
        )
        bit *= 2
    return column


def as_lane_column(cols):
    return jnp.transpose(cols)[:, :, None]


def operator_kernel(slots, *refs):
    extra = len(slots) - 1
    (v_ref, vab_ref, vbe_ref, h_ref, e_ref, n_ref, up_ref, upb_ref, ew_ref, ns_ref,
     ve_ref, vw_ref, vn_ref, vs_ref) = refs[:14]
    partner_refs = (v_ref,) + refs[14:14 + extra]
    img_ref, part_ref = refs[14 + extra:]
    block, rows, cols = v_ref.shape
    i = pl.program_id(0)
    last_block = pl.num_programs(0) - 1
    lane = lax.broadcasted_iota(jnp.int32, (rows, cols), 1)
    row = lax.broadcasted_iota(jnp.int32, (rows, cols), 0)
    first_lane, last_lane = lane == 0, lane == cols - 1
    first_row, last_row = row == 0, row == rows - 1
    zero = jnp.zeros((rows, cols), jnp.float32)
    above = jnp.where(i == last_block, zero, vab_ref[0])
    below = jnp.where(i == 0, zero, vbe_ref[0])
    up_below = jnp.where(i == 0, zero, upb_ref[0])

    @pl.when(i == 0)
    def _():
        part_ref[...] = jnp.zeros_like(part_ref)

    edge = min(cols, 128)
    lane_e = lax.broadcasted_iota(jnp.int32, (rows, edge), 1)

    def first_tile(halo_ref, k, rolled):
        fixed = jnp.where(lane_e == 0, jnp.broadcast_to(halo_ref[k], (rows, edge)), rolled[:, :edge])
        return jnp.concatenate([fixed, rolled[:, edge:]], axis=1) if cols > edge else fixed

    def last_tile(halo_ref, k, rolled):
        fixed = jnp.where(lane_e == edge - 1, jnp.broadcast_to(halo_ref[k], (rows, edge)),
                          rolled[:, cols - edge:])
        return jnp.concatenate([rolled[:, :cols - edge], fixed], axis=1) if cols > edge else fixed

    def level(k, up_side, down_side, lower, accs):
        v = v_ref[k]
        east_side = last_tile(ve_ref, k, pltpu.roll(v, cols - 1, 1))
        west_side = first_tile(vw_ref, k, pltpu.roll(v, 1, 1))
        north_side = jnp.where(last_row, jnp.broadcast_to(vn_ref[k], (rows, cols)),
                               pltpu.roll(v, rows - 1, 0))
        south_side = jnp.where(first_row, jnp.broadcast_to(vs_ref[k], (rows, cols)),
                               pltpu.roll(v, 1, 0))
        east = e_ref[k]
        north = n_ref[k]
        west = ew_ref[k]
        south = ns_ref[k]
        image = (
            h_ref[k] * v
            + east * (v - east_side)
            + west * (v - west_side)
            + north * (v - north_side)
            + south * (v - south_side)
            + up_ref[k] * (v - up_side)
            + lower * (v - down_side)
        )
        img_ref[k] = image
        return tuple(acc + ref[k] * image for acc, ref in zip(accs, partner_refs))

    accs = (zero,) * len(slots)
    if block == 1:
        accs = level(0, above, below, up_below, accs)
    else:
        accs = level(0, v_ref[1], below, up_below, accs)
        accs = lax.fori_loop(
            1, block - 1,
            lambda k, c: level(k, v_ref[k + 1], v_ref[k - 1], up_ref[k - 1], c), accs,
            unroll=4,
        )
        accs = level(block - 1, above, v_ref[block - 2], up_ref[block - 2], accs)
    add_totals(part_ref, slots, accs)


def apply_operator(direction, coefs, halos, slots, extra=()):
    helm_diag, east_coef, north_coef, upper, east_west, north_south = coefs
    east_halo, west_halo, north_halo, south_halo = halos
    levels, rows, cols = direction.shape
    block = LEVEL_BLOCK if levels % LEVEL_BLOCK == 0 else levels
    blocks = levels // block
    full = pl.BlockSpec((block, rows, cols), lambda i: (i, 0, 0))
    lane_col = pl.BlockSpec((block, rows, 1), lambda i: (i, 0, 0))
    row_spec = pl.BlockSpec((block, 1, cols), lambda i: (i, 0, 0))
    above = pl.BlockSpec((1, rows, cols), lambda i: (jnp.minimum((i + 1) * block, levels - 1), 0, 0))
    below = pl.BlockSpec((1, rows, cols), lambda i: (jnp.maximum(i * block - 1, 0), 0, 0))
    kernel = lambda *refs: operator_kernel(slots, *refs)
    image, part = pl.pallas_call(
        kernel,
        grid=(blocks,),
        in_specs=[full, above, below, full, full, full, full, below, full, full,
                  lane_col, lane_col, row_spec, row_spec] + [full] * len(extra),
        out_specs=[full, tile_spec()],
        out_shape=[jax.ShapeDtypeStruct(direction.shape, jnp.float32), tile_shape()],
    )(direction, direction, direction, helm_diag, east_coef, north_coef, upper, upper,
      east_west, north_south, east_halo, west_halo, north_halo, south_halo, *extra)
    return image, part


def finish_kernel(sums_ref, p0_ref, q_ref, r0_ref, a0_ref, aq_ref, sol_ref, res_ref):
    block, rows, cols = p0_ref.shape
    sums = sums_ref[...]
    norm0, curv0, r0q, a0q, qaq, p0aq = (
        jnp.broadcast_to(sums[j:j + 1, :], sums.shape) for j in range(6)
    )
    step0 = norm0 / curv0
    norm1 = norm0 - step0 * (r0q + curv0) + step0 * step0 * a0q
    p1ap1 = curv0 - step0 * (p0aq + a0q) + step0 * step0 * qaq
    p1a0 = curv0 - step0 * a0q
    d0ap1 = curv0 - step0 * p0aq
    beta = norm1 / norm0
    curv1 = p1ap1 + beta * (p1a0 + d0ap1) + beta * beta * curv0
    step1 = norm1 / curv1
    widen = lambda x: jnp.concatenate([x[:rows]] * (cols // x.shape[1]), axis=1)
    step0, beta, step1 = widen(step0), widen(beta), widen(step1)

    def level(k, carry):
        p0 = p0_ref[k]
        a0 = a0_ref[k]
        precond1 = p0 - step0 * q_ref[k]
        direction1 = precond1 + beta * p0
        image1 = (a0 - step0 * aq_ref[k]) + beta * a0
        sol_ref[k] = step0 * p0 + step1 * direction1
        res_ref[k] = (r0_ref[k] - step0 * a0) - step1 * image1
        return carry

    lax.fori_loop(0, block, level, 0, unroll=2)


def finish(sums, precond0, basis, right_side, image0, image_q):
    levels, rows, cols = precond0.shape
    block = LEVEL_BLOCK if levels % LEVEL_BLOCK == 0 else levels
    full = pl.BlockSpec((block, rows, cols), lambda i: (i, 0, 0))
    field = jax.ShapeDtypeStruct(precond0.shape, jnp.float32)
    return pl.pallas_call(
        finish_kernel,
        grid=(levels // block,),
        in_specs=[tile_spec(), full, full, full, full, full],
        out_specs=[full, full],
        out_shape=[field, field],
    )(sums, precond0, basis, right_side, image0, image_q)


def exchange(direction, top, bottom, tables, use_mortar):
    count = lax.axis_size("belt")
    east = lax.ppermute(jnp.transpose(direction[:, :, 0]), "belt",
                        [((i + 1) % count, i) for i in range(count)])
    whole = gather_rows(east)
    west = lax.ppermute(jnp.transpose(direction[:, :, -1]), "belt",
                        [(i, (i + 1) % count) for i in range(count)])
    south, north = mer_rows(top, bottom)
    first_map, second_map, first_weight, second_weight = tables
    arrived = first_weight[:, None] * whole[first_map] + second_weight[:, None] * whole[second_map]
    east = jnp.where(use_mortar, arrived, east)
    return as_lane_column(east), as_lane_column(west), north, south


def on_device(
    right_side,
    helm_diag,
    east_coef,
    north_coef,
    vert_coef,
    mortar_weights,
    weight_index,
    edge_map,
    refined,
):
    belt_index = lax.axis_index("belt")
    mer_index = lax.axis_index("mer")
    per_panel = lax.axis_size("belt") // 4
    rows = right_side.shape[1]
    row_start = mer_index * rows
    own_edge = belt_index // per_panel
    row_flags = lax.dynamic_slice_in_dim(refined[own_edge], row_start, rows, 0)
    at_edge = (belt_index + 1) % per_panel == 0
    use_mortar = jnp.logical_and(at_edge, row_flags == 1)[:, None]
    tables = edge_tables(own_edge, row_start, rows, weight_index, edge_map, mortar_weights)
    levels, _, cols = right_side.shape
    block = BLOCK_COLS if cols % BLOCK_COLS == 0 else cols
    coef_west, _ = belt_cols(east_coef)
    coef_south, _ = mer_rows(north_coef[:, -1:, :], north_coef[:, :1, :])
    east_left = jnp.stack(
        [jnp.transpose(coef_west)]
        + [east_coef[:, :, j * block - 1] for j in range(1, cols // block)],
        axis=0,
    )[..., None]
    upper = jnp.concatenate([vert_coef, jnp.zeros_like(vert_coef[:1])], axis=0)

    inverse_pivot, ratio_values, precond0, top0, bottom0, west_coef, south_coef, part0 = (
        factor_solve(helm_diag, east_coef, north_coef, vert_coef, right_side, east_left, coef_south)
    )
    coefs = (helm_diag, east_coef, north_coef, upper, west_coef, south_coef)
    image0, curv_part0 = apply_operator(
        precond0, coefs, exchange(precond0, top0, bottom0, tables, use_mortar), (1,)
    )
    basis, top_q, bottom_q, basis_part = solve(
        image0, inverse_pivot, ratio_values, vert_coef, (right_side,), (2, 3)
    )
    image_q, image_q_part = apply_operator(
        basis, coefs, exchange(basis, top_q, bottom_q, tables, use_mortar), (4, 5), (precond0,)
    )
    sums = tree_sum(part0 + curv_part0 + basis_part + image_q_part)
    return finish(sums, precond0, basis, right_side, image0, image_q)


def solution(mesh):
    placed = (
        P(None, "mer", "belt"),
        P(None, "mer", "belt"),
        P(None, "mer", "belt"),
        P(None, "mer", "belt"),
        P(None, "mer", "belt"),
        P(),
        P(),
        P(),
        P(),
    )
    return jax.shard_map(
        on_device,
        mesh=mesh,
        in_specs=placed,
        out_specs=(P(None, "mer", "belt"), P(None, "mer", "belt")),
        check_vma=False,
    )
```

```python
import jax
import jax.numpy as jnp
from jax import lax
from jax.experimental import pallas as pl
from jax.experimental.pallas import tpu as pltpu
from jax.sharding import PartitionSpec as P

ITERS = 2
BLOCK_COLS = 384
LEVEL_BLOCK = 40


def tree_sum(values):
    for axis in ("mer", "belt"):
        count = lax.axis_size(axis)
        if count & (count - 1):
            values = lax.psum(values, axis)
            continue
        bit = 1
        while bit < count:
            values = values + lax.ppermute(values, axis, [(i, i ^ bit) for i in range(count)])
            bit *= 2
    return values


def add_totals(part_ref, slots, accs):
    row = lax.broadcasted_iota(jnp.int32, part_ref.shape, 0)
    tile = part_ref[...]
    for slot, acc in zip(slots, accs):
        tile = tile + jnp.where(row == slot, jnp.sum(acc), 0.0)
    part_ref[...] = tile


def tile_spec():
    return pl.BlockSpec((8, 128), lambda j: (0, 0))


def tile_shape():
    return jax.ShapeDtypeStruct((8, 128), jnp.float32)


def row_block(levels, block):
    return pl.BlockSpec((levels, 1, block), lambda j: (0, 0, j))


def row_shape(levels, cols):
    return jax.ShapeDtypeStruct((levels, 1, cols), jnp.float32)


def column_spec(levels, rows, cols):
    return pl.BlockSpec((levels, rows, cols), lambda j: (0, 0, j))


def factor_solve_kernel(h_ref, e_ref, n_ref, v_ref, r_ref, eleft_ref, nsouth_ref,
                        inv_ref, ratio_ref, p_ref, top_ref, bottom_ref, w_ref, s_ref, part_ref):
    levels, rows, cols = h_ref.shape

    @pl.when(pl.program_id(0) == 0)
    def _():
        part_ref[...] = jnp.zeros_like(part_ref)

    zero = jnp.zeros((rows, cols), jnp.float32)
    first_lane = lax.broadcasted_iota(jnp.int32, (rows, cols), 1) == 0
    first_row = lax.broadcasted_iota(jnp.int32, (rows, cols), 0) == 0

    def forward(k, up, down, prev, elim):
        east = e_ref[k]
        north = n_ref[k]
        west = jnp.where(first_lane, jnp.broadcast_to(eleft_ref[k], (rows, cols)),
                         pltpu.roll(east, 1, 1))
        south = jnp.where(first_row, jnp.broadcast_to(nsouth_ref[k], (rows, cols)),
                          pltpu.roll(north, 1, 0))
        w_ref[k] = west
        s_ref[k] = south
        diag = h_ref[k] + east + west + north + south + up + down
        ratio = down / prev
        pivot = diag - down * ratio
        inv_ref[k] = 1.0 / pivot
        ratio_ref[k] = ratio
        elim = r_ref[k] + ratio * elim
        p_ref[k] = elim
        return pivot, elim

    carry = forward(0, v_ref[0], zero, jnp.ones_like(zero), zero)
    carry = lax.fori_loop(
        1, levels - 1, lambda k, c: forward(k, v_ref[k], v_ref[k - 1], *c), carry, unroll=16
    )
    forward(levels - 1, zero, v_ref[levels - 2], *carry)

    def backward(k, up, succ, acc):
        value = inv_ref[k] * (p_ref[k] + up * succ)
        p_ref[k] = value
        top_ref[k] = value[rows - 1:rows]
        bottom_ref[k] = value[:1]
        return value, acc + r_ref[k] * value

    carry = backward(levels - 1, zero, zero, zero)
    carry = lax.fori_loop(
        0, levels - 1, lambda i, c: backward(levels - 2 - i, v_ref[levels - 2 - i], *c), carry,
        unroll=16,
    )
    add_totals(part_ref, (0,), (carry[1],))


def factor_solve(helm_diag, east_coef, north_coef, vert_coef, rhs, east_left, north_south):
    levels, rows, cols = rhs.shape
    block = BLOCK_COLS if cols % BLOCK_COLS == 0 else cols
    full = column_spec(levels, rows, block)
    vspec = column_spec(levels - 1, rows, block)
    field = jax.ShapeDtypeStruct(rhs.shape, jnp.float32)
    return pl.pallas_call(
        factor_solve_kernel,
        grid=(cols // block,),
        in_specs=[full, full, full, vspec, full,
                  pl.BlockSpec((None, levels, rows, 1), lambda j: (j, 0, 0, 0)),
                  pl.BlockSpec((levels, 1, block), lambda j: (0, 0, j))],
        out_specs=[full, full, full, row_block(levels, block), row_block(levels, block),
                   full, full, tile_spec()],
        out_shape=[field, field, field, row_shape(levels, cols), row_shape(levels, cols),
                   field, field, tile_shape()],
    )(helm_diag, east_coef, north_coef, vert_coef, rhs, east_left, north_south)


def solve_kernel(slots, *refs):
    count = len(slots)
    val_ref, inv_ref, ratio_ref, v_ref = refs[:4]
    partner_refs = refs[4:4 + count - 1] + (val_ref,)
    p_ref, top_ref, bottom_ref, part_ref = refs[4 + count - 1:]
    levels = val_ref.shape[0]
    zero = jnp.zeros(val_ref.shape[1:], jnp.float32)

    @pl.when(pl.program_id(0) == 0)
    def _():
        part_ref[...] = jnp.zeros_like(part_ref)

    def forward(k, elim):
        elim = val_ref[k] + ratio_ref[k] * elim
        p_ref[k] = elim
        return elim

    lax.fori_loop(0, levels, forward, zero, unroll=16)

    def backward(k, up, succ, accs):
        value = inv_ref[k] * (p_ref[k] + up * succ)
        p_ref[k] = value
        top_ref[k] = value[value.shape[0] - 1:]
        bottom_ref[k] = value[:1]
        return value, tuple(acc + ref[k] * value for acc, ref in zip(accs, partner_refs))

    carry = backward(levels - 1, zero, zero, (zero,) * count)
    carry = lax.fori_loop(
        0, levels - 1, lambda i, c: backward(levels - 2 - i, v_ref[levels - 2 - i], *c), carry,
        unroll=16,
    )
    add_totals(part_ref, slots, carry[1])


def solve(values, inverse_pivot, ratio_values, vert_coef, partners, slots):
    levels, rows, cols = values.shape
    block = BLOCK_COLS if cols % BLOCK_COLS == 0 else cols
    full = column_spec(levels, rows, block)
    vspec = column_spec(levels - 1, rows, block)
    return pl.pallas_call(
        lambda *refs: solve_kernel(slots, *refs),
        grid=(cols // block,),
        in_specs=[full, full, full, vspec] + [full] * len(partners),
        out_specs=[full, row_block(levels, block), row_block(levels, block), tile_spec()],
        out_shape=[jax.ShapeDtypeStruct(values.shape, jnp.float32), row_shape(levels, cols),
                   row_shape(levels, cols), tile_shape()],
    )(values, inverse_pivot, ratio_values, vert_coef, *partners)


def edge_tables(edge_num, row_start, rows, weight_index, edge_map, mortar_weights):
    maps = lax.dynamic_slice_in_dim(edge_map[edge_num], row_start, rows, 0)
    picks = lax.dynamic_slice_in_dim(weight_index[edge_num], row_start, rows, 0)
    return (maps[:, 0], maps[:, 1], mortar_weights[picks, 0], mortar_weights[picks, 1])


def belt_cols(field):
    count = lax.axis_size("belt")
    first = jnp.transpose(field[:, :, 0])
    last = jnp.transpose(field[:, :, -1])
    west = lax.ppermute(last, "belt", [(i, (i + 1) % count) for i in range(count)])
    east = lax.ppermute(first, "belt", [((i + 1) % count, i) for i in range(count)])
    return west, east


def mer_rows(top, bottom):
    count = lax.axis_size("mer")
    south = lax.ppermute(top, "mer", [(i, i + 1) for i in range(count - 1)])
    north = lax.ppermute(bottom, "mer", [(i + 1, i) for i in range(count - 1)])
    return south, north


def gather_rows(column):
    count = lax.axis_size("mer")
    if count & (count - 1):
        return lax.all_gather(column, "mer", axis=0, tiled=True)
    me = lax.axis_index("mer")
    bit = 1
    while bit < count:
        other = lax.ppermute(column, "mer", [(i, i ^ bit) for i in range(count)])
        low_half = (me & bit) == 0
        column = jnp.concatenate(
            [jnp.where(low_half, column, other), jnp.where(low_half, other, column)], axis=0
        )
        bit *= 2
    return column


def as_lane_column(cols):
    return jnp.transpose(cols)[:, :, None]


def operator_kernel(slots, *refs):
    extra = len(slots) - 1
    (v_ref, vab_ref, vbe_ref, h_ref, e_ref, n_ref, up_ref, upb_ref, ew_ref, ns_ref,
     ve_ref, vw_ref, vn_ref, vs_ref) = refs[:14]
    partner_refs = (v_ref,) + refs[14:14 + extra]
    img_ref, part_ref = refs[14 + extra:]
    block, rows, cols = v_ref.shape
    i = pl.program_id(0)
    last_block = pl.num_programs(0) - 1
    lane = lax.broadcasted_iota(jnp.int32, (rows, cols), 1)
    row = lax.broadcasted_iota(jnp.int32, (rows, cols), 0)
    first_lane, last_lane = lane == 0, lane == cols - 1
    first_row, last_row = row == 0, row == rows - 1
    zero = jnp.zeros((rows, cols), jnp.float32)
    above = jnp.where(i == last_block, zero, vab_ref[0])
    below = jnp.where(i == 0, zero, vbe_ref[0])
    up_below = jnp.where(i == 0, zero, upb_ref[0])

    @pl.when(i == 0)
    def _():
        part_ref[...] = jnp.zeros_like(part_ref)

    edge = min(cols, 128)
    lane_e = lax.broadcasted_iota(jnp.int32, (rows, edge), 1)

    def first_tile(halo_ref, k, rolled):
        fixed = jnp.where(lane_e == 0, jnp.broadcast_to(halo_ref[k], (rows, edge)), rolled[:, :edge])
        return jnp.concatenate([fixed, rolled[:, edge:]], axis=1) if cols > edge else fixed

    def last_tile(halo_ref, k, rolled):
        fixed = jnp.where(lane_e == edge - 1, jnp.broadcast_to(halo_ref[k], (rows, edge)),
                          rolled[:, cols - edge:])
        return jnp.concatenate([rolled[:, :cols - edge], fixed], axis=1) if cols > edge else fixed

    def level(k, up_side, down_side, lower, accs):
        v = v_ref[k]
        east_side = last_tile(ve_ref, k, pltpu.roll(v, cols - 1, 1))
        west_side = first_tile(vw_ref, k, pltpu.roll(v, 1, 1))
        north_side = jnp.where(last_row, jnp.broadcast_to(vn_ref[k], (rows, cols)),
                               pltpu.roll(v, rows - 1, 0))
        south_side = jnp.where(first_row, jnp.broadcast_to(vs_ref[k], (rows, cols)),
                               pltpu.roll(v, 1, 0))
        east = e_ref[k]
        north = n_ref[k]
        west = ew_ref[k]
        south = ns_ref[k]
        image = (
            h_ref[k] * v
            + east * (v - east_side)
            + west * (v - west_side)
            + north * (v - north_side)
            + south * (v - south_side)
            + up_ref[k] * (v - up_side)
            + lower * (v - down_side)
        )
        img_ref[k] = image
        return tuple(acc + ref[k] * image for acc, ref in zip(accs, partner_refs))

    accs = (zero,) * len(slots)
    if block == 1:
        accs = level(0, above, below, up_below, accs)
    else:
        accs = level(0, v_ref[1], below, up_below, accs)
        accs = lax.fori_loop(
            1, block - 1,
            lambda k, c: level(k, v_ref[k + 1], v_ref[k - 1], up_ref[k - 1], c), accs,
            unroll=4,
        )
        accs = level(block - 1, above, v_ref[block - 2], up_ref[block - 2], accs)
    add_totals(part_ref, slots, accs)


def apply_operator(direction, coefs, halos, slots, extra=()):
    helm_diag, east_coef, north_coef, upper, east_west, north_south = coefs
    east_halo, west_halo, north_halo, south_halo = halos
    levels, rows, cols = direction.shape
    block = LEVEL_BLOCK if levels % LEVEL_BLOCK == 0 else levels
    blocks = levels // block
    full = pl.BlockSpec((block, rows, cols), lambda i: (i, 0, 0))
    lane_col = pl.BlockSpec((block, rows, 1), lambda i: (i, 0, 0))
    row_spec = pl.BlockSpec((block, 1, cols), lambda i: (i, 0, 0))
    above = pl.BlockSpec((1, rows, cols), lambda i: (jnp.minimum((i + 1) * block, levels - 1), 0, 0))
    below = pl.BlockSpec((1, rows, cols), lambda i: (jnp.maximum(i * block - 1, 0), 0, 0))
    kernel = lambda *refs: operator_kernel(slots, *refs)
    image, part = pl.pallas_call(
        kernel,
        grid=(blocks,),
        in_specs=[full, above, below, full, full, full, full, below, full, full,
                  lane_col, lane_col, row_spec, row_spec] + [full] * len(extra),
        out_specs=[full, tile_spec()],
        out_shape=[jax.ShapeDtypeStruct(direction.shape, jnp.float32), tile_shape()],
    )(direction, direction, direction, helm_diag, east_coef, north_coef, upper, upper,
      east_west, north_south, east_halo, west_halo, north_halo, south_halo, *extra)
    return image, part


def finish_kernel(sums_ref, p0_ref, q_ref, r0_ref, a0_ref, aq_ref, sol_ref, res_ref):
    block, rows, cols = p0_ref.shape
    sums = sums_ref[...]
    norm0, curv0, r0q, a0q, qaq, p0aq = (
        jnp.broadcast_to(sums[j:j + 1, :], sums.shape) for j in range(6)
    )
    step0 = norm0 / curv0
    norm1 = norm0 - step0 * (r0q + curv0) + step0 * step0 * a0q
    p1ap1 = curv0 - step0 * (p0aq + a0q) + step0 * step0 * qaq
    p1a0 = curv0 - step0 * a0q
    d0ap1 = curv0 - step0 * p0aq
    beta = norm1 / norm0
    curv1 = p1ap1 + beta * (p1a0 + d0ap1) + beta * beta * curv0
    step1 = norm1 / curv1
    widen = lambda x: jnp.concatenate([x[:rows]] * (cols // x.shape[1]), axis=1)
    step0, beta, step1 = widen(step0), widen(beta), widen(step1)

    def level(k, carry):
        p0 = p0_ref[k]
        a0 = a0_ref[k]
        precond1 = p0 - step0 * q_ref[k]
        direction1 = precond1 + beta * p0
        image1 = (a0 - step0 * aq_ref[k]) + beta * a0
        sol_ref[k] = step0 * p0 + step1 * direction1
        res_ref[k] = (r0_ref[k] - step0 * a0) - step1 * image1
        return carry

    lax.fori_loop(0, block, level, 0, unroll=4)


def finish(sums, precond0, basis, right_side, image0, image_q):
    levels, rows, cols = precond0.shape
    block = LEVEL_BLOCK if levels % LEVEL_BLOCK == 0 else levels
    full = pl.BlockSpec((block, rows, cols), lambda i: (i, 0, 0))
    field = jax.ShapeDtypeStruct(precond0.shape, jnp.float32)
    return pl.pallas_call(
        finish_kernel,
        grid=(levels // block,),
        in_specs=[tile_spec(), full, full, full, full, full],
        out_specs=[full, full],
        out_shape=[field, field],
    )(sums, precond0, basis, right_side, image0, image_q)


def exchange(direction, top, bottom, tables, use_mortar):
    count = lax.axis_size("belt")
    east = lax.ppermute(jnp.transpose(direction[:, :, 0]), "belt",
                        [((i + 1) % count, i) for i in range(count)])
    whole = gather_rows(east)
    west = lax.ppermute(jnp.transpose(direction[:, :, -1]), "belt",
                        [(i, (i + 1) % count) for i in range(count)])
    south, north = mer_rows(top, bottom)
    first_map, second_map, first_weight, second_weight = tables
    arrived = first_weight[:, None] * whole[first_map] + second_weight[:, None] * whole[second_map]
    east = jnp.where(use_mortar, arrived, east)
    return as_lane_column(east), as_lane_column(west), north, south


def on_device(
    right_side,
    helm_diag,
    east_coef,
    north_coef,
    vert_coef,
    mortar_weights,
    weight_index,
    edge_map,
    refined,
):
    belt_index = lax.axis_index("belt")
    mer_index = lax.axis_index("mer")
    per_panel = lax.axis_size("belt") // 4
    rows = right_side.shape[1]
    row_start = mer_index * rows
    own_edge = belt_index // per_panel
    row_flags = lax.dynamic_slice_in_dim(refined[own_edge], row_start, rows, 0)
    at_edge = (belt_index + 1) % per_panel == 0
    use_mortar = jnp.logical_and(at_edge, row_flags == 1)[:, None]
    tables = edge_tables(own_edge, row_start, rows, weight_index, edge_map, mortar_weights)
    levels, _, cols = right_side.shape
    block = BLOCK_COLS if cols % BLOCK_COLS == 0 else cols
    coef_west, _ = belt_cols(east_coef)
    coef_south, _ = mer_rows(north_coef[:, -1:, :], north_coef[:, :1, :])
    east_left = jnp.stack(
        [jnp.transpose(coef_west)]
        + [east_coef[:, :, j * block - 1] for j in range(1, cols // block)],
        axis=0,
    )[..., None]
    upper = jnp.concatenate([vert_coef, jnp.zeros_like(vert_coef[:1])], axis=0)

    inverse_pivot, ratio_values, precond0, top0, bottom0, west_coef, south_coef, part0 = (
        factor_solve(helm_diag, east_coef, north_coef, vert_coef, right_side, east_left, coef_south)
    )
    coefs = (helm_diag, east_coef, north_coef, upper, west_coef, south_coef)
    image0, curv_part0 = apply_operator(
        precond0, coefs, exchange(precond0, top0, bottom0, tables, use_mortar), (1,)
    )
    basis, top_q, bottom_q, basis_part = solve(
        image0, inverse_pivot, ratio_values, vert_coef, (right_side,), (2, 3)
    )
    image_q, image_q_part = apply_operator(
        basis, coefs, exchange(basis, top_q, bottom_q, tables, use_mortar), (4, 5), (precond0,)
    )
    sums = tree_sum(part0 + curv_part0 + basis_part + image_q_part)
    return finish(sums, precond0, basis, right_side, image0, image_q)


def solution(mesh):
    placed = (
        P(None, "mer", "belt"),
        P(None, "mer", "belt"),
        P(None, "mer", "belt"),
        P(None, "mer", "belt"),
        P(None, "mer", "belt"),
        P(),
        P(),
        P(),
        P(),
    )
    return jax.shard_map(
        on_device,
        mesh=mesh,
        in_specs=placed,
        out_specs=(P(None, "mer", "belt"), P(None, "mer", "belt")),
        check_vma=False,
    )
```
